32 devices in a mesh: ctx: 8 (over z, core), tp: 4 (over y, x).
Axes of the slice: x: 2, y: 2, z: 4, core: 2. Of those that a mesh axis runs over, the one named last changes fastest.
Arguments:
- q_proj: bfloat16 [1024, 4096], P('ctx', 'tp'), may hold values from -6 to 6
- k_proj: bfloat16 [1024, 4096], P('ctx', 'tp'), may hold values from -6 to 6
- v_proj: bfloat16 [1024, 4096], P('ctx', 'tp'), may hold values from -6 to 6
- saved_conv: bfloat16 [1024, 4096], P('ctx', 'tp'), may hold values from -6 to 6
- out_grad: bfloat16 [1024, 4096], P('ctx', 'tp'), may hold values from -6 to 6
- out_weight: bfloat16 [4096, 4096], P('tp'), may hold values from -0.09375 to 0.09375
- filter_taps: bfloat16 [1024, 4096], P('ctx', 'tp'), may hold values from -1.1 to 1.1
Outputs:
- dq_grad: bfloat16 [1024, 4096], P('ctx', 'tp')
- dk_grad: bfloat16 [1024, 4096], P('ctx', 'tp')
- dv_grad: bfloat16 [1024, 4096], P('ctx', 'tp')
- filter_grad: float32 [1024, 4096], P('ctx', 'tp')
The draws below stay inside these ranges and needn't reach their ends.
All inputs are finite; a program needn't handle non-finite values.
Results may differ from the reference program's by a relative error of at most 0.003.
Values may be sent and summed in bfloat16 or wider, within the bound.
No kernel may reach another device: no remote copies, remote signals or barrier semaphores. Data moves between devices by JAX's collectives and lax.ppermute only.
A program may use at most 128 MiB of HBM per device.

```python
import math
import jax
import jax.numpy as jnp

D = 4096
SEQ = 1024


def draw_filter_taps(key, part):
    first, second = jax.random.split(jax.random.fold_in(key, 7))
    noise = jnp.clip(jax.random.normal(first, (SEQ, D), jnp.float32), -4.0, 4.0)
    log_rate = jax.random.uniform(second, (1, D), jnp.float32, math.log(0.5 / SEQ), math.log(1.0 / 30.0))
    rate = jnp.exp(log_rate)
    lags = jnp.arange(SEQ, dtype=jnp.float32)[:, None]
    scale = jnp.sqrt((1.0 - jnp.exp(-2.0 * rate)) / (1.0 - jnp.exp(-2.0 * rate * SEQ)))
    return (noise * scale * jnp.exp(-rate * lags)).astype(jnp.bfloat16)


def block_scale(rng, shape, cuts, smallest, largest):
    factor_of = 1.0
    for position, shards_of in cuts:
        heights = jax.random.uniform(jax.random.fold_in(jax.random.fold_in(rng, 6), position), (shards_of,), jnp.float32, smallest / len(cuts), largest / len(cuts))
        factor_of = factor_of * jnp.repeat(jnp.exp(heights), shape[position] // shards_of).reshape((-1,) + (1,) * (len(shape) - 1 - position))
    return factor_of


def centred(rng, extent, scale, limit, cuts=(), kind=jnp.bfloat16):
    entries = scale * jax.random.normal(rng, extent, jnp.float32)
    if cuts:
        entries = entries * block_scale(rng, extent, cuts, -0.22, 0.18)
    return jnp.clip(entries, -limit, limit).astype(kind)


def setup_inputs(seed: int = 0) -> dict:
    key_list = jax.random.split(jax.random.key(seed), 8)
    return {
        "q_proj": centred(key_list[0], (SEQ, D), 1.0, 6.0, ((0, 8), (1, 4))),
        "k_proj": centred(key_list[1], (SEQ, D), 1.0, 6.0, ((0, 8), (1, 4))),
        "v_proj": centred(key_list[2], (SEQ, D), 1.0, 6.0, ((0, 8), (1, 4))),
        "saved_conv": centred(key_list[3], (SEQ, D), 1.0, 6.0, ((0, 8), (1, 4))),
        "out_grad": centred(key_list[4], (SEQ, D), 1.0, 6.0, ((0, 8), (1, 4))),
        "out_weight": centred(key_list[5], (D, D), D ** -0.5, 0.09375, ((0, 4),)),
        "filter_taps": draw_filter_taps(jax.random.fold_in(key_list[7], 71), 0),
    }


def reference(q_proj, k_proj, v_proj, saved_conv, out_grad, out_weight, filter_taps):
    d_gated = jnp.dot(out_grad, out_weight.T, preferred_element_type=jnp.float32)
    dq_grad = (d_gated * saved_conv.astype(jnp.float32)).astype(jnp.bfloat16)
    dz = d_gated * q_proj.astype(jnp.float32)
    gated = (k_proj.astype(jnp.float32) * v_proj.astype(jnp.float32)).astype(jnp.bfloat16)
    length = 2 * SEQ
    dz_spec = jnp.fft.rfft(dz, n=length, axis=0)
    filter_spec = jnp.fft.rfft(filter_taps.astype(jnp.float32), n=length, axis=0)
    du = jnp.fft.irfft(jnp.conj(filter_spec) * dz_spec, n=length, axis=0)[:SEQ].astype(jnp.float32)
    gated_spec = jnp.fft.rfft(gated.astype(jnp.float32), n=length, axis=0)
    lagged = jnp.fft.irfft(jnp.conj(gated_spec) * dz_spec, n=length, axis=0)[:SEQ].astype(jnp.float32)
    filter_grad = lagged * (float(SEQ) ** -0.5)
    dk_grad = (du * v_proj.astype(jnp.float32)).astype(jnp.bfloat16)
    dv_grad = (du * k_proj.astype(jnp.float32)).astype(jnp.bfloat16)
    return dq_grad, dk_grad, dv_grad, filter_grad.astype(jnp.float32)
```

```python
import math

import jax
import jax.numpy as jnp
from jax import lax
from jax.sharding import PartitionSpec as P


BLOCK = 128


def split_bf16(value):
    upper = lax.optimization_barrier(value.astype(jnp.bfloat16))
    lower = (value - upper.astype(jnp.float32)).astype(jnp.bfloat16)
    return upper, lower


def gather_matmul(out_grad, out_weight):
    count = lax.axis_size("tp")
    me = lax.axis_index("tp")
    width = out_grad.shape[1]
    total = None
    for shift in range(count):
        if shift == 0:
            piece = out_grad
        else:
            piece = lax.ppermute(out_grad, "tp", [(i, (i + shift) % count) for i in range(count)])
        source = (me - shift) % count
        weight = lax.dynamic_slice_in_dim(out_weight, source * width, width, axis=1)
        part = lax.dot_general(
            piece, weight, (((1,), (1,)), ((), ())), preferred_element_type=jnp.float32
        )
        total = part if total is None else total + part
    return total


def make_tables(size):
    index = jnp.arange(size, dtype=jnp.int32)
    long_index = jnp.arange(2 * size, dtype=jnp.int32)
    angle = (index[:, None] * index[None, :] % (2 * size)).astype(jnp.float32) * (math.pi / size)
    angle_back = (long_index[:, None] * index[None, :] % (2 * size)).astype(jnp.float32) * (
        math.pi / size
    )
    weight = jnp.where(index == 0, 1.0, 2.0).astype(jnp.float32) / (2.0 * size)
    alternate = (1 - 2 * (index % 2)).astype(jnp.float32)
    alternate_back = (1 - 2 * (long_index % 2)).astype(jnp.float32) / (2.0 * size)
    return {
        "cos": split_bf16(jnp.cos(angle)),
        "sin": split_bf16(-jnp.sin(angle)),
        "alt": alternate.astype(jnp.bfloat16),
        "icos": split_bf16(jnp.cos(angle_back) * weight[None, :]),
        "isin": split_bf16(-jnp.sin(angle_back) * weight[None, :]),
        "ialt": alternate_back,
    }


def apply(table, signal_hi, signal_lo=None):
    def one(left, right):
        return jnp.einsum("kn,bnc->bkc", left, right, preferred_element_type=jnp.float32)

    out = one(table[0], signal_hi) + one(table[1], signal_hi)
    if signal_lo is not None:
        out = out + one(table[0], signal_lo)
    return out


def forward(tables, signal_hi, signal_lo=None):
    real = apply(tables["cos"], signal_hi, signal_lo)
    imag = apply(tables["sin"], signal_hi, signal_lo)
    nyq = jnp.einsum("n,bnc->bc", tables["alt"], signal_hi, preferred_element_type=jnp.float32)
    if signal_lo is not None:
        nyq = nyq + jnp.einsum(
            "n,bnc->bc", tables["alt"], signal_lo, preferred_element_type=jnp.float32
        )
    return real, imag, nyq


def inverse(tables, spectrum, start, count):
    real_hi, real_lo = split_bf16(spectrum[0])
    imag_hi, imag_lo = split_bf16(spectrum[1])
    icos = tuple(t[start : start + count] for t in tables["icos"])
    isin = tuple(t[start : start + count] for t in tables["isin"])
    ialt = tables["ialt"][start : start + count]
    return (
        apply(icos, real_hi, real_lo)
        + apply(isin, imag_hi, imag_lo)
        + ialt[None, :, None] * spectrum[2][:, None, :]
    )


def conj_times(first, second):
    real = first[0][None] * second[0] + first[1][None] * second[1]
    imag = first[0][None] * second[1] - first[1][None] * second[0]
    return real, imag, first[2][None] * second[2]


def long_correlations(dz_hi, dz_lo, gated, taps, seq_scale):
    seq, chans = gated.shape
    size = min(BLOCK, seq)
    blocks = seq // size
    tables = make_tables(size)
    shape = (blocks, size, chans)
    dz_spec = forward(tables, dz_hi.reshape(shape), dz_lo.reshape(shape))
    gated_spec = forward(tables, gated.reshape(shape))
    taps_spec = forward(tables, taps.reshape(shape))
    parity = (1 - 2 * (jnp.arange(size, dtype=jnp.int32) % 2)).astype(jnp.float32)[None, :, None]
    parity_top = float(1 - 2 * (size % 2))

    def earlier(stack):
        return jnp.concatenate([jnp.zeros_like(stack[:1]), stack[:-1]], axis=0)

    lag_spec = (
        earlier(taps_spec[0]) + parity * taps_spec[0],
        earlier(taps_spec[1]) + parity * taps_spec[1],
        earlier(taps_spec[2]) + parity_top * taps_spec[2],
    )
    padded = tuple(jnp.concatenate([part, jnp.zeros_like(part)], axis=0) for part in dz_spec)
    du_spec = None
    lag_sums = None
    for offset in range(blocks):
        window = tuple(part[offset : offset + blocks] for part in padded)
        du_term = conj_times(tuple(part[offset] for part in lag_spec), window)
        lag_term = conj_times(tuple(part[offset] for part in gated_spec), window)
        if du_spec is None:
            du_spec, lag_sums = du_term, lag_term
        else:
            du_spec = tuple(a + b for a, b in zip(du_spec, du_term))
            lag_sums = tuple(a + b for a, b in zip(lag_sums, lag_term))
    du = inverse(tables, du_spec, size, size).reshape(seq, chans)
    lagged = inverse(tables, lag_sums, 0, 2 * size)
    later_half = jnp.concatenate([lagged[1:, size:], jnp.zeros_like(lagged[:1, size:])], axis=0)
    filter_grad = (lagged[:, :size] + later_half).reshape(seq, chans) * seq_scale
    return du, filter_grad


def body(q_proj, k_proj, v_proj, saved_conv, out_grad, out_weight, filter_taps):
    rows = q_proj.shape[0]
    blocks = lax.axis_size("ctx")
    seq = rows * blocks
    d_gated = gather_matmul(out_grad, out_weight)
    dq_grad = (d_gated * saved_conv.astype(jnp.float32)).astype(jnp.bfloat16)
    dz = d_gated * q_proj.astype(jnp.float32)
    gated = (k_proj.astype(jnp.float32) * v_proj.astype(jnp.float32)).astype(jnp.bfloat16)
    dz_hi, dz_lo = split_bf16(dz)
    outgoing = jnp.stack([dz_hi, dz_lo, gated, filter_taps])
    incoming = lax.all_to_all(outgoing, "ctx", 2, 1, tiled=True)
    du_t, filter_t = long_correlations(
        incoming[0], incoming[1], incoming[2], incoming[3], float(seq) ** -0.5
    )
    back = lax.all_to_all(jnp.stack([du_t, filter_t]), "ctx", 1, 2, tiled=True)
    du_local = back[0]
    filter_grad = back[1]
    dk_grad = (du_local * v_proj.astype(jnp.float32)).astype(jnp.bfloat16)
    dv_grad = (du_local * k_proj.astype(jnp.float32)).astype(jnp.bfloat16)
    return (dq_grad, dk_grad, dv_grad, filter_grad)


def solution(mesh):
    in_specs = (
        P("ctx", "tp"),
        P("ctx", "tp"),
        P("ctx", "tp"),
        P("ctx", "tp"),
        P("ctx", "tp"),
        P("tp", None),
        P("ctx", "tp"),
    )
    out_specs = (P("ctx", "tp"), P("ctx", "tp"), P("ctx", "tp"), P("ctx", "tp"))
    return jax.shard_map(body, mesh=mesh, in_specs=in_specs, out_specs=out_specs, check_vma=False)
```

```python
import math

import jax
import jax.numpy as jnp
from jax import lax
from jax.sharding import PartitionSpec as P


BLOCK = 128


def split_bf16(value):
    upper = lax.optimization_barrier(value.astype(jnp.bfloat16))
    lower = (value - upper.astype(jnp.float32)).astype(jnp.bfloat16)
    return upper, lower


def gather_matmul(out_grad, out_weight):
    count = lax.axis_size("tp")
    me = lax.axis_index("tp")
    width = out_grad.shape[1]
    total = None
    for shift in range(count):
        if shift == 0:
            piece = out_grad
        else:
            piece = lax.ppermute(out_grad, "tp", [(i, (i + shift) % count) for i in range(count)])
        source = (me - shift) % count
        weight = lax.dynamic_slice_in_dim(out_weight, source * width, width, axis=1)
        part = lax.dot_general(
            piece, weight, (((1,), (1,)), ((), ())), preferred_element_type=jnp.float32
        )
        total = part if total is None else total + part
    return total


def make_tables(size):
    index = jnp.arange(size, dtype=jnp.int32)
    long_index = jnp.arange(2 * size, dtype=jnp.int32)
    angle = (index[:, None] * index[None, :] % (2 * size)).astype(jnp.float32) * (math.pi / size)
    angle_back = (long_index[:, None] * index[None, :] % (2 * size)).astype(jnp.float32) * (
        math.pi / size
    )
    weight = jnp.where(index == 0, 1.0, 2.0).astype(jnp.float32) / (2.0 * size)
    alternate = (1 - 2 * (index % 2)).astype(jnp.float32)
    alternate_back = (1 - 2 * (long_index % 2)).astype(jnp.float32) / (2.0 * size)
    return {
        "cos": split_bf16(jnp.cos(angle)),
        "sin": split_bf16(-jnp.sin(angle)),
        "alt": alternate.astype(jnp.bfloat16),
        "icos": split_bf16(jnp.cos(angle_back) * weight[None, :]),
        "isin": split_bf16(-jnp.sin(angle_back) * weight[None, :]),
        "ialt": alternate_back,
    }


def apply(table, signal_hi, signal_lo=None):
    def one(left, right):
        return jnp.einsum("kn,bnc->bkc", left, right, preferred_element_type=jnp.float32)

    out = one(table[0], signal_hi) + one(table[1], signal_hi)
    if signal_lo is not None:
        out = out + one(table[0], signal_lo)
    return out


def forward(tables, signal_hi, signal_lo=None):
    real = apply(tables["cos"], signal_hi, signal_lo)
    imag = apply(tables["sin"], signal_hi, signal_lo)
    nyq = jnp.einsum("n,bnc->bc", tables["alt"], signal_hi, preferred_element_type=jnp.float32)
    if signal_lo is not None:
        nyq = nyq + jnp.einsum(
            "n,bnc->bc", tables["alt"], signal_lo, preferred_element_type=jnp.float32
        )
    return real, imag, nyq


def inverse(tables, spectrum, start, count):
    real_hi, real_lo = split_bf16(spectrum[0])
    imag_hi, imag_lo = split_bf16(spectrum[1])
    icos = tuple(t[start : start + count] for t in tables["icos"])
    isin = tuple(t[start : start + count] for t in tables["isin"])
    ialt = tables["ialt"][start : start + count]
    return (
        apply(icos, real_hi, real_lo)
        + apply(isin, imag_hi, imag_lo)
        + ialt[None, :, None] * spectrum[2][:, None, :]
    )


def conj_times(first, second):
    real = first[0][None] * second[0] + first[1][None] * second[1]
    imag = first[0][None] * second[1] - first[1][None] * second[0]
    return real, imag, first[2][None] * second[2]


def long_correlations(dz_hi, dz_lo, gated, taps, seq_scale):
    seq, chans = gated.shape
    size = min(BLOCK, seq)
    blocks = seq // size
    tables = make_tables(size)
    shape = (blocks, size, chans)
    dz_spec = forward(tables, dz_hi.reshape(shape), dz_lo.reshape(shape))
    gated_spec = forward(tables, gated.reshape(shape))
    taps_spec = forward(tables, taps.reshape(shape))
    parity = (1 - 2 * (jnp.arange(size, dtype=jnp.int32) % 2)).astype(jnp.float32)[None, :, None]
    parity_top = float(1 - 2 * (size % 2))

    def earlier(stack):
        return jnp.concatenate([jnp.zeros_like(stack[:1]), stack[:-1]], axis=0)

    lag_spec = (
        earlier(taps_spec[0]) + parity * taps_spec[0],
        earlier(taps_spec[1]) + parity * taps_spec[1],
        earlier(taps_spec[2]) + parity_top * taps_spec[2],
    )
    padded = tuple(jnp.concatenate([part, jnp.zeros_like(part)], axis=0) for part in dz_spec)
    du_spec = None
    lag_sums = None
    for offset in range(blocks):
        window = tuple(part[offset : offset + blocks] for part in padded)
        du_term = conj_times(tuple(part[offset] for part in lag_spec), window)
        lag_term = conj_times(tuple(part[offset] for part in gated_spec), window)
        if du_spec is None:
            du_spec, lag_sums = du_term, lag_term
        else:
            du_spec = tuple(a + b for a, b in zip(du_spec, du_term))
            lag_sums = tuple(a + b for a, b in zip(lag_sums, lag_term))
    du = inverse(tables, du_spec, size, size).reshape(seq, chans)
    lagged = inverse(tables, lag_sums, 0, 2 * size)
    later_half = jnp.concatenate([lagged[1:, size:], jnp.zeros_like(lagged[:1, size:])], axis=0)
    filter_grad = (lagged[:, :size] + later_half).reshape(seq, chans) * seq_scale
    return du, filter_grad


def to_groups(value, groups):
    rows, chans = value.shape
    return value.reshape(rows, groups, chans // groups).transpose(1, 0, 2)


def from_groups(value):
    groups, rows, chans = value.shape
    return value.transpose(1, 0, 2).reshape(rows, groups * chans)


def transpose_ctx(stacked):
    return lax.all_to_all(stacked, "ctx", 0, 0, tiled=True)


def body(q_proj, k_proj, v_proj, saved_conv, out_grad, out_weight, filter_taps):
    rows, chans = q_proj.shape
    blocks = lax.axis_size("ctx")
    seq = rows * blocks
    gated = (k_proj.astype(jnp.float32) * v_proj.astype(jnp.float32)).astype(jnp.bfloat16)
    inputs_t = transpose_ctx(
        jnp.stack([to_groups(gated, blocks), to_groups(filter_taps, blocks)], axis=1)
    )
    d_gated = gather_matmul(out_grad, out_weight)
    dq_grad = (d_gated * saved_conv.astype(jnp.float32)).astype(jnp.bfloat16)
    dz = d_gated * q_proj.astype(jnp.float32)
    dz_hi, dz_lo = split_bf16(dz)
    dz_t = transpose_ctx(jnp.stack([to_groups(dz_hi, blocks), to_groups(dz_lo, blocks)], axis=1))
    sub = chans // blocks
    du_t, filter_t = long_correlations(
        dz_t[:, 0].reshape(seq, sub),
        dz_t[:, 1].reshape(seq, sub),
        inputs_t[:, 0].reshape(seq, sub),
        inputs_t[:, 1].reshape(seq, sub),
        float(seq) ** -0.5,
    )
    du_local = from_groups(transpose_ctx(du_t.reshape(blocks, rows, sub)))
    filter_grad = from_groups(transpose_ctx(filter_t.reshape(blocks, rows, sub)))
    dk_grad = (du_local * v_proj.astype(jnp.float32)).astype(jnp.bfloat16)
    dv_grad = (du_local * k_proj.astype(jnp.float32)).astype(jnp.bfloat16)
    return (dq_grad, dk_grad, dv_grad, filter_grad)


def solution(mesh):
    in_specs = (
        P("ctx", "tp"),
        P("ctx", "tp"),
        P("ctx", "tp"),
        P("ctx", "tp"),
        P("ctx", "tp"),
        P("tp", None),
        P("ctx", "tp"),
    )
    out_specs = (P("ctx", "tp"), P("ctx", "tp"), P("ctx", "tp"), P("ctx", "tp"))
    return jax.shard_map(body, mesh=mesh, in_specs=in_specs, out_specs=out_specs, check_vma=False)
```

```python
import math

import jax
import numpy as np
import jax.numpy as jnp
from jax import lax
from jax.sharding import PartitionSpec as P


BLOCK = 128


def split_bf16(value):
    upper = lax.optimization_barrier(value.astype(jnp.bfloat16))
    lower = (value - upper.astype(jnp.float32)).astype(jnp.bfloat16)
    return upper, lower


def gather_matmul(out_grad, out_weight):
    count = lax.axis_size("tp")
    me = lax.axis_index("tp")
    pieces = [out_grad]
    for shift in range(1, count):
        pieces.append(
            lax.ppermute(out_grad, "tp", [(i, (i + shift) % count) for i in range(count)])
        )
    stacked = jnp.stack(pieces)
    ordered = [
        lax.dynamic_index_in_dim(stacked, (me - source) % count, 0, keepdims=False)
        for source in range(count)
    ]
    gathered = jnp.concatenate(ordered, axis=1)
    return lax.dot_general(
        gathered, out_weight, (((1,), (1,)), ((), ())), preferred_element_type=jnp.float32
    )


def split_constant(table):
    upper = table.astype(jnp.bfloat16)
    lower = (table - upper.astype(np.float64)).astype(jnp.bfloat16)
    return jnp.asarray(upper), jnp.asarray(lower)


def make_tables(size):
    index = np.arange(size)
    long_index = np.arange(2 * size)
    angle = (index[:, None] * index[None, :] % (2 * size)) * (math.pi / size)
    angle_back = (long_index[:, None] * index[None, :] % (2 * size)) * (math.pi / size)
    weight = np.where(index == 0, 1.0, 2.0) / (2.0 * size)
    alternate = 1.0 - 2.0 * (index % 2)
    alternate_back = (1.0 - 2.0 * (long_index % 2)) / (2.0 * size)
    return {
        "cos": split_constant(np.cos(angle)),
        "sin": split_constant(-np.sin(angle)),
        "alt": jnp.asarray(alternate.astype(jnp.bfloat16)),
        "icos": split_constant(np.cos(angle_back) * weight[None, :]),
        "isin": split_constant(-np.sin(angle_back) * weight[None, :]),
        "ialt": jnp.asarray(alternate_back.astype(np.float32)),
    }


def apply(table, signal_hi, signal_lo=None):
    def one(left, right):
        return jnp.einsum("kn,bnc->bkc", left, right, preferred_element_type=jnp.float32)

    out = one(table[0], signal_hi) + one(table[1], signal_hi)
    if signal_lo is not None:
        out = out + one(table[0], signal_lo)
    return out


def forward(tables, signal_hi, signal_lo=None):
    real = apply(tables["cos"], signal_hi, signal_lo)
    imag = apply(tables["sin"], signal_hi, signal_lo)
    nyq = jnp.einsum("n,bnc->bc", tables["alt"], signal_hi, preferred_element_type=jnp.float32)
    if signal_lo is not None:
        nyq = nyq + jnp.einsum(
            "n,bnc->bc", tables["alt"], signal_lo, preferred_element_type=jnp.float32
        )
    return real, imag, nyq


def inverse(tables, spectrum, start, count):
    real_hi, real_lo = split_bf16(spectrum[0])
    imag_hi, imag_lo = split_bf16(spectrum[1])
    icos = tuple(t[start : start + count] for t in tables["icos"])
    isin = tuple(t[start : start + count] for t in tables["isin"])
    ialt = tables["ialt"][start : start + count]
    return (
        apply(icos, real_hi, real_lo)
        + apply(isin, imag_hi, imag_lo)
        + ialt[None, :, None] * spectrum[2][:, None, :]
    )


def conj_times(first, second):
    real = first[0][None] * second[0] + first[1][None] * second[1]
    imag = first[0][None] * second[1] - first[1][None] * second[0]
    return real, imag, first[2][None] * second[2]


def long_correlations(dz_hi, dz_lo, gated, taps, seq_scale):
    seq, chans = gated.shape
    size = min(BLOCK, seq)
    blocks = seq // size
    tables = make_tables(size)
    shape = (blocks, size, chans)
    dz_spec = forward(tables, dz_hi.reshape(shape), dz_lo.reshape(shape))
    gated_spec = forward(tables, gated.reshape(shape))
    taps_spec = forward(tables, taps.reshape(shape))
    parity = (1 - 2 * (jnp.arange(size, dtype=jnp.int32) % 2)).astype(jnp.float32)[None, :, None]
    parity_top = float(1 - 2 * (size % 2))

    def earlier(stack):
        return jnp.concatenate([jnp.zeros_like(stack[:1]), stack[:-1]], axis=0)

    lag_spec = (
        earlier(taps_spec[0]) + parity * taps_spec[0],
        earlier(taps_spec[1]) + parity * taps_spec[1],
        earlier(taps_spec[2]) + parity_top * taps_spec[2],
    )
    padded = tuple(jnp.concatenate([part, jnp.zeros_like(part)], axis=0) for part in dz_spec)
    du_spec = None
    lag_sums = None
    for offset in range(blocks):
        window = tuple(part[offset : offset + blocks] for part in padded)
        du_term = conj_times(tuple(part[offset] for part in lag_spec), window)
        lag_term = conj_times(tuple(part[offset] for part in gated_spec), window)
        if du_spec is None:
            du_spec, lag_sums = du_term, lag_term
        else:
            du_spec = tuple(a + b for a, b in zip(du_spec, du_term))
            lag_sums = tuple(a + b for a, b in zip(lag_sums, lag_term))
    du = inverse(tables, du_spec, size, size).reshape(seq, chans)
    lagged = inverse(tables, lag_sums, 0, 2 * size)
    later_half = jnp.concatenate([lagged[1:, size:], jnp.zeros_like(lagged[:1, size:])], axis=0)
    filter_grad = (lagged[:, :size] + later_half).reshape(seq, chans) * seq_scale
    return du, filter_grad


def to_groups(value, groups):
    rows, chans = value.shape
    return value.reshape(rows, groups, chans // groups).transpose(1, 0, 2)


def from_groups(value):
    groups, rows, chans = value.shape
    return value.transpose(1, 0, 2).reshape(rows, groups * chans)


def transpose_ctx(stacked):
    return lax.all_to_all(stacked, "ctx", 0, 0, tiled=True)


def body(q_proj, k_proj, v_proj, saved_conv, out_grad, out_weight, filter_taps):
    rows, chans = q_proj.shape
    blocks = lax.axis_size("ctx")
    seq = rows * blocks
    gated = (k_proj.astype(jnp.float32) * v_proj.astype(jnp.float32)).astype(jnp.bfloat16)
    inputs_t = transpose_ctx(
        jnp.stack([to_groups(gated, blocks), to_groups(filter_taps, blocks)], axis=1)
    )
    d_gated = gather_matmul(out_grad, out_weight)
    dq_grad = (d_gated * saved_conv.astype(jnp.float32)).astype(jnp.bfloat16)
    dz = d_gated * q_proj.astype(jnp.float32)
    dz_hi, dz_lo = split_bf16(dz)
    dz_t = transpose_ctx(jnp.stack([to_groups(dz_hi, blocks), to_groups(dz_lo, blocks)], axis=1))
    sub = chans // blocks
    du_t, filter_t = long_correlations(
        dz_t[:, 0].reshape(seq, sub),
        dz_t[:, 1].reshape(seq, sub),
        inputs_t[:, 0].reshape(seq, sub),
        inputs_t[:, 1].reshape(seq, sub),
        float(seq) ** -0.5,
    )
    back = transpose_ctx(jnp.stack([du_t, filter_t], axis=1).reshape(blocks, rows, 2, sub))
    du_local = from_groups(back[:, :, 0])
    filter_grad = from_groups(back[:, :, 1])
    dk_grad = (du_local * v_proj.astype(jnp.float32)).astype(jnp.bfloat16)
    dv_grad = (du_local * k_proj.astype(jnp.float32)).astype(jnp.bfloat16)
    return (dq_grad, dk_grad, dv_grad, filter_grad)


def solution(mesh):
    in_specs = (
        P("ctx", "tp"),
        P("ctx", "tp"),
        P("ctx", "tp"),
        P("ctx", "tp"),
        P("ctx", "tp"),
        P("tp", None),
        P("ctx", "tp"),
    )
    out_specs = (P("ctx", "tp"), P("ctx", "tp"), P("ctx", "tp"), P("ctx", "tp"))
    return jax.shard_map(body, mesh=mesh, in_specs=in_specs, out_specs=out_specs, check_vma=False)
```

```python
import math

import jax
import numpy as np
import jax.numpy as jnp
from jax import lax
from jax.sharding import PartitionSpec as P


BLOCK = 128


def split_bf16(value):
    upper = lax.optimization_barrier(value.astype(jnp.bfloat16))
    lower = (value - upper.astype(jnp.float32)).astype(jnp.bfloat16)
    return upper, lower


def gather_tp(out_grad):
    count = lax.axis_size("tp")
    me = lax.axis_index("tp")
    pieces = [out_grad]
    for shift in range(1, count):
        pieces.append(
            lax.ppermute(out_grad, "tp", [(i, (i + shift) % count) for i in range(count)])
        )
    stacked = jnp.stack(pieces)
    ordered = [
        lax.dynamic_index_in_dim(stacked, (me - source) % count, 0, keepdims=False)
        for source in range(count)
    ]
    return jnp.concatenate(ordered, axis=1)


def split_constant(table):
    upper = table.astype(jnp.bfloat16)
    lower = (table - upper.astype(np.float64)).astype(jnp.bfloat16)
    return jnp.asarray(upper), jnp.asarray(lower)


def make_tables(size):
    index = np.arange(size)
    long_index = np.arange(2 * size)
    angle = (index[:, None] * index[None, :] % (2 * size)) * (math.pi / size)
    angle_back = (long_index[:, None] * index[None, :] % (2 * size)) * (math.pi / size)
    weight = np.where(index == 0, 1.0, 2.0) / (2.0 * size)
    alternate = 1.0 - 2.0 * (index % 2)
    alternate_back = (1.0 - 2.0 * (long_index % 2)) / (2.0 * size)
    return {
        "cos": split_constant(np.cos(angle)),
        "sin": split_constant(-np.sin(angle)),
        "alt": jnp.asarray(alternate.astype(jnp.bfloat16)),
        "icos": split_constant(np.cos(angle_back) * weight[None, :]),
        "isin": split_constant(-np.sin(angle_back) * weight[None, :]),
        "ialt": jnp.asarray(alternate_back.astype(np.float32)),
    }


def apply(table, signal_hi, signal_lo=None):
    def one(left, right):
        return jnp.einsum("kn,bnc->bkc", left, right, preferred_element_type=jnp.float32)

    out = one(table[0], signal_hi) + one(table[1], signal_hi)
    if signal_lo is not None:
        out = out + one(table[0], signal_lo)
    return out


def forward(tables, signal_hi, signal_lo=None):
    real = apply(tables["cos"], signal_hi, signal_lo)
    imag = apply(tables["sin"], signal_hi, signal_lo)
    nyq = jnp.einsum("n,bnc->bc", tables["alt"], signal_hi, preferred_element_type=jnp.float32)
    if signal_lo is not None:
        nyq = nyq + jnp.einsum(
            "n,bnc->bc", tables["alt"], signal_lo, preferred_element_type=jnp.float32
        )
    return real, imag, nyq


def inverse(tables, spectrum, start, count):
    real_hi, real_lo = split_bf16(spectrum[0])
    imag_hi, imag_lo = split_bf16(spectrum[1])
    icos = tuple(t[start : start + count] for t in tables["icos"])
    isin = tuple(t[start : start + count] for t in tables["isin"])
    ialt = tables["ialt"][start : start + count]
    return (
        apply(icos, real_hi, real_lo)
        + apply(isin, imag_hi, imag_lo)
        + ialt[None, :, None] * spectrum[2][:, None, :]
    )


def conj_times(first, second):
    real = first[0][None] * second[0] + first[1][None] * second[1]
    imag = first[0][None] * second[1] - first[1][None] * second[0]
    return real, imag, first[2][None] * second[2]


def long_correlations(dz_hi, dz_lo, gated, taps, seq_scale):
    seq, chans = gated.shape
    size = min(BLOCK, seq)
    blocks = seq // size
    tables = make_tables(size)
    shape = (blocks, size, chans)
    dz_spec = forward(tables, dz_hi.reshape(shape), dz_lo.reshape(shape))
    gated_spec = forward(tables, gated.reshape(shape))
    taps_spec = forward(tables, taps.reshape(shape))
    parity = (1 - 2 * (jnp.arange(size, dtype=jnp.int32) % 2)).astype(jnp.float32)[None, :, None]
    parity_top = float(1 - 2 * (size % 2))

    def earlier(stack):
        return jnp.concatenate([jnp.zeros_like(stack[:1]), stack[:-1]], axis=0)

    lag_spec = (
        earlier(taps_spec[0]) + parity * taps_spec[0],
        earlier(taps_spec[1]) + parity * taps_spec[1],
        earlier(taps_spec[2]) + parity_top * taps_spec[2],
    )
    padded = tuple(jnp.concatenate([part, jnp.zeros_like(part)], axis=0) for part in dz_spec)
    du_spec = None
    lag_sums = None
    for offset in range(blocks):
        window = tuple(part[offset : offset + blocks] for part in padded)
        du_term = conj_times(tuple(part[offset] for part in lag_spec), window)
        lag_term = conj_times(tuple(part[offset] for part in gated_spec), window)
        if du_spec is None:
            du_spec, lag_sums = du_term, lag_term
        else:
            du_spec = tuple(a + b for a, b in zip(du_spec, du_term))
            lag_sums = tuple(a + b for a, b in zip(lag_sums, lag_term))
    du = inverse(tables, du_spec, size, size).reshape(seq, chans)
    lagged = inverse(tables, lag_sums, 0, 2 * size)
    later_half = jnp.concatenate([lagged[1:, size:], jnp.zeros_like(lagged[:1, size:])], axis=0)
    filter_grad = (lagged[:, :size] + later_half).reshape(seq, chans) * seq_scale
    return du, filter_grad


def transpose_ctx(stacked):
    return lax.all_to_all(stacked, "ctx", 0, 0, tiled=True)


def body(q_proj, k_proj, v_proj, saved_conv, out_grad, out_weight, filter_taps):
    rows, chans = q_proj.shape
    blocks = lax.axis_size("ctx")
    seq = rows * blocks
    sub = chans // blocks
    halves = 2 if sub % 2 == 0 else 1
    part = sub // halves
    split = (rows, blocks, halves, part)

    def grouped(value):
        return value.reshape(split).transpose(1, 2, 0, 3)

    gated = (k_proj.astype(jnp.float32) * v_proj.astype(jnp.float32)).astype(jnp.bfloat16)
    inputs_t = transpose_ctx(jnp.stack([grouped(gated), grouped(filter_taps)], axis=2))
    gathered = gather_tp(out_grad)
    weight = out_weight.reshape(blocks, halves, part, out_weight.shape[1])
    queries = q_proj.reshape(split)
    saved = saved_conv.reshape(split)
    dq_parts = []
    back_parts = []
    for half in range(halves):
        d_gated = jnp.einsum(
            "to,gjo->tgj", gathered, weight[:, half], preferred_element_type=jnp.float32
        )
        dq_parts.append((d_gated * saved[:, :, half].astype(jnp.float32)).astype(jnp.bfloat16))
        dz = d_gated * queries[:, :, half].astype(jnp.float32)
        dz_hi, dz_lo = split_bf16(dz)
        dz_t = transpose_ctx(jnp.stack([dz_hi, dz_lo]).transpose(2, 0, 1, 3))
        du_t, filter_t = long_correlations(
            dz_t[:, 0].reshape(seq, part),
            dz_t[:, 1].reshape(seq, part),
            inputs_t[:, half, 0].reshape(seq, part),
            inputs_t[:, half, 1].reshape(seq, part),
            float(seq) ** -0.5,
        )
        back_parts.append(
            transpose_ctx(jnp.stack([du_t, filter_t]).reshape(2, blocks, rows, part).transpose(1, 0, 2, 3))
        )
    dq_grad = jnp.stack(dq_parts, axis=2).reshape(rows, chans)
    back = jnp.stack(back_parts, axis=2)
    du_local = back[:, 0].transpose(2, 0, 1, 3).reshape(rows, chans)
    filter_grad = back[:, 1].transpose(2, 0, 1, 3).reshape(rows, chans)
    dk_grad = (du_local * v_proj.astype(jnp.float32)).astype(jnp.bfloat16)
    dv_grad = (du_local * k_proj.astype(jnp.float32)).astype(jnp.bfloat16)
    return (dq_grad, dk_grad, dv_grad, filter_grad)


def solution(mesh):
    in_specs = (
        P("ctx", "tp"),
        P("ctx", "tp"),
        P("ctx", "tp"),
        P("ctx", "tp"),
        P("ctx", "tp"),
        P("tp", None),
        P("ctx", "tp"),
    )
    out_specs = (P("ctx", "tp"), P("ctx", "tp"), P("ctx", "tp"), P("ctx", "tp"))
    return jax.shard_map(body, mesh=mesh, in_specs=in_specs, out_specs=out_specs, check_vma=False)
```

```python
import math

import jax
import numpy as np
import jax.numpy as jnp
from jax import lax
from jax.sharding import PartitionSpec as P


BLOCK = 128


def split_bf16(value):
    upper = lax.optimization_barrier(value.astype(jnp.bfloat16))
    lower = (value - upper.astype(jnp.float32)).astype(jnp.bfloat16)
    return upper, lower


def gather_matmul(out_grad, out_weight):
    count = lax.axis_size("tp")
    me = lax.axis_index("tp")
    pieces = [out_grad]
    for shift in range(1, count):
        pieces.append(
            lax.ppermute(out_grad, "tp", [(i, (i + shift) % count) for i in range(count)])
        )
    stacked = jnp.stack(pieces)
    ordered = [
        lax.dynamic_index_in_dim(stacked, (me - source) % count, 0, keepdims=False)
        for source in range(count)
    ]
    gathered = jnp.concatenate(ordered, axis=1)
    return lax.dot_general(
        gathered, out_weight, (((1,), (1,)), ((), ())), preferred_element_type=jnp.float32
    )


def split_constant(table):
    upper = table.astype(jnp.bfloat16)
    lower = (table - upper.astype(np.float64)).astype(jnp.bfloat16)
    return jnp.asarray(upper), jnp.asarray(lower)


def make_tables(size):
    index = np.arange(size)
    long_index = np.arange(2 * size)
    angle = (index[:, None] * index[None, :] % (2 * size)) * (math.pi / size)
    angle_back = (long_index[:, None] * index[None, :] % (2 * size)) * (math.pi / size)
    weight = np.where(index == 0, 1.0, 2.0) / (2.0 * size)
    alternate = 1.0 - 2.0 * (index % 2)
    alternate_back = (1.0 - 2.0 * (long_index % 2)) / (2.0 * size)
    return {
        "cos": split_constant(np.cos(angle)),
        "sin": split_constant(-np.sin(angle)),
        "alt": jnp.asarray(alternate.astype(jnp.bfloat16)),
        "icos": split_constant(np.cos(angle_back) * weight[None, :]),
        "isin": split_constant(-np.sin(angle_back) * weight[None, :]),
        "ialt": jnp.asarray(alternate_back.astype(np.float32)),
    }


def apply(table, signal_hi, signal_lo=None):
    def one(left, right):
        return jnp.einsum("kn,bnc->bkc", left, right, preferred_element_type=jnp.float32)

    out = one(table[0], signal_hi) + one(table[1], signal_hi)
    if signal_lo is not None:
        out = out + one(table[0], signal_lo)
    return out


def forward(tables, signal_hi, signal_lo=None):
    real = apply(tables["cos"], signal_hi, signal_lo)
    imag = apply(tables["sin"], signal_hi, signal_lo)
    nyq = jnp.einsum("n,bnc->bc", tables["alt"], signal_hi, preferred_element_type=jnp.float32)
    if signal_lo is not None:
        nyq = nyq + jnp.einsum(
            "n,bnc->bc", tables["alt"], signal_lo, preferred_element_type=jnp.float32
        )
    return real, imag, nyq


def inverse(tables, spectrum, start, count):
    real_hi, real_lo = split_bf16(spectrum[0])
    imag_hi, imag_lo = split_bf16(spectrum[1])
    icos = tuple(t[start : start + count] for t in tables["icos"])
    isin = tuple(t[start : start + count] for t in tables["isin"])
    ialt = tables["ialt"][start : start + count]
    return (
        apply(icos, real_hi, real_lo)
        + apply(isin, imag_hi, imag_lo)
        + ialt[None, :, None] * spectrum[2][:, None, :]
    )


def conj_times(first, second):
    real = first[0][None] * second[0] + first[1][None] * second[1]
    imag = first[0][None] * second[1] - first[1][None] * second[0]
    return real, imag, first[2][None] * second[2]


def long_correlations(dz_hi, dz_lo, gated, taps, seq_scale):
    seq, chans = gated.shape
    size = min(BLOCK, seq)
    blocks = seq // size
    tables = make_tables(size)
    shape = (blocks, size, chans)
    dz_spec = forward(tables, dz_hi.reshape(shape), dz_lo.reshape(shape))
    gated_spec = forward(tables, gated.reshape(shape))
    taps_spec = forward(tables, taps.reshape(shape))
    parity = (1 - 2 * (jnp.arange(size, dtype=jnp.int32) % 2)).astype(jnp.float32)[None, :, None]
    parity_top = float(1 - 2 * (size % 2))

    def earlier(stack):
        return jnp.concatenate([jnp.zeros_like(stack[:1]), stack[:-1]], axis=0)

    lag_spec = (
        earlier(taps_spec[0]) + parity * taps_spec[0],
        earlier(taps_spec[1]) + parity * taps_spec[1],
        earlier(taps_spec[2]) + parity_top * taps_spec[2],
    )
    padded = tuple(jnp.concatenate([part, jnp.zeros_like(part)], axis=0) for part in dz_spec)
    du_spec = None
    lag_sums = None
    for offset in range(blocks):
        window = tuple(part[offset : offset + blocks] for part in padded)
        du_term = conj_times(tuple(part[offset] for part in lag_spec), window)
        lag_term = conj_times(tuple(part[offset] for part in gated_spec), window)
        if du_spec is None:
            du_spec, lag_sums = du_term, lag_term
        else:
            du_spec = tuple(a + b for a, b in zip(du_spec, du_term))
            lag_sums = tuple(a + b for a, b in zip(lag_sums, lag_term))
    du = inverse(tables, du_spec, size, size).reshape(seq, chans)
    lagged = inverse(tables, lag_sums, 0, 2 * size)
    later_half = jnp.concatenate([lagged[1:, size:], jnp.zeros_like(lagged[:1, size:])], axis=0)
    filter_grad = (lagged[:, :size] + later_half).reshape(seq, chans) * seq_scale
    return du, filter_grad


def to_groups(value, groups):
    rows, chans = value.shape
    return value.reshape(rows, groups, chans // groups).transpose(1, 0, 2)


def from_groups(value):
    groups, rows, chans = value.shape
    return value.transpose(1, 0, 2).reshape(rows, groups * chans)


def transpose_ctx(stacked):
    count = lax.axis_size("ctx")
    me = lax.axis_index("ctx")
    received = []
    for shift in range(count):
        chunk = lax.dynamic_index_in_dim(stacked, (me + shift) % count, 0, keepdims=False)
        if shift:
            chunk = lax.ppermute(chunk, "ctx", [(i, (i + shift) % count) for i in range(count)])
        received.append(chunk)
    received = jnp.stack(received)
    return jnp.stack(
        [
            lax.dynamic_index_in_dim(received, (me - source) % count, 0, keepdims=False)
            for source in range(count)
        ]
    )


def body(q_proj, k_proj, v_proj, saved_conv, out_grad, out_weight, filter_taps):
    rows, chans = q_proj.shape
    blocks = lax.axis_size("ctx")
    seq = rows * blocks
    gated = (k_proj.astype(jnp.float32) * v_proj.astype(jnp.float32)).astype(jnp.bfloat16)
    inputs_t = transpose_ctx(
        jnp.stack([to_groups(gated, blocks), to_groups(filter_taps, blocks)], axis=1)
    )
    d_gated = gather_matmul(out_grad, out_weight)
    dq_grad = (d_gated * saved_conv.astype(jnp.float32)).astype(jnp.bfloat16)
    dz = d_gated * q_proj.astype(jnp.float32)
    dz_hi, dz_lo = split_bf16(dz)
    dz_t = transpose_ctx(jnp.stack([to_groups(dz_hi, blocks), to_groups(dz_lo, blocks)], axis=1))
    sub = chans // blocks
    du_t, filter_t = long_correlations(
        dz_t[:, 0].reshape(seq, sub),
        dz_t[:, 1].reshape(seq, sub),
        inputs_t[:, 0].reshape(seq, sub),
        inputs_t[:, 1].reshape(seq, sub),
        float(seq) ** -0.5,
    )
    back = transpose_ctx(jnp.stack([du_t, filter_t], axis=1).reshape(blocks, rows, 2, sub))
    du_local = from_groups(back[:, :, 0])
    filter_grad = from_groups(back[:, :, 1])
    dk_grad = (du_local * v_proj.astype(jnp.float32)).astype(jnp.bfloat16)
    dv_grad = (du_local * k_proj.astype(jnp.float32)).astype(jnp.bfloat16)
    return (dq_grad, dk_grad, dv_grad, filter_grad)


def solution(mesh):
    in_specs = (
        P("ctx", "tp"),
        P("ctx", "tp"),
        P("ctx", "tp"),
        P("ctx", "tp"),
        P("ctx", "tp"),
        P("tp", None),
        P("ctx", "tp"),
    )
    out_specs = (P("ctx", "tp"), P("ctx", "tp"), P("ctx", "tp"), P("ctx", "tp"))
    return jax.shard_map(body, mesh=mesh, in_specs=in_specs, out_specs=out_specs, check_vma=False)
```

```python
import math

import jax
import numpy as np
import jax.numpy as jnp
from jax import lax
from jax.sharding import PartitionSpec as P


BLOCK = 128


def split_bf16(value):
    upper = lax.optimization_barrier(value.astype(jnp.bfloat16))
    lower = (value - upper.astype(jnp.float32)).astype(jnp.bfloat16)
    return upper, lower


def gather_tp(out_grad):
    count = lax.axis_size("tp")
    me = lax.axis_index("tp")
    pieces = [out_grad]
    for shift in range(1, count):
        pieces.append(
            lax.ppermute(out_grad, "tp", [(i, (i + shift) % count) for i in range(count)])
        )
    stacked = jnp.stack(pieces)
    ordered = [
        lax.dynamic_index_in_dim(stacked, (me - source) % count, 0, keepdims=False)
        for source in range(count)
    ]
    return jnp.concatenate(ordered, axis=1)


def split_constant(table):
    upper = table.astype(jnp.bfloat16)
    lower = (table - upper.astype(np.float64)).astype(jnp.bfloat16)
    return jnp.asarray(upper), jnp.asarray(lower)


def make_tables(size):
    index = np.arange(size)
    long_index = np.arange(2 * size)
    angle = (index[:, None] * index[None, :] % (2 * size)) * (math.pi / size)
    angle_back = (long_index[:, None] * index[None, :] % (2 * size)) * (math.pi / size)
    weight = np.where(index == 0, 1.0, 2.0) / (2.0 * size)
    alternate = 1.0 - 2.0 * (index % 2)
    alternate_back = (1.0 - 2.0 * (long_index % 2)) / (2.0 * size)
    return {
        "cos": split_constant(np.cos(angle)),
        "sin": split_constant(-np.sin(angle)),
        "alt": jnp.asarray(alternate.astype(jnp.bfloat16)),
        "icos": split_constant(np.cos(angle_back) * weight[None, :]),
        "isin": split_constant(-np.sin(angle_back) * weight[None, :]),
        "ialt": jnp.asarray(alternate_back.astype(np.float32)),
    }


def apply(table, signal_hi, signal_lo=None):
    def one(left, right):
        return jnp.einsum("kn,bnc->bkc", left, right, preferred_element_type=jnp.float32)

    out = one(table[0], signal_hi) + one(table[1], signal_hi)
    if signal_lo is not None:
        out = out + one(table[0], signal_lo)
    return out


def forward(tables, signal_hi, signal_lo=None):
    real = apply(tables["cos"], signal_hi, signal_lo)
    imag = apply(tables["sin"], signal_hi, signal_lo)
    nyq = jnp.einsum("n,bnc->bc", tables["alt"], signal_hi, preferred_element_type=jnp.float32)
    if signal_lo is not None:
        nyq = nyq + jnp.einsum(
            "n,bnc->bc", tables["alt"], signal_lo, preferred_element_type=jnp.float32
        )
    return real, imag, nyq


def inverse(tables, spectrum, start, count):
    real_hi, real_lo = split_bf16(spectrum[0])
    imag_hi, imag_lo = split_bf16(spectrum[1])
    icos = tuple(t[start : start + count] for t in tables["icos"])
    isin = tuple(t[start : start + count] for t in tables["isin"])
    ialt = tables["ialt"][start : start + count]
    return (
        apply(icos, real_hi, real_lo)
        + apply(isin, imag_hi, imag_lo)
        + ialt[None, :, None] * spectrum[2][:, None, :]
    )


def conj_times(first, second):
    real = first[0][None] * second[0] + first[1][None] * second[1]
    imag = first[0][None] * second[1] - first[1][None] * second[0]
    return real, imag, first[2][None] * second[2]


def long_correlations(dz_hi, dz_lo, gated, taps, seq_scale):
    seq, chans = gated.shape
    size = min(BLOCK, seq)
    blocks = seq // size
    tables = make_tables(size)
    shape = (blocks, size, chans)
    dz_spec = forward(tables, dz_hi.reshape(shape), dz_lo.reshape(shape))
    gated_spec = forward(tables, gated.reshape(shape))
    taps_spec = forward(tables, taps.reshape(shape))
    parity = (1 - 2 * (jnp.arange(size, dtype=jnp.int32) % 2)).astype(jnp.float32)[None, :, None]
    parity_top = float(1 - 2 * (size % 2))

    def earlier(stack):
        return jnp.concatenate([jnp.zeros_like(stack[:1]), stack[:-1]], axis=0)

    lag_spec = (
        earlier(taps_spec[0]) + parity * taps_spec[0],
        earlier(taps_spec[1]) + parity * taps_spec[1],
        earlier(taps_spec[2]) + parity_top * taps_spec[2],
    )
    padded = tuple(jnp.concatenate([part, jnp.zeros_like(part)], axis=0) for part in dz_spec)
    du_spec = None
    lag_sums = None
    for offset in range(blocks):
        window = tuple(part[offset : offset + blocks] for part in padded)
        du_term = conj_times(tuple(part[offset] for part in lag_spec), window)
        lag_term = conj_times(tuple(part[offset] for part in gated_spec), window)
        if du_spec is None:
            du_spec, lag_sums = du_term, lag_term
        else:
            du_spec = tuple(a + b for a, b in zip(du_spec, du_term))
            lag_sums = tuple(a + b for a, b in zip(lag_sums, lag_term))
    du = inverse(tables, du_spec, size, size).reshape(seq, chans)
    lagged = inverse(tables, lag_sums, 0, 2 * size)
    later_half = jnp.concatenate([lagged[1:, size:], jnp.zeros_like(lagged[:1, size:])], axis=0)
    filter_grad = (lagged[:, :size] + later_half).reshape(seq, chans) * seq_scale
    return du, filter_grad


def to_groups(value, groups):
    rows, chans = value.shape
    return value.reshape(rows, groups, chans // groups).transpose(1, 0, 2)


def from_groups(value):
    groups, rows, chans = value.shape
    return value.transpose(1, 0, 2).reshape(rows, groups * chans)


def transpose_ctx(stacked):
    count = lax.axis_size("ctx")
    me = lax.axis_index("ctx")
    received = []
    for shift in range(count):
        chunk = lax.dynamic_index_in_dim(stacked, (me + shift) % count, 0, keepdims=False)
        if shift:
            chunk = lax.ppermute(chunk, "ctx", [(i, (i + shift) % count) for i in range(count)])
        received.append(chunk)
    received = jnp.stack(received)
    return jnp.stack(
        [
            lax.dynamic_index_in_dim(received, (me - source) % count, 0, keepdims=False)
            for source in range(count)
        ]
    )


def body(q_proj, k_proj, v_proj, saved_conv, out_grad, out_weight, filter_taps):
    rows, chans = q_proj.shape
    blocks = lax.axis_size("ctx")
    seq = rows * blocks
    gated = (k_proj.astype(jnp.float32) * v_proj.astype(jnp.float32)).astype(jnp.bfloat16)
    inputs = jnp.stack([to_groups(gated, blocks), to_groups(filter_taps, blocks)], axis=1)
    gathered = gather_tp(out_grad)
    gathered, inputs = lax.optimization_barrier((gathered, inputs))
    inputs_t = transpose_ctx(inputs)
    d_gated = lax.dot_general(
        gathered, out_weight, (((1,), (1,)), ((), ())), preferred_element_type=jnp.float32
    )
    dq_grad = (d_gated * saved_conv.astype(jnp.float32)).astype(jnp.bfloat16)
    dz = d_gated * q_proj.astype(jnp.float32)
    dz_hi, dz_lo = split_bf16(dz)
    dz_t = transpose_ctx(jnp.stack([to_groups(dz_hi, blocks), to_groups(dz_lo, blocks)], axis=1))
    sub = chans // blocks
    du_t, filter_t = long_correlations(
        dz_t[:, 0].reshape(seq, sub),
        dz_t[:, 1].reshape(seq, sub),
        inputs_t[:, 0].reshape(seq, sub),
        inputs_t[:, 1].reshape(seq, sub),
        float(seq) ** -0.5,
    )
    back = transpose_ctx(jnp.stack([du_t, filter_t], axis=1).reshape(blocks, rows, 2, sub))
    du_local = from_groups(back[:, :, 0])
    filter_grad = from_groups(back[:, :, 1])
    dk_grad = (du_local * v_proj.astype(jnp.float32)).astype(jnp.bfloat16)
    dv_grad = (du_local * k_proj.astype(jnp.float32)).astype(jnp.bfloat16)
    return (dq_grad, dk_grad, dv_grad, filter_grad)


def solution(mesh):
    in_specs = (
        P("ctx", "tp"),
        P("ctx", "tp"),
        P("ctx", "tp"),
        P("ctx", "tp"),
        P("ctx", "tp"),
        P("tp", None),
        P("ctx", "tp"),
    )
    out_specs = (P("ctx", "tp"), P("ctx", "tp"), P("ctx", "tp"), P("ctx", "tp"))
    return jax.shard_map(body, mesh=mesh, in_specs=in_specs, out_specs=out_specs, check_vma=False)
```

```python
import math

import jax
import numpy as np
import jax.numpy as jnp
from jax import lax
from jax.sharding import PartitionSpec as P


BLOCK = 128


def split_bf16(value):
    upper = lax.optimization_barrier(value.astype(jnp.bfloat16))
    lower = (value - upper.astype(jnp.float32)).astype(jnp.bfloat16)
    return upper, lower


def partner_of(index, step, count):
    if count & (count - 1) == 0:
        return index ^ step
    return (index + step) % count


def source_of(index, step, count):
    if count & (count - 1) == 0:
        return index ^ step
    return (index - step) % count


def exchange(value, axis, step):
    count = lax.axis_size(axis)
    return lax.ppermute(value, axis, [(i, partner_of(i, step, count)) for i in range(count)])


def gather_matmul(out_grad, out_weight):
    count = lax.axis_size("tp")
    me = lax.axis_index("tp")
    pieces = [out_grad] + [exchange(out_grad, "tp", step) for step in range(1, count)]
    stacked = jnp.stack(pieces)
    ordered = [
        lax.dynamic_index_in_dim(stacked, source_of(me, source, count), 0, keepdims=False)
        for source in range(count)
    ]
    gathered = jnp.concatenate(ordered, axis=1)
    return lax.dot_general(
        gathered, out_weight, (((1,), (1,)), ((), ())), preferred_element_type=jnp.float32
    )


def split_constant(table):
    upper = table.astype(jnp.bfloat16)
    lower = (table - upper.astype(np.float64)).astype(jnp.bfloat16)
    return jnp.asarray(upper), jnp.asarray(lower)


def make_tables(size):
    index = np.arange(size)
    long_index = np.arange(2 * size)
    angle = (index[:, None] * index[None, :] % (2 * size)) * (math.pi / size)
    angle_back = (long_index[:, None] * index[None, :] % (2 * size)) * (math.pi / size)
    weight = np.where(index == 0, 1.0, 2.0) / (2.0 * size)
    alternate = 1.0 - 2.0 * (index % 2)
    alternate_back = (1.0 - 2.0 * (long_index % 2)) / (2.0 * size)
    return {
        "cos": split_constant(np.cos(angle)),
        "sin": split_constant(-np.sin(angle)),
        "alt": jnp.asarray(alternate.astype(jnp.bfloat16)),
        "icos": split_constant(np.cos(angle_back) * weight[None, :]),
        "isin": split_constant(-np.sin(angle_back) * weight[None, :]),
        "ialt": jnp.asarray(alternate_back.astype(np.float32)),
    }


def apply(table, signal_hi, signal_lo=None):
    def one(left, right):
        return jnp.einsum("kn,bnc->bkc", left, right, preferred_element_type=jnp.float32)

    out = one(table[0], signal_hi) + one(table[1], signal_hi)
    if signal_lo is not None:
        out = out + one(table[0], signal_lo)
    return out


def forward(tables, signal_hi, signal_lo=None):
    real = apply(tables["cos"], signal_hi, signal_lo)
    imag = apply(tables["sin"], signal_hi, signal_lo)
    nyq = jnp.einsum("n,bnc->bc", tables["alt"], signal_hi, preferred_element_type=jnp.float32)
    if signal_lo is not None:
        nyq = nyq + jnp.einsum(
            "n,bnc->bc", tables["alt"], signal_lo, preferred_element_type=jnp.float32
        )
    return real, imag, nyq


def inverse(tables, spectrum, start, count):
    real_hi, real_lo = split_bf16(spectrum[0])
    imag_hi, imag_lo = split_bf16(spectrum[1])
    icos = tuple(t[start : start + count] for t in tables["icos"])
    isin = tuple(t[start : start + count] for t in tables["isin"])
    ialt = tables["ialt"][start : start + count]
    return (
        apply(icos, real_hi, real_lo)
        + apply(isin, imag_hi, imag_lo)
        + ialt[None, :, None] * spectrum[2][:, None, :]
    )


def conj_times(first, second):
    real = first[0][None] * second[0] + first[1][None] * second[1]
    imag = first[0][None] * second[1] - first[1][None] * second[0]
    return real, imag, first[2][None] * second[2]


def long_correlations(dz_hi, dz_lo, gated, taps, seq_scale):
    seq, chans = gated.shape
    size = min(BLOCK, seq)
    blocks = seq // size
    tables = make_tables(size)
    shape = (blocks, size, chans)
    dz_spec = forward(tables, dz_hi.reshape(shape), dz_lo.reshape(shape))
    gated_spec = forward(tables, gated.reshape(shape))
    taps_spec = forward(tables, taps.reshape(shape))
    parity = (1 - 2 * (jnp.arange(size, dtype=jnp.int32) % 2)).astype(jnp.float32)[None, :, None]
    parity_top = float(1 - 2 * (size % 2))

    def earlier(stack):
        return jnp.concatenate([jnp.zeros_like(stack[:1]), stack[:-1]], axis=0)

    lag_spec = (
        earlier(taps_spec[0]) + parity * taps_spec[0],
        earlier(taps_spec[1]) + parity * taps_spec[1],
        earlier(taps_spec[2]) + parity_top * taps_spec[2],
    )
    padded = tuple(jnp.concatenate([part, jnp.zeros_like(part)], axis=0) for part in dz_spec)
    du_spec = None
    lag_sums = None
    for offset in range(blocks):
        window = tuple(part[offset : offset + blocks] for part in padded)
        du_term = conj_times(tuple(part[offset] for part in lag_spec), window)
        lag_term = conj_times(tuple(part[offset] for part in gated_spec), window)
        if du_spec is None:
            du_spec, lag_sums = du_term, lag_term
        else:
            du_spec = tuple(a + b for a, b in zip(du_spec, du_term))
            lag_sums = tuple(a + b for a, b in zip(lag_sums, lag_term))
    du = inverse(tables, du_spec, size, size).reshape(seq, chans)
    lagged = inverse(tables, lag_sums, 0, 2 * size)
    later_half = jnp.concatenate([lagged[1:, size:], jnp.zeros_like(lagged[:1, size:])], axis=0)
    filter_grad = (lagged[:, :size] + later_half).reshape(seq, chans) * seq_scale
    return du, filter_grad


def to_groups(value, groups):
    rows, chans = value.shape
    return value.reshape(rows, groups, chans // groups).transpose(1, 0, 2)


def from_groups(value):
    groups, rows, chans = value.shape
    return value.transpose(1, 0, 2).reshape(rows, groups * chans)


def transpose_ctx(stacked):
    count = lax.axis_size("ctx")
    me = lax.axis_index("ctx")
    received = []
    for step in range(count):
        chunk = lax.dynamic_index_in_dim(stacked, partner_of(me, step, count), 0, keepdims=False)
        if step:
            chunk = exchange(chunk, "ctx", step)
        received.append(chunk)
    received = jnp.stack(received)
    return jnp.stack(
        [
            lax.dynamic_index_in_dim(received, source_of(me, source, count), 0, keepdims=False)
            for source in range(count)
        ]
    )


def body(q_proj, k_proj, v_proj, saved_conv, out_grad, out_weight, filter_taps):
    rows, chans = q_proj.shape
    blocks = lax.axis_size("ctx")
    seq = rows * blocks
    gated = (k_proj.astype(jnp.float32) * v_proj.astype(jnp.float32)).astype(jnp.bfloat16)
    inputs_t = transpose_ctx(
        jnp.stack([to_groups(gated, blocks), to_groups(filter_taps, blocks)], axis=1)
    )
    d_gated = gather_matmul(out_grad, out_weight)
    dq_grad = (d_gated * saved_conv.astype(jnp.float32)).astype(jnp.bfloat16)
    dz = d_gated * q_proj.astype(jnp.float32)
    dz_hi, dz_lo = split_bf16(dz)
    dz_t = transpose_ctx(jnp.stack([to_groups(dz_hi, blocks), to_groups(dz_lo, blocks)], axis=1))
    sub = chans // blocks
    du_t, filter_t = long_correlations(
        dz_t[:, 0].reshape(seq, sub),
        dz_t[:, 1].reshape(seq, sub),
        inputs_t[:, 0].reshape(seq, sub),
        inputs_t[:, 1].reshape(seq, sub),
        float(seq) ** -0.5,
    )
    back = transpose_ctx(jnp.stack([du_t, filter_t], axis=1).reshape(blocks, rows, 2, sub))
    du_local = from_groups(back[:, :, 0])
    filter_grad = from_groups(back[:, :, 1])
    dk_grad = (du_local * v_proj.astype(jnp.float32)).astype(jnp.bfloat16)
    dv_grad = (du_local * k_proj.astype(jnp.float32)).astype(jnp.bfloat16)
    return (dq_grad, dk_grad, dv_grad, filter_grad)


def solution(mesh):
    in_specs = (
        P("ctx", "tp"),
        P("ctx", "tp"),
        P("ctx", "tp"),
        P("ctx", "tp"),
        P("ctx", "tp"),
        P("tp", None),
        P("ctx", "tp"),
    )
    out_specs = (P("ctx", "tp"), P("ctx", "tp"), P("ctx", "tp"), P("ctx", "tp"))
    return jax.shard_map(body, mesh=mesh, in_specs=in_specs, out_specs=out_specs, check_vma=False)
```

```python
import math

import jax
import numpy as np
import jax.numpy as jnp
from jax import lax
from jax.sharding import PartitionSpec as P


BLOCK = 128


def split_bf16(value):
    upper = lax.optimization_barrier(value.astype(jnp.bfloat16))
    lower = (value - upper.astype(jnp.float32)).astype(jnp.bfloat16)
    return upper, lower


def gather_matmul(out_grad, out_weight):
    count = lax.axis_size("tp")
    me = lax.axis_index("tp")
    pieces = [out_grad]
    for shift in range(1, count):
        pieces.append(
            lax.ppermute(out_grad, "tp", [(i, (i + shift) % count) for i in range(count)])
        )
    stacked = jnp.stack(pieces)
    ordered = [
        lax.dynamic_index_in_dim(stacked, (me - source) % count, 0, keepdims=False)
        for source in range(count)
    ]
    gathered = jnp.concatenate(ordered, axis=1)
    return lax.dot_general(
        gathered, out_weight, (((1,), (1,)), ((), ())), preferred_element_type=jnp.float32
    )


def split_constant(table):
    upper = table.astype(jnp.bfloat16)
    lower = (table - upper.astype(np.float64)).astype(jnp.bfloat16)
    return jnp.asarray(upper), jnp.asarray(lower)


def make_tables(size):
    index = np.arange(size)
    long_index = np.arange(2 * size)
    angle = (index[:, None] * index[None, :] % (2 * size)) * (math.pi / size)
    angle_back = (long_index[:, None] * index[None, :] % (2 * size)) * (math.pi / size)
    weight = np.where(index == 0, 1.0, 2.0) / (2.0 * size)
    alternate = 1.0 - 2.0 * (index % 2)
    alternate_back = (1.0 - 2.0 * (long_index % 2)) / (2.0 * size)
    return {
        "cos": split_constant(np.cos(angle)),
        "sin": split_constant(-np.sin(angle)),
        "alt": jnp.asarray(alternate.astype(jnp.bfloat16)),
        "icos": split_constant(np.cos(angle_back) * weight[None, :]),
        "isin": split_constant(-np.sin(angle_back) * weight[None, :]),
        "ialt": jnp.asarray(alternate_back.astype(np.float32)),
    }


def apply(table, signal_hi, signal_lo=None):
    def one(left, right):
        return jnp.einsum("kn,bnc->bkc", left, right, preferred_element_type=jnp.float32)

    out = one(table[0], signal_hi) + one(table[1], signal_hi)
    if signal_lo is not None:
        out = out + one(table[0], signal_lo)
    return out


def forward(tables, signal_hi, signal_lo=None):
    real = apply(tables["cos"], signal_hi, signal_lo)
    imag = apply(tables["sin"], signal_hi, signal_lo)
    nyq = jnp.einsum("n,bnc->bc", tables["alt"], signal_hi, preferred_element_type=jnp.float32)
    if signal_lo is not None:
        nyq = nyq + jnp.einsum(
            "n,bnc->bc", tables["alt"], signal_lo, preferred_element_type=jnp.float32
        )
    return real, imag, nyq


def inverse(tables, spectrum, start, count):
    real_hi, real_lo = split_bf16(spectrum[0])
    imag_hi, imag_lo = split_bf16(spectrum[1])
    icos = tuple(t[start : start + count] for t in tables["icos"])
    isin = tuple(t[start : start + count] for t in tables["isin"])
    ialt = tables["ialt"][start : start + count]
    return (
        apply(icos, real_hi, real_lo)
        + apply(isin, imag_hi, imag_lo)
        + ialt[None, :, None] * spectrum[2][:, None, :]
    )


def conj_times(first, second):
    real = first[0][None] * second[0] + first[1][None] * second[1]
    imag = first[0][None] * second[1] - first[1][None] * second[0]
    return real, imag, first[2][None] * second[2]


def long_correlations(dz_hi, dz_lo, gated, taps, seq_scale):
    seq, chans = gated.shape
    size = min(BLOCK, seq)
    blocks = seq // size
    tables = make_tables(size)
    shape = (blocks, size, chans)
    dz_spec = forward(tables, dz_hi.reshape(shape), dz_lo.reshape(shape))
    gated_spec = forward(tables, gated.reshape(shape))
    taps_spec = forward(tables, taps.reshape(shape))
    parity = (1 - 2 * (jnp.arange(size, dtype=jnp.int32) % 2)).astype(jnp.float32)[None, :, None]
    parity_top = float(1 - 2 * (size % 2))

    def earlier(stack):
        return jnp.concatenate([jnp.zeros_like(stack[:1]), stack[:-1]], axis=0)

    lag_spec = (
        earlier(taps_spec[0]) + parity * taps_spec[0],
        earlier(taps_spec[1]) + parity * taps_spec[1],
        earlier(taps_spec[2]) + parity_top * taps_spec[2],
    )
    padded = tuple(jnp.concatenate([part, jnp.zeros_like(part)], axis=0) for part in dz_spec)
    du_spec = None
    lag_sums = None
    for offset in range(blocks):
        window = tuple(part[offset : offset + blocks] for part in padded)
        du_term = conj_times(tuple(part[offset] for part in lag_spec), window)
        lag_term = conj_times(tuple(part[offset] for part in gated_spec), window)
        if du_spec is None:
            du_spec, lag_sums = du_term, lag_term
        else:
            du_spec = tuple(a + b for a, b in zip(du_spec, du_term))
            lag_sums = tuple(a + b for a, b in zip(lag_sums, lag_term))
    du = inverse(tables, du_spec, size, size).reshape(seq, chans)
    lagged = inverse(tables, lag_sums, 0, 2 * size)
    later_half = jnp.concatenate([lagged[1:, size:], jnp.zeros_like(lagged[:1, size:])], axis=0)
    filter_grad = (lagged[:, :size] + later_half).reshape(seq, chans) * seq_scale
    return du, filter_grad


def to_groups(value, groups):
    rows, chans = value.shape
    return value.reshape(rows, groups, chans // groups).transpose(1, 0, 2)


def from_groups(value):
    groups, rows, chans = value.shape
    return value.transpose(1, 0, 2).reshape(rows, groups * chans)


def all_to_all_ctx(stacked):
    return lax.all_to_all(stacked, "ctx", 0, 0, tiled=True)


def transpose_ctx(stacked):
    count = lax.axis_size("ctx")
    me = lax.axis_index("ctx")
    received = []
    for shift in range(count):
        chunk = lax.dynamic_index_in_dim(stacked, (me + shift) % count, 0, keepdims=False)
        if shift:
            chunk = lax.ppermute(chunk, "ctx", [(i, (i + shift) % count) for i in range(count)])
        received.append(chunk)
    received = jnp.stack(received)
    return jnp.stack(
        [
            lax.dynamic_index_in_dim(received, (me - source) % count, 0, keepdims=False)
            for source in range(count)
        ]
    )


def body(q_proj, k_proj, v_proj, saved_conv, out_grad, out_weight, filter_taps):
    rows, chans = q_proj.shape
    blocks = lax.axis_size("ctx")
    seq = rows * blocks
    gated = (k_proj.astype(jnp.float32) * v_proj.astype(jnp.float32)).astype(jnp.bfloat16)
    inputs_t = all_to_all_ctx(
        jnp.stack([to_groups(gated, blocks), to_groups(filter_taps, blocks)], axis=1)
    )
    d_gated = gather_matmul(out_grad, out_weight)
    dq_grad = (d_gated * saved_conv.astype(jnp.float32)).astype(jnp.bfloat16)
    dz = d_gated * q_proj.astype(jnp.float32)
    dz_hi, dz_lo = split_bf16(dz)
    dz_t = transpose_ctx(jnp.stack([to_groups(dz_hi, blocks), to_groups(dz_lo, blocks)], axis=1))
    sub = chans // blocks
    du_t, filter_t = long_correlations(
        dz_t[:, 0].reshape(seq, sub),
        dz_t[:, 1].reshape(seq, sub),
        inputs_t[:, 0].reshape(seq, sub),
        inputs_t[:, 1].reshape(seq, sub),
        float(seq) ** -0.5,
    )
    back = transpose_ctx(jnp.stack([du_t, filter_t], axis=1).reshape(blocks, rows, 2, sub))
    du_local = from_groups(back[:, :, 0])
    filter_grad = from_groups(back[:, :, 1])
    dk_grad = (du_local * v_proj.astype(jnp.float32)).astype(jnp.bfloat16)
    dv_grad = (du_local * k_proj.astype(jnp.float32)).astype(jnp.bfloat16)
    return (dq_grad, dk_grad, dv_grad, filter_grad)


def solution(mesh):
    in_specs = (
        P("ctx", "tp"),
        P("ctx", "tp"),
        P("ctx", "tp"),
        P("ctx", "tp"),
        P("ctx", "tp"),
        P("tp", None),
        P("ctx", "tp"),
    )
    out_specs = (P("ctx", "tp"), P("ctx", "tp"), P("ctx", "tp"), P("ctx", "tp"))
    return jax.shard_map(body, mesh=mesh, in_specs=in_specs, out_specs=out_specs, check_vma=False)
```

```python
import math

import jax
import numpy as np
import jax.numpy as jnp
from jax import lax
from jax.experimental import pallas as pl
from jax.sharding import PartitionSpec as P


BLOCK = 128


def split_bf16(value):
    upper = lax.optimization_barrier(value.astype(jnp.bfloat16))
    lower = (value - upper.astype(jnp.float32)).astype(jnp.bfloat16)
    return upper, lower


def gather_tp(out_grad):
    count = lax.axis_size("tp")
    me = lax.axis_index("tp")
    pieces = [out_grad]
    for shift in range(1, count):
        pieces.append(
            lax.ppermute(out_grad, "tp", [(i, (i + shift) % count) for i in range(count)])
        )
    stacked = jnp.stack(pieces)
    ordered = [
        lax.dynamic_index_in_dim(stacked, (me - source) % count, 0, keepdims=False)
        for source in range(count)
    ]
    return jnp.concatenate(ordered, axis=1)


def gate_kernel(grad_ref, weight_ref, saved_ref, query_ref, dq_ref, dz_ref):
    product = lax.dot_general(
        grad_ref[...], weight_ref[...], (((1,), (1,)), ((), ())),
        preferred_element_type=jnp.float32,
    )
    dq_ref[...] = (product * saved_ref[...].astype(jnp.float32)).astype(dq_ref.dtype)
    dz_ref[...] = product * query_ref[...].astype(jnp.float32)


def gate_matmul(gathered, out_weight, saved_conv, q_proj):
    rows, width = gathered.shape
    chans = out_weight.shape[0]
    tile = min(chans, 256)
    return pl.pallas_call(
        gate_kernel,
        grid=(chans // tile,),
        in_specs=[
            pl.BlockSpec((rows, width), lambda i: (0, 0)),
            pl.BlockSpec((tile, width), lambda i: (i, 0)),
            pl.BlockSpec((rows, tile), lambda i: (0, i)),
            pl.BlockSpec((rows, tile), lambda i: (0, i)),
        ],
        out_specs=[
            pl.BlockSpec((rows, tile), lambda i: (0, i)),
            pl.BlockSpec((rows, tile), lambda i: (0, i)),
        ],
        out_shape=[
            jax.ShapeDtypeStruct((rows, chans), jnp.bfloat16),
            jax.ShapeDtypeStruct((rows, chans), jnp.float32),
        ],
    )(gathered, out_weight, saved_conv, q_proj)


def split_constant(table):
    upper = table.astype(jnp.bfloat16)
    lower = (table - upper.astype(np.float64)).astype(jnp.bfloat16)
    return jnp.asarray(upper), jnp.asarray(lower)


def make_tables(size):
    index = np.arange(size)
    long_index = np.arange(2 * size)
    angle = (index[:, None] * index[None, :] % (2 * size)) * (math.pi / size)
    angle_back = (long_index[:, None] * index[None, :] % (2 * size)) * (math.pi / size)
    weight = np.where(index == 0, 1.0, 2.0) / (2.0 * size)
    alternate = 1.0 - 2.0 * (index % 2)
    alternate_back = (1.0 - 2.0 * (long_index % 2)) / (2.0 * size)
    return {
        "cos": split_constant(np.cos(angle)),
        "sin": split_constant(-np.sin(angle)),
        "alt": jnp.asarray(alternate.astype(jnp.bfloat16)),
        "icos": split_constant(np.cos(angle_back) * weight[None, :]),
        "isin": split_constant(-np.sin(angle_back) * weight[None, :]),
        "ialt": jnp.asarray(alternate_back.astype(np.float32)),
    }


def apply(table, signal_hi, signal_lo=None):
    def one(left, right):
        return jnp.einsum("kn,bnc->bkc", left, right, preferred_element_type=jnp.float32)

    out = one(table[0], signal_hi) + one(table[1], signal_hi)
    if signal_lo is not None:
        out = out + one(table[0], signal_lo)
    return out


def forward(tables, signal_hi, signal_lo=None):
    real = apply(tables["cos"], signal_hi, signal_lo)
    imag = apply(tables["sin"], signal_hi, signal_lo)
    nyq = jnp.einsum("n,bnc->bc", tables["alt"], signal_hi, preferred_element_type=jnp.float32)
    if signal_lo is not None:
        nyq = nyq + jnp.einsum(
            "n,bnc->bc", tables["alt"], signal_lo, preferred_element_type=jnp.float32
        )
    return real, imag, nyq


def inverse(tables, spectrum, start, count):
    real_hi, real_lo = split_bf16(spectrum[0])
    imag_hi, imag_lo = split_bf16(spectrum[1])
    icos = tuple(t[start : start + count] for t in tables["icos"])
    isin = tuple(t[start : start + count] for t in tables["isin"])
    ialt = tables["ialt"][start : start + count]
    return (
        apply(icos, real_hi, real_lo)
        + apply(isin, imag_hi, imag_lo)
        + ialt[None, :, None] * spectrum[2][:, None, :]
    )


def conj_times(first, second):
    real = first[0][None] * second[0] + first[1][None] * second[1]
    imag = first[0][None] * second[1] - first[1][None] * second[0]
    return real, imag, first[2][None] * second[2]


def long_correlations(dz_hi, dz_lo, gated, taps, seq_scale):
    seq, chans = gated.shape
    size = min(BLOCK, seq)
    blocks = seq // size
    tables = make_tables(size)
    shape = (blocks, size, chans)
    dz_spec = forward(tables, dz_hi.reshape(shape), dz_lo.reshape(shape))
    gated_spec = forward(tables, gated.reshape(shape))
    taps_spec = forward(tables, taps.reshape(shape))
    parity = (1 - 2 * (jnp.arange(size, dtype=jnp.int32) % 2)).astype(jnp.float32)[None, :, None]
    parity_top = float(1 - 2 * (size % 2))

    def earlier(stack):
        return jnp.concatenate([jnp.zeros_like(stack[:1]), stack[:-1]], axis=0)

    lag_spec = (
        earlier(taps_spec[0]) + parity * taps_spec[0],
        earlier(taps_spec[1]) + parity * taps_spec[1],
        earlier(taps_spec[2]) + parity_top * taps_spec[2],
    )
    padded = tuple(jnp.concatenate([part, jnp.zeros_like(part)], axis=0) for part in dz_spec)
    du_spec = None
    lag_sums = None
    for offset in range(blocks):
        window = tuple(part[offset : offset + blocks] for part in padded)
        du_term = conj_times(tuple(part[offset] for part in lag_spec), window)
        lag_term = conj_times(tuple(part[offset] for part in gated_spec), window)
        if du_spec is None:
            du_spec, lag_sums = du_term, lag_term
        else:
            du_spec = tuple(a + b for a, b in zip(du_spec, du_term))
            lag_sums = tuple(a + b for a, b in zip(lag_sums, lag_term))
    du = inverse(tables, du_spec, size, size).reshape(seq, chans)
    lagged = inverse(tables, lag_sums, 0, 2 * size)
    later_half = jnp.concatenate([lagged[1:, size:], jnp.zeros_like(lagged[:1, size:])], axis=0)
    filter_grad = (lagged[:, :size] + later_half).reshape(seq, chans) * seq_scale
    return du, filter_grad


def to_groups(value, groups):
    rows, chans = value.shape
    return value.reshape(rows, groups, chans // groups).transpose(1, 0, 2)


def from_groups(value):
    groups, rows, chans = value.shape
    return value.transpose(1, 0, 2).reshape(rows, groups * chans)


def all_to_all_ctx(stacked):
    return lax.all_to_all(stacked, "ctx", 0, 0, tiled=True)


def transpose_ctx(stacked):
    count = lax.axis_size("ctx")
    me = lax.axis_index("ctx")
    received = []
    for shift in range(count):
        chunk = lax.dynamic_index_in_dim(stacked, (me + shift) % count, 0, keepdims=False)
        if shift:
            chunk = lax.ppermute(chunk, "ctx", [(i, (i + shift) % count) for i in range(count)])
        received.append(chunk)
    received = jnp.stack(received)
    return jnp.stack(
        [
            lax.dynamic_index_in_dim(received, (me - source) % count, 0, keepdims=False)
            for source in range(count)
        ]
    )


def body(q_proj, k_proj, v_proj, saved_conv, out_grad, out_weight, filter_taps):
    rows, chans = q_proj.shape
    blocks = lax.axis_size("ctx")
    seq = rows * blocks
    gated = (k_proj.astype(jnp.float32) * v_proj.astype(jnp.float32)).astype(jnp.bfloat16)
    inputs_t = all_to_all_ctx(
        jnp.stack([to_groups(gated, blocks), to_groups(filter_taps, blocks)], axis=1)
    )
    dq_grad, dz = gate_matmul(gather_tp(out_grad), out_weight, saved_conv, q_proj)
    dz_hi, dz_lo = split_bf16(dz)
    dz_t = transpose_ctx(jnp.stack([to_groups(dz_hi, blocks), to_groups(dz_lo, blocks)], axis=1))
    sub = chans // blocks
    du_t, filter_t = long_correlations(
        dz_t[:, 0].reshape(seq, sub),
        dz_t[:, 1].reshape(seq, sub),
        inputs_t[:, 0].reshape(seq, sub),
        inputs_t[:, 1].reshape(seq, sub),
        float(seq) ** -0.5,
    )
    back = transpose_ctx(jnp.stack([du_t, filter_t], axis=1).reshape(blocks, rows, 2, sub))
    du_local = from_groups(back[:, :, 0])
    filter_grad = from_groups(back[:, :, 1])
    dk_grad = (du_local * v_proj.astype(jnp.float32)).astype(jnp.bfloat16)
    dv_grad = (du_local * k_proj.astype(jnp.float32)).astype(jnp.bfloat16)
    return (dq_grad, dk_grad, dv_grad, filter_grad)


def solution(mesh):
    in_specs = (
        P("ctx", "tp"),
        P("ctx", "tp"),
        P("ctx", "tp"),
        P("ctx", "tp"),
        P("ctx", "tp"),
        P("tp", None),
        P("ctx", "tp"),
    )
    out_specs = (P("ctx", "tp"), P("ctx", "tp"), P("ctx", "tp"), P("ctx", "tp"))
    return jax.shard_map(body, mesh=mesh, in_specs=in_specs, out_specs=out_specs, check_vma=False)
```

```python
import math

import jax
import numpy as np
import jax.numpy as jnp
from jax import lax
from jax.sharding import PartitionSpec as P


BLOCK = 128


def split_bf16(value):
    upper = lax.optimization_barrier(value.astype(jnp.bfloat16))
    lower = (value - upper.astype(jnp.float32)).astype(jnp.bfloat16)
    return upper, lower


def gather_matmul(out_grad, out_weight):
    count = lax.axis_size("tp")
    me = lax.axis_index("tp")
    pieces = [out_grad]
    for shift in range(1, count):
        pieces.append(
            lax.ppermute(out_grad, "tp", [(i, (i + shift) % count) for i in range(count)])
        )
    stacked = jnp.stack(pieces)
    ordered = [
        lax.dynamic_index_in_dim(stacked, (me - source) % count, 0, keepdims=False)
        for source in range(count)
    ]
    gathered = jnp.concatenate(ordered, axis=1)
    return lax.dot_general(
        gathered, out_weight, (((1,), (1,)), ((), ())), preferred_element_type=jnp.float32
    )


def split_constant(table):
    upper = table.astype(jnp.bfloat16)
    lower = (table - upper.astype(np.float64)).astype(jnp.bfloat16)
    return jnp.asarray(upper), jnp.asarray(lower)


def make_tables(size):
    index = np.arange(size)
    long_index = np.arange(2 * size)
    angle = (index[:, None] * index[None, :] % (2 * size)) * (math.pi / size)
    angle_back = (long_index[:, None] * index[None, :] % (2 * size)) * (math.pi / size)
    weight = np.where(index == 0, 1.0, 2.0) / (2.0 * size)
    forward = np.concatenate([np.cos(angle), -np.sin(angle)], axis=0)
    backward = np.concatenate(
        [np.cos(angle_back) * weight[None, :], -np.sin(angle_back) * weight[None, :]], axis=1
    )
    alternate = 1.0 - 2.0 * (index % 2)
    alternate_back = (1.0 - 2.0 * (long_index % 2)) / (2.0 * size)
    return {
        "fwd": split_constant(forward),
        "alt": jnp.asarray(alternate.astype(jnp.bfloat16)),
        "inv": split_constant(backward),
        "ialt": jnp.asarray(alternate_back.astype(np.float32)),
    }


def table_times(table, signal):
    return jnp.einsum("kn,snc->skc", table, signal, preferred_element_type=jnp.float32)


def conj_times(first, second):
    real = first[0][None] * second[0] + first[1][None] * second[1]
    imag = first[0][None] * second[1] - first[1][None] * second[0]
    return real, imag, first[2][None] * second[2]


def long_correlations(dz_hi, dz_lo, gated, taps, seq_scale):
    seq, chans = gated.shape
    size = min(BLOCK, seq)
    blocks = seq // size
    tables = make_tables(size)
    signals = jnp.stack([dz_hi, dz_lo, gated, taps]).reshape(4 * blocks, size, chans)
    upper = table_times(tables["fwd"][0], signals).reshape(4, blocks, 2 * size, chans)
    exact = jnp.stack([dz_hi, gated, taps]).reshape(3 * blocks, size, chans)
    lower = table_times(tables["fwd"][1], exact).reshape(3, blocks, 2 * size, chans)
    top = jnp.einsum("n,snc->sc", tables["alt"], signals, preferred_element_type=jnp.float32)
    top = top.reshape(4, blocks, chans)
    dz_full = upper[0] + upper[1] + lower[0]
    gated_full = upper[2] + lower[1]
    taps_full = upper[3] + lower[2]
    dz_spec = (dz_full[:, :size], dz_full[:, size:], top[0] + top[1])
    gated_spec = (gated_full[:, :size], gated_full[:, size:], top[2])
    taps_spec = (taps_full[:, :size], taps_full[:, size:], top[3])
    parity = (1 - 2 * (jnp.arange(size, dtype=jnp.int32) % 2)).astype(jnp.float32)[None, :, None]
    parity_top = float(1 - 2 * (size % 2))

    def earlier(stack):
        return jnp.concatenate([jnp.zeros_like(stack[:1]), stack[:-1]], axis=0)

    lag_spec = (
        earlier(taps_spec[0]) + parity * taps_spec[0],
        earlier(taps_spec[1]) + parity * taps_spec[1],
        earlier(taps_spec[2]) + parity_top * taps_spec[2],
    )
    padded = tuple(jnp.concatenate([part, jnp.zeros_like(part)], axis=0) for part in dz_spec)
    du_spec = None
    lag_sums = None
    for offset in range(blocks):
        window = tuple(part[offset : offset + blocks] for part in padded)
        du_term = conj_times(tuple(part[offset] for part in lag_spec), window)
        lag_term = conj_times(tuple(part[offset] for part in gated_spec), window)
        if du_spec is None:
            du_spec, lag_sums = du_term, lag_term
        else:
            du_spec = tuple(a + b for a, b in zip(du_spec, du_term))
            lag_sums = tuple(a + b for a, b in zip(lag_sums, lag_term))
    spectra = jnp.stack(
        [
            jnp.concatenate([du_spec[0], du_spec[1]], axis=1),
            jnp.concatenate([lag_sums[0], lag_sums[1]], axis=1),
        ]
    ).reshape(2 * blocks, 2 * size, chans)
    spectra_hi, spectra_lo = split_bf16(spectra)
    inv_hi, inv_lo = tables["inv"]
    signal = (
        table_times(inv_hi, spectra_hi)
        + table_times(inv_hi, spectra_lo)
        + table_times(inv_lo, spectra_hi)
    ).reshape(2, blocks, 2 * size, chans)
    tops = jnp.stack([du_spec[2], lag_sums[2]])
    signal = signal + tables["ialt"][None, None, :, None] * tops[:, :, None, :]
    du = signal[0, :, size:].reshape(seq, chans)
    lagged = signal[1]
    later_half = jnp.concatenate([lagged[1:, size:], jnp.zeros_like(lagged[:1, size:])], axis=0)
    filter_grad = (lagged[:, :size] + later_half).reshape(seq, chans) * seq_scale
    return du, filter_grad


def to_groups(value, groups):
    rows, chans = value.shape
    return value.reshape(rows, groups, chans // groups).transpose(1, 0, 2)


def from_groups(value):
    groups, rows, chans = value.shape
    return value.transpose(1, 0, 2).reshape(rows, groups * chans)


def all_to_all_ctx(stacked):
    return lax.all_to_all(stacked, "ctx", 0, 0, tiled=True)


def transpose_ctx(stacked):
    count = lax.axis_size("ctx")
    me = lax.axis_index("ctx")
    received = []
    for shift in range(count):
        chunk = lax.dynamic_index_in_dim(stacked, (me + shift) % count, 0, keepdims=False)
        if shift:
            chunk = lax.ppermute(chunk, "ctx", [(i, (i + shift) % count) for i in range(count)])
        received.append(chunk)
    received = jnp.stack(received)
    return jnp.stack(
        [
            lax.dynamic_index_in_dim(received, (me - source) % count, 0, keepdims=False)
            for source in range(count)
        ]
    )


def body(q_proj, k_proj, v_proj, saved_conv, out_grad, out_weight, filter_taps):
    rows, chans = q_proj.shape
    blocks = lax.axis_size("ctx")
    seq = rows * blocks
    gated = (k_proj.astype(jnp.float32) * v_proj.astype(jnp.float32)).astype(jnp.bfloat16)
    inputs_t = all_to_all_ctx(
        jnp.stack([to_groups(gated, blocks), to_groups(filter_taps, blocks)], axis=1)
    )
    d_gated = gather_matmul(out_grad, out_weight)
    dq_grad = (d_gated * saved_conv.astype(jnp.float32)).astype(jnp.bfloat16)
    dz = d_gated * q_proj.astype(jnp.float32)
    dz_hi, dz_lo = split_bf16(dz)
    dz_t = transpose_ctx(jnp.stack([to_groups(dz_hi, blocks), to_groups(dz_lo, blocks)], axis=1))
    sub = chans // blocks
    du_t, filter_t = long_correlations(
        dz_t[:, 0].reshape(seq, sub),
        dz_t[:, 1].reshape(seq, sub),
        inputs_t[:, 0].reshape(seq, sub),
        inputs_t[:, 1].reshape(seq, sub),
        float(seq) ** -0.5,
    )
    back = transpose_ctx(jnp.stack([du_t, filter_t], axis=1).reshape(blocks, rows, 2, sub))
    du_local = from_groups(back[:, :, 0])
    filter_grad = from_groups(back[:, :, 1])
    dk_grad = (du_local * v_proj.astype(jnp.float32)).astype(jnp.bfloat16)
    dv_grad = (du_local * k_proj.astype(jnp.float32)).astype(jnp.bfloat16)
    return (dq_grad, dk_grad, dv_grad, filter_grad)


def solution(mesh):
    in_specs = (
        P("ctx", "tp"),
        P("ctx", "tp"),
        P("ctx", "tp"),
        P("ctx", "tp"),
        P("ctx", "tp"),
        P("tp", None),
        P("ctx", "tp"),
    )
    out_specs = (P("ctx", "tp"), P("ctx", "tp"), P("ctx", "tp"), P("ctx", "tp"))
    return jax.shard_map(body, mesh=mesh, in_specs=in_specs, out_specs=out_specs, check_vma=False)
```

```python
import math

import jax
import numpy as np
import jax.numpy as jnp
from jax import lax
from jax.sharding import PartitionSpec as P


BLOCK = 128


def split_bf16(value):
    upper = lax.optimization_barrier(value.astype(jnp.bfloat16))
    lower = (value - upper.astype(jnp.float32)).astype(jnp.bfloat16)
    return upper, lower


def gather_matmul(out_grad, out_weight):
    count = lax.axis_size("tp")
    me = lax.axis_index("tp")
    pieces = [out_grad]
    for shift in range(1, count):
        pieces.append(
            lax.ppermute(out_grad, "tp", [(i, (i + shift) % count) for i in range(count)])
        )
    stacked = jnp.stack(pieces)
    ordered = [
        lax.dynamic_index_in_dim(stacked, (me - source) % count, 0, keepdims=False)
        for source in range(count)
    ]
    gathered = jnp.concatenate(ordered, axis=1)
    return lax.dot_general(
        gathered, out_weight, (((1,), (1,)), ((), ())), preferred_element_type=jnp.float32
    )


def split_constant(table):
    upper = table.astype(jnp.bfloat16)
    lower = (table - upper.astype(np.float64)).astype(jnp.bfloat16)
    return jnp.asarray(upper), jnp.asarray(lower)


def make_tables(size):
    index = np.arange(size)
    long_index = np.arange(2 * size)
    angle = (index[:, None] * index[None, :] % (2 * size)) * (math.pi / size)
    angle_back = (long_index[:, None] * index[None, :] % (2 * size)) * (math.pi / size)
    weight = np.where(index == 0, 1.0, 2.0) / (2.0 * size)
    forward = np.concatenate([np.cos(angle), -np.sin(angle)], axis=0)
    backward = np.concatenate(
        [np.cos(angle_back) * weight[None, :], -np.sin(angle_back) * weight[None, :]], axis=1
    )
    alternate = 1.0 - 2.0 * (index % 2)
    alternate_back = (1.0 - 2.0 * (long_index % 2)) / (2.0 * size)
    return {
        "fwd": split_constant(forward),
        "alt": jnp.asarray(alternate.astype(jnp.bfloat16)),
        "inv": split_constant(backward),
        "ialt": jnp.asarray(alternate_back.astype(np.float32)),
    }


def table_times(table, signal):
    return jnp.einsum("kn,snc->skc", table, signal, preferred_element_type=jnp.float32)


def conj_times(first, second):
    real = first[0][None] * second[0] + first[1][None] * second[1]
    imag = first[0][None] * second[1] - first[1][None] * second[0]
    return real, imag, first[2][None] * second[2]


def long_correlations(dz_hi, dz_lo, gated, taps, seq_scale):
    seq, chans = gated.shape
    size = min(BLOCK, seq)
    blocks = seq // size
    tables = make_tables(size)
    signals = jnp.stack([dz_hi, dz_lo, gated, taps]).reshape(4 * blocks, size, chans)
    upper = table_times(tables["fwd"][0], signals).reshape(4, blocks, 2 * size, chans)
    exact = jnp.stack([dz_hi, gated, taps]).reshape(3 * blocks, size, chans)
    lower = table_times(tables["fwd"][1], exact).reshape(3, blocks, 2 * size, chans)
    top = jnp.einsum("n,snc->sc", tables["alt"], signals, preferred_element_type=jnp.float32)
    top = top.reshape(4, blocks, chans)
    dz_full = upper[0] + upper[1] + lower[0]
    gated_full = upper[2] + lower[1]
    taps_full = upper[3] + lower[2]
    dz_spec = (dz_full[:, :size], dz_full[:, size:], top[0] + top[1])
    gated_spec = (gated_full[:, :size], gated_full[:, size:], top[2])
    taps_spec = (taps_full[:, :size], taps_full[:, size:], top[3])
    parity = (1 - 2 * (jnp.arange(size, dtype=jnp.int32) % 2)).astype(jnp.float32)[None, :, None]
    parity_top = float(1 - 2 * (size % 2))

    def earlier(stack):
        return jnp.concatenate([jnp.zeros_like(stack[:1]), stack[:-1]], axis=0)

    lag_spec = (
        earlier(taps_spec[0]) + parity * taps_spec[0],
        earlier(taps_spec[1]) + parity * taps_spec[1],
        earlier(taps_spec[2]) + parity_top * taps_spec[2],
    )
    padded = tuple(jnp.concatenate([part, jnp.zeros_like(part)], axis=0) for part in dz_spec)
    du_spec = None
    lag_sums = None
    for offset in range(blocks):
        window = tuple(part[offset : offset + blocks] for part in padded)
        du_term = conj_times(tuple(part[offset] for part in lag_spec), window)
        lag_term = conj_times(tuple(part[offset] for part in gated_spec), window)
        if du_spec is None:
            du_spec, lag_sums = du_term, lag_term
        else:
            du_spec = tuple(a + b for a, b in zip(du_spec, du_term))
            lag_sums = tuple(a + b for a, b in zip(lag_sums, lag_term))
    spectra = jnp.stack(
        [
            jnp.concatenate([du_spec[0], du_spec[1]], axis=1),
            jnp.concatenate([lag_sums[0], lag_sums[1]], axis=1),
        ]
    ).reshape(2 * blocks, 2 * size, chans)
    spectra_hi, spectra_lo = split_bf16(spectra)
    inv_hi, inv_lo = tables["inv"]
    signal = (
        table_times(inv_hi, spectra_hi)
        + table_times(inv_hi, spectra_lo)
        + table_times(inv_lo, spectra_hi)
    ).reshape(2, blocks, 2 * size, chans)
    tops = jnp.stack([du_spec[2], lag_sums[2]])
    signal = signal + tables["ialt"][None, None, :, None] * tops[:, :, None, :]
    du = signal[0, :, size:].reshape(seq, chans)
    lagged = signal[1]
    later_half = jnp.concatenate([lagged[1:, size:], jnp.zeros_like(lagged[:1, size:])], axis=0)
    filter_grad = (lagged[:, :size] + later_half).reshape(seq, chans) * seq_scale
    return du, filter_grad


def to_groups(value, groups):
    rows, chans = value.shape
    return value.reshape(rows, groups, chans // groups).transpose(1, 0, 2)


def from_groups(value):
    groups, rows, chans = value.shape
    return value.transpose(1, 0, 2).reshape(rows, groups * chans)


def all_to_all_ctx(stacked):
    return lax.all_to_all(stacked, "ctx", 0, 0, tiled=True)


def transpose_ctx(stacked):
    count = lax.axis_size("ctx")
    me = lax.axis_index("ctx")
    received = []
    for shift in range(count):
        chunk = lax.dynamic_index_in_dim(stacked, (me + shift) % count, 0, keepdims=False)
        if shift:
            chunk = lax.ppermute(chunk, "ctx", [(i, (i + shift) % count) for i in range(count)])
        received.append(chunk)
    received = jnp.stack(received)
    return jnp.stack(
        [
            lax.dynamic_index_in_dim(received, (me - source) % count, 0, keepdims=False)
            for source in range(count)
        ]
    )


def body(q_proj, k_proj, v_proj, saved_conv, out_grad, out_weight, filter_taps):
    rows, chans = q_proj.shape
    blocks = lax.axis_size("ctx")
    seq = rows * blocks
    gated = (k_proj.astype(jnp.float32) * v_proj.astype(jnp.float32)).astype(jnp.bfloat16)
    inputs_t = all_to_all_ctx(
        jnp.stack([to_groups(gated, blocks), to_groups(filter_taps, blocks)], axis=1)
    )
    d_gated = gather_matmul(out_grad, out_weight)
    dq_grad = (d_gated * saved_conv.astype(jnp.float32)).astype(jnp.bfloat16)
    dz = d_gated * q_proj.astype(jnp.float32)
    dz_hi, dz_lo = split_bf16(dz)
    dz_t = transpose_ctx(jnp.stack([to_groups(dz_hi, blocks), to_groups(dz_lo, blocks)], axis=1))
    sub = chans // blocks
    du_t, filter_t = long_correlations(
        dz_t[:, 0].reshape(seq, sub),
        dz_t[:, 1].reshape(seq, sub),
        inputs_t[:, 0].reshape(seq, sub),
        inputs_t[:, 1].reshape(seq, sub),
        float(seq) ** -0.5,
    )
    du_hi, du_lo = split_bf16(du_t)
    outgoing = jnp.stack([du_hi, du_lo, filter_t.astype(jnp.bfloat16)], axis=1)
    back = transpose_ctx(outgoing.reshape(blocks, rows, 3, sub))
    du_local = from_groups(back[:, :, 0].astype(jnp.float32) + back[:, :, 1].astype(jnp.float32))
    filter_grad = from_groups(back[:, :, 2].astype(jnp.float32))
    dk_grad = (du_local * v_proj.astype(jnp.float32)).astype(jnp.bfloat16)
    dv_grad = (du_local * k_proj.astype(jnp.float32)).astype(jnp.bfloat16)
    return (dq_grad, dk_grad, dv_grad, filter_grad)


def solution(mesh):
    in_specs = (
        P("ctx", "tp"),
        P("ctx", "tp"),
        P("ctx", "tp"),
        P("ctx", "tp"),
        P("ctx", "tp"),
        P("tp", None),
        P("ctx", "tp"),
    )
    out_specs = (P("ctx", "tp"), P("ctx", "tp"), P("ctx", "tp"), P("ctx", "tp"))
    return jax.shard_map(body, mesh=mesh, in_specs=in_specs, out_specs=out_specs, check_vma=False)
```

```python
import math

import jax
import numpy as np
import jax.numpy as jnp
from jax import lax
from jax.sharding import PartitionSpec as P


BLOCK = 128


def split_bf16(value):
    upper = lax.optimization_barrier(value.astype(jnp.bfloat16))
    lower = (value - upper.astype(jnp.float32)).astype(jnp.bfloat16)
    return upper, lower


def gather_matmul(out_grad, out_weight):
    count = lax.axis_size("tp")
    me = lax.axis_index("tp")
    pieces = [out_grad]
    for shift in range(1, count):
        pieces.append(
            lax.ppermute(out_grad, "tp", [(i, (i + shift) % count) for i in range(count)])
        )
    stacked = jnp.stack(pieces)
    ordered = [
        lax.dynamic_index_in_dim(stacked, (me - source) % count, 0, keepdims=False)
        for source in range(count)
    ]
    gathered = jnp.concatenate(ordered, axis=1)
    return lax.dot_general(
        gathered, out_weight, (((1,), (1,)), ((), ())), preferred_element_type=jnp.float32
    )


def split_constant(table):
    upper = table.astype(jnp.bfloat16)
    lower = (table - upper.astype(np.float64)).astype(jnp.bfloat16)
    return jnp.asarray(upper), jnp.asarray(lower)


def make_tables(size):
    index = np.arange(size)
    long_index = np.arange(2 * size)
    angle = (index[:, None] * index[None, :] % (2 * size)) * (math.pi / size)
    angle_back = (long_index[:, None] * index[None, :] % (2 * size)) * (math.pi / size)
    weight = np.where(index == 0, 1.0, 2.0) / (2.0 * size)
    forward = np.concatenate([np.cos(angle), -np.sin(angle)], axis=0)
    backward = np.concatenate(
        [np.cos(angle_back) * weight[None, :], -np.sin(angle_back) * weight[None, :]], axis=1
    )
    alternate = 1.0 - 2.0 * (index % 2)
    alternate_back = (1.0 - 2.0 * (long_index % 2)) / (2.0 * size)
    return {
        "fwd": split_constant(forward),
        "alt": jnp.asarray(alternate.astype(jnp.bfloat16)),
        "inv": split_constant(backward),
        "ialt": jnp.asarray(alternate_back.astype(np.float32)),
    }


def table_times(table, signal):
    return jnp.einsum("kn,snc->skc", table, signal, preferred_element_type=jnp.float32)


def conj_times(first, second):
    real = first[0][None] * second[0] + first[1][None] * second[1]
    imag = first[0][None] * second[1] - first[1][None] * second[0]
    return real, imag, first[2][None] * second[2]


def long_correlations(dz_hi, dz_lo, gated, taps, seq_scale):
    seq, chans = gated.shape
    size = min(BLOCK, seq)
    blocks = seq // size
    tables = make_tables(size)
    signals = jnp.stack([dz_hi, dz_lo, gated, taps]).reshape(4 * blocks, size, chans)
    upper = table_times(tables["fwd"][0], signals).reshape(4, blocks, 2 * size, chans)
    exact = jnp.stack([dz_hi, gated, taps]).reshape(3 * blocks, size, chans)
    lower = table_times(tables["fwd"][1], exact).reshape(3, blocks, 2 * size, chans)
    top = jnp.einsum("n,snc->sc", tables["alt"], signals, preferred_element_type=jnp.float32)
    top = top.reshape(4, blocks, chans)
    dz_full = upper[0] + upper[1] + lower[0]
    gated_full = upper[2] + lower[1]
    taps_full = upper[3] + lower[2]
    dz_spec = (dz_full[:, :size], dz_full[:, size:], top[0] + top[1])
    gated_spec = (gated_full[:, :size], gated_full[:, size:], top[2])
    taps_spec = (taps_full[:, :size], taps_full[:, size:], top[3])
    parity = (1 - 2 * (jnp.arange(size, dtype=jnp.int32) % 2)).astype(jnp.float32)[None, :, None]
    parity_top = float(1 - 2 * (size % 2))

    def earlier(stack):
        return jnp.concatenate([jnp.zeros_like(stack[:1]), stack[:-1]], axis=0)

    lag_spec = (
        earlier(taps_spec[0]) + parity * taps_spec[0],
        earlier(taps_spec[1]) + parity * taps_spec[1],
        earlier(taps_spec[2]) + parity_top * taps_spec[2],
    )
    padded = tuple(jnp.concatenate([part, jnp.zeros_like(part)], axis=0) for part in dz_spec)
    du_spec = None
    lag_sums = None
    for offset in range(blocks):
        window = tuple(part[offset : offset + blocks] for part in padded)
        du_term = conj_times(tuple(part[offset] for part in lag_spec), window)
        lag_term = conj_times(tuple(part[offset] for part in gated_spec), window)
        if du_spec is None:
            du_spec, lag_sums = du_term, lag_term
        else:
            du_spec = tuple(a + b for a, b in zip(du_spec, du_term))
            lag_sums = tuple(a + b for a, b in zip(lag_sums, lag_term))
    spectra = jnp.stack(
        [
            jnp.concatenate([du_spec[0], du_spec[1]], axis=1),
            jnp.concatenate([lag_sums[0], lag_sums[1]], axis=1),
        ]
    ).reshape(2 * blocks, 2 * size, chans)
    spectra_hi, spectra_lo = split_bf16(spectra)
    inv_hi, inv_lo = tables["inv"]
    signal = (
        table_times(inv_hi, spectra_hi)
        + table_times(inv_hi, spectra_lo)
        + table_times(inv_lo, spectra_hi)
    ).reshape(2, blocks, 2 * size, chans)
    tops = jnp.stack([du_spec[2], lag_sums[2]])
    signal = signal + tables["ialt"][None, None, :, None] * tops[:, :, None, :]
    du = signal[0, :, size:].reshape(seq, chans)
    lagged = signal[1]
    later_half = jnp.concatenate([lagged[1:, size:], jnp.zeros_like(lagged[:1, size:])], axis=0)
    filter_grad = (lagged[:, :size] + later_half).reshape(seq, chans) * seq_scale
    return du, filter_grad


def to_groups(value, groups):
    rows, chans = value.shape
    return value.reshape(rows, groups, chans // groups).transpose(1, 0, 2)


def from_groups(value):
    groups, rows, chans = value.shape
    return value.transpose(1, 0, 2).reshape(rows, groups * chans)


def all_to_all_ctx(stacked):
    return lax.all_to_all(stacked, "ctx", 0, 0, tiled=True)


def transpose_ctx(stacked):
    count = lax.axis_size("ctx")
    me = lax.axis_index("ctx")
    if count % 2:
        return transpose_ring(stacked, count, me)
    outer = count // 2
    core = me % 2
    chip = me // 2
    paired = stacked.reshape((outer, 2) + stacked.shape[1:])
    mine = lax.dynamic_index_in_dim(paired, core, 1, keepdims=False)
    other = lax.dynamic_index_in_dim(paired, 1 - core, 1, keepdims=False)
    other = lax.ppermute(other, "ctx", [(i, i ^ 1) for i in range(count)])
    held = jnp.stack([mine, other], axis=1)
    received = []
    for shift in range(outer):
        chunk = lax.dynamic_index_in_dim(held, (chip + shift) % outer, 0, keepdims=False)
        if shift:
            chunk = lax.ppermute(
                chunk,
                "ctx",
                [(i, 2 * ((i // 2 + shift) % outer) + i % 2) for i in range(count)],
            )
        received.append(chunk)
    received = jnp.stack(received)
    ordered = jnp.stack(
        [
            lax.dynamic_index_in_dim(received, (chip - source) % outer, 0, keepdims=False)
            for source in range(outer)
        ]
    )
    first = lax.dynamic_index_in_dim(ordered, core, 1, keepdims=False)
    second = lax.dynamic_index_in_dim(ordered, 1 - core, 1, keepdims=False)
    return jnp.stack([first, second], axis=1).reshape(stacked.shape)


def transpose_ring(stacked, count, me):
    received = []
    for shift in range(count):
        chunk = lax.dynamic_index_in_dim(stacked, (me + shift) % count, 0, keepdims=False)
        if shift:
            chunk = lax.ppermute(chunk, "ctx", [(i, (i + shift) % count) for i in range(count)])
        received.append(chunk)
    received = jnp.stack(received)
    return jnp.stack(
        [
            lax.dynamic_index_in_dim(received, (me - source) % count, 0, keepdims=False)
            for source in range(count)
        ]
    )


def body(q_proj, k_proj, v_proj, saved_conv, out_grad, out_weight, filter_taps):
    rows, chans = q_proj.shape
    blocks = lax.axis_size("ctx")
    seq = rows * blocks
    gated = (k_proj.astype(jnp.float32) * v_proj.astype(jnp.float32)).astype(jnp.bfloat16)
    inputs_t = all_to_all_ctx(
        jnp.stack([to_groups(gated, blocks), to_groups(filter_taps, blocks)], axis=1)
    )
    d_gated = gather_matmul(out_grad, out_weight)
    dq_grad = (d_gated * saved_conv.astype(jnp.float32)).astype(jnp.bfloat16)
    dz = d_gated * q_proj.astype(jnp.float32)
    dz_hi, dz_lo = split_bf16(dz)
    dz_t = transpose_ctx(jnp.stack([to_groups(dz_hi, blocks), to_groups(dz_lo, blocks)], axis=1))
    sub = chans // blocks
    du_t, filter_t = long_correlations(
        dz_t[:, 0].reshape(seq, sub),
        dz_t[:, 1].reshape(seq, sub),
        inputs_t[:, 0].reshape(seq, sub),
        inputs_t[:, 1].reshape(seq, sub),
        float(seq) ** -0.5,
    )
    back = transpose_ctx(jnp.stack([du_t, filter_t], axis=1).reshape(blocks, rows, 2, sub))
    du_local = from_groups(back[:, :, 0])
    filter_grad = from_groups(back[:, :, 1])
    dk_grad = (du_local * v_proj.astype(jnp.float32)).astype(jnp.bfloat16)
    dv_grad = (du_local * k_proj.astype(jnp.float32)).astype(jnp.bfloat16)
    return (dq_grad, dk_grad, dv_grad, filter_grad)


def solution(mesh):
    in_specs = (
        P("ctx", "tp"),
        P("ctx", "tp"),
        P("ctx", "tp"),
        P("ctx", "tp"),
        P("ctx", "tp"),
        P("tp", None),
        P("ctx", "tp"),
    )
    out_specs = (P("ctx", "tp"), P("ctx", "tp"), P("ctx", "tp"), P("ctx", "tp"))
    return jax.shard_map(body, mesh=mesh, in_specs=in_specs, out_specs=out_specs, check_vma=False)
```

```python
import math

import jax
import numpy as np
import jax.numpy as jnp
from jax import lax
from jax.sharding import PartitionSpec as P


BLOCK = 128


def split_bf16(value):
    upper = lax.optimization_barrier(value.astype(jnp.bfloat16))
    lower = (value - upper.astype(jnp.float32)).astype(jnp.bfloat16)
    return upper, lower


def gather_matmul(out_grad, out_weight):
    count = lax.axis_size("tp")
    me = lax.axis_index("tp")
    pieces = [out_grad]
    for shift in range(1, count):
        pieces.append(
            lax.ppermute(out_grad, "tp", [(i, (i + shift) % count) for i in range(count)])
        )
    stacked = jnp.stack(pieces)
    ordered = [
        lax.dynamic_index_in_dim(stacked, (me - source) % count, 0, keepdims=False)
        for source in range(count)
    ]
    gathered = jnp.concatenate(ordered, axis=1)
    return lax.dot_general(
        gathered, out_weight, (((1,), (1,)), ((), ())), preferred_element_type=jnp.float32
    )


def split_constant(table):
    upper = table.astype(jnp.bfloat16)
    lower = (table - upper.astype(np.float64)).astype(jnp.bfloat16)
    return jnp.asarray(upper), jnp.asarray(lower)


def make_tables(size):
    index = np.arange(size)
    long_index = np.arange(2 * size)
    angle = (index[:, None] * index[None, :] % (2 * size)) * (math.pi / size)
    angle_back = (long_index[:, None] * index[None, :] % (2 * size)) * (math.pi / size)
    weight = np.where(index == 0, 1.0, 2.0) / (2.0 * size)
    forward = np.concatenate([np.cos(angle), -np.sin(angle)], axis=0)
    backward = np.concatenate(
        [np.cos(angle_back) * weight[None, :], -np.sin(angle_back) * weight[None, :]], axis=1
    )
    alternate = 1.0 - 2.0 * (index % 2)
    alternate_back = (1.0 - 2.0 * (long_index % 2)) / (2.0 * size)
    return {
        "fwd": split_constant(forward),
        "alt": jnp.asarray(alternate.astype(jnp.bfloat16)),
        "inv": split_constant(backward),
        "ialt": jnp.asarray(alternate_back.astype(np.float32)),
    }


def table_times(table, signal):
    return jnp.einsum("kn,snc->skc", table, signal, preferred_element_type=jnp.float32)


def conj_times(first, second):
    real = first[0][None] * second[0] + first[1][None] * second[1]
    imag = first[0][None] * second[1] - first[1][None] * second[0]
    return real, imag, first[2][None] * second[2]


def long_correlations(dz_hi, dz_lo, gated, taps, seq_scale):
    seq, chans = gated.shape
    size = min(BLOCK, seq)
    blocks = seq // size
    tables = make_tables(size)
    signals = jnp.stack([dz_hi, dz_lo, gated, taps]).reshape(4 * blocks, size, chans)
    upper = table_times(tables["fwd"][0], signals).reshape(4, blocks, 2 * size, chans)
    exact = jnp.stack([dz_hi, gated, taps]).reshape(3 * blocks, size, chans)
    lower = table_times(tables["fwd"][1], exact).reshape(3, blocks, 2 * size, chans)
    top = jnp.einsum("n,snc->sc", tables["alt"], signals, preferred_element_type=jnp.float32)
    top = top.reshape(4, blocks, chans)
    dz_full = upper[0] + upper[1] + lower[0]
    gated_full = upper[2] + lower[1]
    taps_full = upper[3] + lower[2]
    dz_spec = (dz_full[:, :size], dz_full[:, size:], top[0] + top[1])
    gated_spec = (gated_full[:, :size], gated_full[:, size:], top[2])
    taps_spec = (taps_full[:, :size], taps_full[:, size:], top[3])
    parity = (1 - 2 * (jnp.arange(size, dtype=jnp.int32) % 2)).astype(jnp.float32)[None, :, None]
    parity_top = float(1 - 2 * (size % 2))

    def earlier(stack):
        return jnp.concatenate([jnp.zeros_like(stack[:1]), stack[:-1]], axis=0)

    lag_spec = (
        earlier(taps_spec[0]) + parity * taps_spec[0],
        earlier(taps_spec[1]) + parity * taps_spec[1],
        earlier(taps_spec[2]) + parity_top * taps_spec[2],
    )
    padded = tuple(jnp.concatenate([part, jnp.zeros_like(part)], axis=0) for part in dz_spec)
    du_spec = None
    lag_sums = None
    for offset in range(blocks):
        window = tuple(part[offset : offset + blocks] for part in padded)
        du_term = conj_times(tuple(part[offset] for part in lag_spec), window)
        lag_term = conj_times(tuple(part[offset] for part in gated_spec), window)
        if du_spec is None:
            du_spec, lag_sums = du_term, lag_term
        else:
            du_spec = tuple(a + b for a, b in zip(du_spec, du_term))
            lag_sums = tuple(a + b for a, b in zip(lag_sums, lag_term))
    spectra = jnp.stack(
        [
            jnp.concatenate([du_spec[0], du_spec[1]], axis=1),
            jnp.concatenate([lag_sums[0], lag_sums[1]], axis=1),
        ]
    ).reshape(2 * blocks, 2 * size, chans)
    spectra_hi, spectra_lo = split_bf16(spectra)
    inv_hi, inv_lo = tables["inv"]
    signal = (
        table_times(inv_hi, spectra_hi)
        + table_times(inv_hi, spectra_lo)
        + table_times(inv_lo, spectra_hi)
    ).reshape(2, blocks, 2 * size, chans)
    tops = jnp.stack([du_spec[2], lag_sums[2]])
    signal = signal + tables["ialt"][None, None, :, None] * tops[:, :, None, :]
    du = signal[0, :, size:].reshape(seq, chans)
    lagged = signal[1]
    later_half = jnp.concatenate([lagged[1:, size:], jnp.zeros_like(lagged[:1, size:])], axis=0)
    filter_grad = (lagged[:, :size] + later_half).reshape(seq, chans) * seq_scale
    return du, filter_grad


def to_groups(value, groups):
    rows, chans = value.shape
    return value.reshape(rows, groups, chans // groups).transpose(1, 0, 2)


def from_groups(value):
    groups, rows, chans = value.shape
    return value.transpose(1, 0, 2).reshape(rows, groups * chans)


def all_to_all_ctx(stacked):
    return lax.all_to_all(stacked, "ctx", 0, 0, tiled=True)


def transpose_ctx(stacked):
    count = lax.axis_size("ctx")
    me = lax.axis_index("ctx")
    received = []
    for shift in range(count):
        chunk = lax.dynamic_index_in_dim(stacked, (me + shift) % count, 0, keepdims=False)
        if shift:
            chunk = lax.ppermute(chunk, "ctx", [(i, (i + shift) % count) for i in range(count)])
        received.append(chunk)
    received = jnp.stack(received)
    return jnp.stack(
        [
            lax.dynamic_index_in_dim(received, (me - source) % count, 0, keepdims=False)
            for source in range(count)
        ]
    )


def scatter_lanes(value, sub):
    count = lax.axis_size("ctx")
    me = lax.axis_index("ctx")
    axis = value.ndim - 1
    received = []
    for shift in range(count):
        chunk = lax.dynamic_slice_in_dim(value, ((me + shift) % count) * sub, sub, axis=axis)
        if shift:
            chunk = lax.ppermute(chunk, "ctx", [(i, (i + shift) % count) for i in range(count)])
        received.append(chunk)
    received = jnp.stack(received)
    return jnp.stack(
        [
            lax.dynamic_index_in_dim(received, (me - source) % count, 0, keepdims=False)
            for source in range(count)
        ]
    )


def gather_lanes(value, chans):
    count = lax.axis_size("ctx")
    me = lax.axis_index("ctx")
    sub = value.shape[-1]
    result = jnp.zeros(value.shape[1:-1] + (chans,), value.dtype)
    for shift in range(count):
        chunk = lax.dynamic_index_in_dim(value, (me + shift) % count, 0, keepdims=False)
        if shift:
            chunk = lax.ppermute(chunk, "ctx", [(i, (i + shift) % count) for i in range(count)])
        result = lax.dynamic_update_slice_in_dim(
            result, chunk, ((me - shift) % count) * sub, axis=result.ndim - 1
        )
    return result


def body(q_proj, k_proj, v_proj, saved_conv, out_grad, out_weight, filter_taps):
    rows, chans = q_proj.shape
    blocks = lax.axis_size("ctx")
    seq = rows * blocks
    sub = chans // blocks
    gated = (k_proj.astype(jnp.float32) * v_proj.astype(jnp.float32)).astype(jnp.bfloat16)
    inputs_t = all_to_all_ctx(
        jnp.stack([to_groups(gated, blocks), to_groups(filter_taps, blocks)], axis=1)
    )
    d_gated = gather_matmul(out_grad, out_weight)
    dq_grad = (d_gated * saved_conv.astype(jnp.float32)).astype(jnp.bfloat16)
    dz = d_gated * q_proj.astype(jnp.float32)
    dz_hi, dz_lo = split_bf16(dz)
    dz_t = scatter_lanes(jnp.stack([dz_hi, dz_lo]), sub)
    du_t, filter_t = long_correlations(
        dz_t[:, 0].reshape(seq, sub),
        dz_t[:, 1].reshape(seq, sub),
        inputs_t[:, 0].reshape(seq, sub),
        inputs_t[:, 1].reshape(seq, sub),
        float(seq) ** -0.5,
    )
    outgoing = jnp.stack([du_t, filter_t]).reshape(2, blocks, rows, sub).transpose(1, 0, 2, 3)
    back = gather_lanes(outgoing, chans)
    du_local = back[0]
    filter_grad = back[1]
    dk_grad = (du_local * v_proj.astype(jnp.float32)).astype(jnp.bfloat16)
    dv_grad = (du_local * k_proj.astype(jnp.float32)).astype(jnp.bfloat16)
    return (dq_grad, dk_grad, dv_grad, filter_grad)


def solution(mesh):
    in_specs = (
        P("ctx", "tp"),
        P("ctx", "tp"),
        P("ctx", "tp"),
        P("ctx", "tp"),
        P("ctx", "tp"),
        P("tp", None),
        P("ctx", "tp"),
    )
    out_specs = (P("ctx", "tp"), P("ctx", "tp"), P("ctx", "tp"), P("ctx", "tp"))
    return jax.shard_map(body, mesh=mesh, in_specs=in_specs, out_specs=out_specs, check_vma=False)
```

```python
import math

import jax
import numpy as np
import jax.numpy as jnp
from jax import lax
from jax.sharding import PartitionSpec as P


BLOCK = 128


def split_bf16(value):
    upper = lax.optimization_barrier(value.astype(jnp.bfloat16))
    lower = (value - upper.astype(jnp.float32)).astype(jnp.bfloat16)
    return upper, lower


def gather_matmul(out_grad, out_weight):
    count = lax.axis_size("tp")
    me = lax.axis_index("tp")
    pieces = [out_grad]
    for shift in range(1, count):
        pieces.append(
            lax.ppermute(out_grad, "tp", [(i, (i + shift) % count) for i in range(count)])
        )
    stacked = jnp.stack(pieces)
    ordered = [
        lax.dynamic_index_in_dim(stacked, (me - source) % count, 0, keepdims=False)
        for source in range(count)
    ]
    gathered = jnp.concatenate(ordered, axis=1)
    return lax.dot_general(
        gathered, out_weight, (((1,), (1,)), ((), ())), preferred_element_type=jnp.float32
    )


def split_constant(table):
    upper = table.astype(jnp.bfloat16)
    lower = (table - upper.astype(np.float64)).astype(jnp.bfloat16)
    return jnp.asarray(upper), jnp.asarray(lower)


def make_tables(size):
    index = np.arange(size)
    long_index = np.arange(2 * size)
    angle = (index[:, None] * index[None, :] % (2 * size)) * (math.pi / size)
    angle_back = (long_index[:, None] * index[None, :] % (2 * size)) * (math.pi / size)
    weight = np.where(index == 0, 1.0, 2.0) / (2.0 * size)
    forward = np.concatenate([np.cos(angle), -np.sin(angle)], axis=0)
    backward = np.concatenate(
        [np.cos(angle_back) * weight[None, :], -np.sin(angle_back) * weight[None, :]], axis=1
    )
    alternate = 1.0 - 2.0 * (index % 2)
    alternate_back = (1.0 - 2.0 * (long_index % 2)) / (2.0 * size)
    return {
        "fwd": split_constant(forward),
        "alt": jnp.asarray(alternate.astype(jnp.bfloat16)),
        "inv": split_constant(backward),
        "ialt": jnp.asarray(alternate_back.astype(np.float32)),
    }


def table_times(table, signal):
    return jnp.einsum("kn,snc->skc", table, signal, preferred_element_type=jnp.float32)


def conj_times(first, second):
    real = first[0][None] * second[0] + first[1][None] * second[1]
    imag = first[0][None] * second[1] - first[1][None] * second[0]
    return real, imag, first[2][None] * second[2]


def long_correlations(dz_hi, dz_lo, gated, taps, seq_scale):
    seq, chans = gated.shape
    size = min(BLOCK, seq)
    blocks = seq // size
    tables = make_tables(size)
    signals = jnp.stack([dz_hi, dz_lo, gated, taps]).reshape(4 * blocks, size, chans)
    upper = table_times(tables["fwd"][0], signals).reshape(4, blocks, 2 * size, chans)
    exact = jnp.stack([dz_hi, gated, taps]).reshape(3 * blocks, size, chans)
    lower = table_times(tables["fwd"][1], exact).reshape(3, blocks, 2 * size, chans)
    top = jnp.einsum("n,snc->sc", tables["alt"], signals, preferred_element_type=jnp.float32)
    top = top.reshape(4, blocks, chans)
    dz_full = upper[0] + upper[1] + lower[0]
    gated_full = upper[2] + lower[1]
    taps_full = upper[3] + lower[2]
    dz_spec = (dz_full[:, :size], dz_full[:, size:], top[0] + top[1])
    gated_spec = (gated_full[:, :size], gated_full[:, size:], top[2])
    taps_spec = (taps_full[:, :size], taps_full[:, size:], top[3])
    parity = (1 - 2 * (jnp.arange(size, dtype=jnp.int32) % 2)).astype(jnp.float32)[None, :, None]
    parity_top = float(1 - 2 * (size % 2))

    def earlier(stack):
        return jnp.concatenate([jnp.zeros_like(stack[:1]), stack[:-1]], axis=0)

    lag_spec = (
        earlier(taps_spec[0]) + parity * taps_spec[0],
        earlier(taps_spec[1]) + parity * taps_spec[1],
        earlier(taps_spec[2]) + parity_top * taps_spec[2],
    )
    padded = tuple(jnp.concatenate([part, jnp.zeros_like(part)], axis=0) for part in dz_spec)
    du_spec = None
    lag_sums = None
    for offset in range(blocks):
        window = tuple(part[offset : offset + blocks] for part in padded)
        du_term = conj_times(tuple(part[offset] for part in lag_spec), window)
        lag_term = conj_times(tuple(part[offset] for part in gated_spec), window)
        if du_spec is None:
            du_spec, lag_sums = du_term, lag_term
        else:
            du_spec = tuple(a + b for a, b in zip(du_spec, du_term))
            lag_sums = tuple(a + b for a, b in zip(lag_sums, lag_term))
    spectra = jnp.stack(
        [
            jnp.concatenate([du_spec[0], du_spec[1]], axis=1),
            jnp.concatenate([lag_sums[0], lag_sums[1]], axis=1),
        ]
    ).reshape(2 * blocks, 2 * size, chans)
    spectra_hi, spectra_lo = split_bf16(spectra)
    inv_hi, inv_lo = tables["inv"]
    signal = (
        table_times(inv_hi, spectra_hi)
        + table_times(inv_hi, spectra_lo)
        + table_times(inv_lo, spectra_hi)
    ).reshape(2, blocks, 2 * size, chans)
    tops = jnp.stack([du_spec[2], lag_sums[2]])
    signal = signal + tables["ialt"][None, None, :, None] * tops[:, :, None, :]
    du = signal[0, :, size:].reshape(seq, chans)
    lagged = signal[1]
    later_half = jnp.concatenate([lagged[1:, size:], jnp.zeros_like(lagged[:1, size:])], axis=0)
    filter_grad = (lagged[:, :size] + later_half).reshape(seq, chans) * seq_scale
    return du, filter_grad


def to_groups(value, groups):
    rows, chans = value.shape
    return value.reshape(rows, groups, chans // groups).transpose(1, 0, 2)


def from_groups(value):
    groups, rows, chans = value.shape
    return value.transpose(1, 0, 2).reshape(rows, groups * chans)


def all_to_all_ctx(stacked):
    return lax.all_to_all(stacked, "ctx", 0, 0, tiled=True)


def transpose_ctx(stacked):
    count = lax.axis_size("ctx")
    me = lax.axis_index("ctx")
    received = []
    for shift in range(count):
        chunk = lax.dynamic_index_in_dim(stacked, (me + shift) % count, 0, keepdims=False)
        if shift:
            chunk = lax.ppermute(chunk, "ctx", [(i, (i + shift) % count) for i in range(count)])
        received.append(chunk)
    received = jnp.stack(received)
    return jnp.stack(
        [
            lax.dynamic_index_in_dim(received, (me - source) % count, 0, keepdims=False)
            for source in range(count)
        ]
    )


def scatter_lanes(value, sub):
    count = lax.axis_size("ctx")
    me = lax.axis_index("ctx")
    axis = value.ndim - 1
    received = []
    for shift in range(count):
        chunk = lax.dynamic_slice_in_dim(value, ((me + shift) % count) * sub, sub, axis=axis)
        if shift:
            chunk = lax.ppermute(chunk, "ctx", [(i, (i + shift) % count) for i in range(count)])
        received.append(chunk)
    received = jnp.stack(received)
    return jnp.stack(
        [
            lax.dynamic_index_in_dim(received, (me - source) % count, 0, keepdims=False)
            for source in range(count)
        ]
    )


def gather_lanes(value, chans):
    count = lax.axis_size("ctx")
    me = lax.axis_index("ctx")
    parts, rows, sub = value.shape[1:]
    results = [jnp.zeros((rows, chans), value.dtype) for _ in range(parts)]
    for shift in range(count):
        chunk = lax.dynamic_index_in_dim(value, (me + shift) % count, 0, keepdims=False)
        if shift:
            chunk = lax.ppermute(chunk, "ctx", [(i, (i + shift) % count) for i in range(count)])
        offset = ((me - shift) % count) * sub
        results = [
            lax.dynamic_update_slice_in_dim(result, chunk[part], offset, axis=1)
            for part, result in enumerate(results)
        ]
    return results


def body(q_proj, k_proj, v_proj, saved_conv, out_grad, out_weight, filter_taps):
    rows, chans = q_proj.shape
    blocks = lax.axis_size("ctx")
    seq = rows * blocks
    sub = chans // blocks
    gated = (k_proj.astype(jnp.float32) * v_proj.astype(jnp.float32)).astype(jnp.bfloat16)
    inputs_t = all_to_all_ctx(
        jnp.stack([to_groups(gated, blocks), to_groups(filter_taps, blocks)], axis=1)
    )
    d_gated = gather_matmul(out_grad, out_weight)
    dq_grad = (d_gated * saved_conv.astype(jnp.float32)).astype(jnp.bfloat16)
    dz = d_gated * q_proj.astype(jnp.float32)
    dz_hi, dz_lo = split_bf16(dz)
    dz_t = scatter_lanes(jnp.stack([dz_hi, dz_lo]), sub)
    du_t, filter_t = long_correlations(
        dz_t[:, 0].reshape(seq, sub),
        dz_t[:, 1].reshape(seq, sub),
        inputs_t[:, 0].reshape(seq, sub),
        inputs_t[:, 1].reshape(seq, sub),
        float(seq) ** -0.5,
    )
    outgoing = jnp.stack([du_t, filter_t]).reshape(2, blocks, rows, sub).transpose(1, 0, 2, 3)
    du_local, filter_grad = gather_lanes(outgoing, chans)
    k_late, v_late = lax.optimization_barrier((k_proj, v_proj))
    dk_grad = (du_local * v_late.astype(jnp.float32)).astype(jnp.bfloat16)
    dv_grad = (du_local * k_late.astype(jnp.float32)).astype(jnp.bfloat16)
    return (dq_grad, dk_grad, dv_grad, filter_grad)


def solution(mesh):
    in_specs = (
        P("ctx", "tp"),
        P("ctx", "tp"),
        P("ctx", "tp"),
        P("ctx", "tp"),
        P("ctx", "tp"),
        P("tp", None),
        P("ctx", "tp"),
    )
    out_specs = (P("ctx", "tp"), P("ctx", "tp"), P("ctx", "tp"), P("ctx", "tp"))
    return jax.shard_map(body, mesh=mesh, in_specs=in_specs, out_specs=out_specs, check_vma=False)
```

```python
import math

import jax
import numpy as np
import jax.numpy as jnp
from jax import lax
from jax.sharding import PartitionSpec as P


BLOCK = 128


def split_bf16(value):
    upper = lax.optimization_barrier(value.astype(jnp.bfloat16))
    lower = (value - upper.astype(jnp.float32)).astype(jnp.bfloat16)
    return upper, lower


def gather_matmul(out_grad, out_weight):
    count = lax.axis_size("tp")
    me = lax.axis_index("tp")
    pieces = [out_grad]
    for shift in range(1, count):
        pieces.append(
            lax.ppermute(out_grad, "tp", [(i, (i + shift) % count) for i in range(count)])
        )
    stacked = jnp.stack(pieces)
    ordered = [
        lax.dynamic_index_in_dim(stacked, (me - source) % count, 0, keepdims=False)
        for source in range(count)
    ]
    gathered = jnp.concatenate(ordered, axis=1)
    return lax.dot_general(
        gathered, out_weight, (((1,), (1,)), ((), ())), preferred_element_type=jnp.float32
    )


def split_constant(table):
    upper = table.astype(jnp.bfloat16)
    lower = (table - upper.astype(np.float64)).astype(jnp.bfloat16)
    return jnp.asarray(upper), jnp.asarray(lower)


def make_tables(size):
    index = np.arange(size)
    long_index = np.arange(2 * size)
    angle = (index[:, None] * index[None, :] % (2 * size)) * (math.pi / size)
    angle_back = (long_index[:, None] * index[None, :] % (2 * size)) * (math.pi / size)
    weight = np.where(index == 0, 1.0, 2.0) / (2.0 * size)
    forward = np.concatenate([np.cos(angle), -np.sin(angle)], axis=0)
    backward = np.concatenate(
        [np.cos(angle_back) * weight[None, :], -np.sin(angle_back) * weight[None, :]], axis=1
    )
    alternate = 1.0 - 2.0 * (index % 2)
    alternate_back = (1.0 - 2.0 * (long_index % 2)) / (2.0 * size)
    return {
        "fwd": split_constant(forward),
        "alt": jnp.asarray(alternate.astype(jnp.bfloat16)),
        "inv": split_constant(backward),
        "ialt": jnp.asarray(alternate_back.astype(np.float32)),
    }


def table_times(table, signal):
    return jnp.einsum("kn,snc->skc", table, signal, preferred_element_type=jnp.float32)


def conj_times(first, second):
    real = first[0][None] * second[0] + first[1][None] * second[1]
    imag = first[0][None] * second[1] - first[1][None] * second[0]
    return real, imag, first[2][None] * second[2]


def long_correlations(dz_hi, dz_lo, gated, taps, seq_scale):
    seq, chans = gated.shape
    size = min(BLOCK, seq)
    blocks = seq // size
    tables = make_tables(size)
    signals = jnp.stack([dz_hi, dz_lo, gated, taps]).reshape(4 * blocks, size, chans)
    upper = table_times(tables["fwd"][0], signals).reshape(4, blocks, 2 * size, chans)
    exact = jnp.stack([dz_hi, gated, taps]).reshape(3 * blocks, size, chans)
    lower = table_times(tables["fwd"][1], exact).reshape(3, blocks, 2 * size, chans)
    top = jnp.einsum("n,snc->sc", tables["alt"], signals, preferred_element_type=jnp.float32)
    top = top.reshape(4, blocks, chans)
    dz_full = upper[0] + upper[1] + lower[0]
    gated_full = upper[2] + lower[1]
    taps_full = upper[3] + lower[2]
    dz_spec = (dz_full[:, :size], dz_full[:, size:], top[0] + top[1])
    gated_spec = (gated_full[:, :size], gated_full[:, size:], top[2])
    taps_spec = (taps_full[:, :size], taps_full[:, size:], top[3])
    parity = (1 - 2 * (jnp.arange(size, dtype=jnp.int32) % 2)).astype(jnp.float32)[None, :, None]
    parity_top = float(1 - 2 * (size % 2))

    def earlier(stack):
        return jnp.concatenate([jnp.zeros_like(stack[:1]), stack[:-1]], axis=0)

    lag_spec = (
        earlier(taps_spec[0]) + parity * taps_spec[0],
        earlier(taps_spec[1]) + parity * taps_spec[1],
        earlier(taps_spec[2]) + parity_top * taps_spec[2],
    )
    padded = tuple(jnp.concatenate([part, jnp.zeros_like(part)], axis=0) for part in dz_spec)
    du_spec = None
    lag_sums = None
    for offset in range(blocks):
        window = tuple(part[offset : offset + blocks] for part in padded)
        du_term = conj_times(tuple(part[offset] for part in lag_spec), window)
        lag_term = conj_times(tuple(part[offset] for part in gated_spec), window)
        if du_spec is None:
            du_spec, lag_sums = du_term, lag_term
        else:
            du_spec = tuple(a + b for a, b in zip(du_spec, du_term))
            lag_sums = tuple(a + b for a, b in zip(lag_sums, lag_term))
    spectra = jnp.stack(
        [
            jnp.concatenate([du_spec[0], du_spec[1]], axis=1),
            jnp.concatenate([lag_sums[0], lag_sums[1]], axis=1),
        ]
    ).reshape(2 * blocks, 2 * size, chans)
    spectra_hi, spectra_lo = split_bf16(spectra)
    inv_hi, inv_lo = tables["inv"]
    signal = (
        table_times(inv_hi, spectra_hi)
        + table_times(inv_hi, spectra_lo)
        + table_times(inv_lo, spectra_hi)
    ).reshape(2, blocks, 2 * size, chans)
    tops = jnp.stack([du_spec[2], lag_sums[2]])
    signal = signal + tables["ialt"][None, None, :, None] * tops[:, :, None, :]
    du = signal[0, :, size:].reshape(seq, chans)
    lagged = signal[1]
    later_half = jnp.concatenate([lagged[1:, size:], jnp.zeros_like(lagged[:1, size:])], axis=0)
    filter_grad = (lagged[:, :size] + later_half).reshape(seq, chans) * seq_scale
    return du, filter_grad


def to_groups(value, groups):
    rows, chans = value.shape
    return value.reshape(rows, groups, chans // groups).transpose(1, 0, 2)


def from_groups(value):
    groups, rows, chans = value.shape
    return value.transpose(1, 0, 2).reshape(rows, groups * chans)


def all_to_all_ctx(stacked):
    return lax.all_to_all(stacked, "ctx", 0, 0, tiled=True)


def transpose_ctx(stacked):
    count = lax.axis_size("ctx")
    me = lax.axis_index("ctx")
    received = []
    for shift in range(count):
        chunk = lax.dynamic_index_in_dim(stacked, (me + shift) % count, 0, keepdims=False)
        if shift:
            chunk = lax.ppermute(chunk, "ctx", [(i, (i + shift) % count) for i in range(count)])
        received.append(chunk)
    received = jnp.stack(received)
    return jnp.stack(
        [
            lax.dynamic_index_in_dim(received, (me - source) % count, 0, keepdims=False)
            for source in range(count)
        ]
    )


def scatter_lanes(value, sub):
    count = lax.axis_size("ctx")
    me = lax.axis_index("ctx")
    axis = value.ndim - 1
    received = []
    for shift in range(count):
        chunk = lax.dynamic_slice_in_dim(value, ((me + shift) % count) * sub, sub, axis=axis)
        if shift:
            chunk = lax.ppermute(chunk, "ctx", [(i, (i + shift) % count) for i in range(count)])
        received.append(chunk)
    received = jnp.stack(received)
    return jnp.stack(
        [
            lax.dynamic_index_in_dim(received, (me - source) % count, 0, keepdims=False)
            for source in range(count)
        ]
    )


def gather_lanes(value, chans):
    count = lax.axis_size("ctx")
    me = lax.axis_index("ctx")
    parts, rows, sub = value.shape[1:]
    results = [jnp.zeros((rows, chans), value.dtype) for _ in range(parts)]
    for shift in range(count):
        chunk = lax.dynamic_index_in_dim(value, (me + shift) % count, 0, keepdims=False)
        if shift:
            chunk = lax.ppermute(chunk, "ctx", [(i, (i + shift) % count) for i in range(count)])
        offset = ((me - shift) % count) * sub
        results = [
            lax.dynamic_update_slice_in_dim(result, chunk[part], offset, axis=1)
            for part, result in enumerate(results)
        ]
    return results


def body(q_proj, k_proj, v_proj, saved_conv, out_grad, out_weight, filter_taps):
    rows, chans = q_proj.shape
    blocks = lax.axis_size("ctx")
    seq = rows * blocks
    sub = chans // blocks
    gated = (k_proj.astype(jnp.float32) * v_proj.astype(jnp.float32)).astype(jnp.bfloat16)
    inputs_t = all_to_all_ctx(
        jnp.stack([to_groups(gated, blocks), to_groups(filter_taps, blocks)], axis=1)
    )
    d_gated = gather_matmul(out_grad, out_weight)
    dq_grad = (d_gated * saved_conv.astype(jnp.float32)).astype(jnp.bfloat16)
    dz = d_gated * q_proj.astype(jnp.float32)
    dz_hi, dz_lo = split_bf16(dz)
    dz_t = scatter_lanes(jnp.stack([dz_hi, dz_lo]), sub)
    du_t, filter_t = long_correlations(
        dz_t[:, 0].reshape(seq, sub),
        dz_t[:, 1].reshape(seq, sub),
        inputs_t[:, 0].reshape(seq, sub),
        inputs_t[:, 1].reshape(seq, sub),
        float(seq) ** -0.5,
    )
    du_hi, du_lo = split_bf16(du_t)
    outgoing = jnp.stack([du_hi, du_lo, filter_t.astype(jnp.bfloat16)])
    outgoing = outgoing.reshape(3, blocks, rows, sub).transpose(1, 0, 2, 3)
    du_hi, du_lo, filter_low = gather_lanes(outgoing, chans)
    du_local = du_hi.astype(jnp.float32) + du_lo.astype(jnp.float32)
    filter_grad = filter_low.astype(jnp.float32)
    k_late, v_late = lax.optimization_barrier((k_proj, v_proj))
    dk_grad = (du_local * v_late.astype(jnp.float32)).astype(jnp.bfloat16)
    dv_grad = (du_local * k_late.astype(jnp.float32)).astype(jnp.bfloat16)
    return (dq_grad, dk_grad, dv_grad, filter_grad)


def solution(mesh):
    in_specs = (
        P("ctx", "tp"),
        P("ctx", "tp"),
        P("ctx", "tp"),
        P("ctx", "tp"),
        P("ctx", "tp"),
        P("tp", None),
        P("ctx", "tp"),
    )
    out_specs = (P("ctx", "tp"), P("ctx", "tp"), P("ctx", "tp"), P("ctx", "tp"))
    return jax.shard_map(body, mesh=mesh, in_specs=in_specs, out_specs=out_specs, check_vma=False)
```

```python
import math

import jax
import numpy as np
import jax.numpy as jnp
from jax import lax
from jax.sharding import PartitionSpec as P


BLOCK = 256


def split_bf16(value):
    upper = lax.optimization_barrier(value.astype(jnp.bfloat16))
    lower = (value - upper.astype(jnp.float32)).astype(jnp.bfloat16)
    return upper, lower


def gather_matmul(out_grad, out_weight):
    count = lax.axis_size("tp")
    me = lax.axis_index("tp")
    pieces = [out_grad]
    for shift in range(1, count):
        pieces.append(
            lax.ppermute(out_grad, "tp", [(i, (i + shift) % count) for i in range(count)])
        )
    stacked = jnp.stack(pieces)
    ordered = [
        lax.dynamic_index_in_dim(stacked, (me - source) % count, 0, keepdims=False)
        for source in range(count)
    ]
    gathered = jnp.concatenate(ordered, axis=1)
    return lax.dot_general(
        gathered, out_weight, (((1,), (1,)), ((), ())), preferred_element_type=jnp.float32
    )


def split_constant(table):
    upper = table.astype(jnp.bfloat16)
    lower = (table - upper.astype(np.float64)).astype(jnp.bfloat16)
    return jnp.asarray(upper), jnp.asarray(lower)


def make_tables(size):
    index = np.arange(size)
    long_index = np.arange(2 * size)
    angle = (index[:, None] * index[None, :] % (2 * size)) * (math.pi / size)
    angle_back = (long_index[:, None] * index[None, :] % (2 * size)) * (math.pi / size)
    weight = np.where(index == 0, 1.0, 2.0) / (2.0 * size)
    forward = np.concatenate([np.cos(angle), -np.sin(angle)], axis=0)
    backward = np.concatenate(
        [np.cos(angle_back) * weight[None, :], -np.sin(angle_back) * weight[None, :]], axis=1
    )
    alternate = 1.0 - 2.0 * (index % 2)
    alternate_back = (1.0 - 2.0 * (long_index % 2)) / (2.0 * size)
    return {
        "fwd": split_constant(forward),
        "alt": jnp.asarray(alternate.astype(jnp.bfloat16)),
        "inv": split_constant(backward),
        "ialt": jnp.asarray(alternate_back.astype(np.float32)),
    }


def table_times(table, signal):
    return jnp.einsum("kn,snc->skc", table, signal, preferred_element_type=jnp.float32)


def conj_times(first, second):
    real = first[0][None] * second[0] + first[1][None] * second[1]
    imag = first[0][None] * second[1] - first[1][None] * second[0]
    return real, imag, first[2][None] * second[2]


def long_correlations(dz_hi, dz_lo, gated, taps, seq_scale):
    seq, chans = gated.shape
    size = min(BLOCK, seq)
    blocks = seq // size
    tables = make_tables(size)
    signals = jnp.stack([dz_hi, dz_lo, gated, taps]).reshape(4 * blocks, size, chans)
    upper = table_times(tables["fwd"][0], signals).reshape(4, blocks, 2 * size, chans)
    exact = jnp.stack([dz_hi, gated, taps]).reshape(3 * blocks, size, chans)
    lower = table_times(tables["fwd"][1], exact).reshape(3, blocks, 2 * size, chans)
    top = jnp.einsum("n,snc->sc", tables["alt"], signals, preferred_element_type=jnp.float32)
    top = top.reshape(4, blocks, chans)
    dz_full = upper[0] + upper[1] + lower[0]
    gated_full = upper[2] + lower[1]
    taps_full = upper[3] + lower[2]
    dz_spec = (dz_full[:, :size], dz_full[:, size:], top[0] + top[1])
    gated_spec = (gated_full[:, :size], gated_full[:, size:], top[2])
    taps_spec = (taps_full[:, :size], taps_full[:, size:], top[3])
    parity = (1 - 2 * (jnp.arange(size, dtype=jnp.int32) % 2)).astype(jnp.float32)[None, :, None]
    parity_top = float(1 - 2 * (size % 2))

    def earlier(stack):
        return jnp.concatenate([jnp.zeros_like(stack[:1]), stack[:-1]], axis=0)

    lag_spec = (
        earlier(taps_spec[0]) + parity * taps_spec[0],
        earlier(taps_spec[1]) + parity * taps_spec[1],
        earlier(taps_spec[2]) + parity_top * taps_spec[2],
    )
    padded = tuple(jnp.concatenate([part, jnp.zeros_like(part)], axis=0) for part in dz_spec)
    du_spec = None
    lag_sums = None
    for offset in range(blocks):
        window = tuple(part[offset : offset + blocks] for part in padded)
        du_term = conj_times(tuple(part[offset] for part in lag_spec), window)
        lag_term = conj_times(tuple(part[offset] for part in gated_spec), window)
        if du_spec is None:
            du_spec, lag_sums = du_term, lag_term
        else:
            du_spec = tuple(a + b for a, b in zip(du_spec, du_term))
            lag_sums = tuple(a + b for a, b in zip(lag_sums, lag_term))
    spectra = jnp.stack(
        [
            jnp.concatenate([du_spec[0], du_spec[1]], axis=1),
            jnp.concatenate([lag_sums[0], lag_sums[1]], axis=1),
        ]
    ).reshape(2 * blocks, 2 * size, chans)
    spectra_hi, spectra_lo = split_bf16(spectra)
    inv_hi, inv_lo = tables["inv"]
    signal = (
        table_times(inv_hi, spectra_hi)
        + table_times(inv_hi, spectra_lo)
        + table_times(inv_lo, spectra_hi)
    ).reshape(2, blocks, 2 * size, chans)
    tops = jnp.stack([du_spec[2], lag_sums[2]])
    signal = signal + tables["ialt"][None, None, :, None] * tops[:, :, None, :]
    du = signal[0, :, size:].reshape(seq, chans)
    lagged = signal[1]
    later_half = jnp.concatenate([lagged[1:, size:], jnp.zeros_like(lagged[:1, size:])], axis=0)
    filter_grad = (lagged[:, :size] + later_half).reshape(seq, chans) * seq_scale
    return du, filter_grad


def to_groups(value, groups):
    rows, chans = value.shape
    return value.reshape(rows, groups, chans // groups).transpose(1, 0, 2)


def from_groups(value):
    groups, rows, chans = value.shape
    return value.transpose(1, 0, 2).reshape(rows, groups * chans)


def all_to_all_ctx(stacked):
    return lax.all_to_all(stacked, "ctx", 0, 0, tiled=True)


def transpose_ctx(stacked):
    count = lax.axis_size("ctx")
    me = lax.axis_index("ctx")
    received = []
    for shift in range(count):
        chunk = lax.dynamic_index_in_dim(stacked, (me + shift) % count, 0, keepdims=False)
        if shift:
            chunk = lax.ppermute(chunk, "ctx", [(i, (i + shift) % count) for i in range(count)])
        received.append(chunk)
    received = jnp.stack(received)
    return jnp.stack(
        [
            lax.dynamic_index_in_dim(received, (me - source) % count, 0, keepdims=False)
            for source in range(count)
        ]
    )


def scatter_lanes(value, sub):
    count = lax.axis_size("ctx")
    me = lax.axis_index("ctx")
    axis = value.ndim - 1
    received = []
    for shift in range(count):
        chunk = lax.dynamic_slice_in_dim(value, ((me + shift) % count) * sub, sub, axis=axis)
        if shift:
            chunk = lax.ppermute(chunk, "ctx", [(i, (i + shift) % count) for i in range(count)])
        received.append(chunk)
    received = jnp.stack(received)
    return jnp.stack(
        [
            lax.dynamic_index_in_dim(received, (me - source) % count, 0, keepdims=False)
            for source in range(count)
        ]
    )


def gather_lanes(value, chans):
    count = lax.axis_size("ctx")
    me = lax.axis_index("ctx")
    parts, rows, sub = value.shape[1:]
    results = [jnp.zeros((rows, chans), value.dtype) for _ in range(parts)]
    for shift in range(count):
        chunk = lax.dynamic_index_in_dim(value, (me + shift) % count, 0, keepdims=False)
        if shift:
            chunk = lax.ppermute(chunk, "ctx", [(i, (i + shift) % count) for i in range(count)])
        offset = ((me - shift) % count) * sub
        results = [
            lax.dynamic_update_slice_in_dim(result, chunk[part], offset, axis=1)
            for part, result in enumerate(results)
        ]
    return results


def body(q_proj, k_proj, v_proj, saved_conv, out_grad, out_weight, filter_taps):
    rows, chans = q_proj.shape
    blocks = lax.axis_size("ctx")
    seq = rows * blocks
    sub = chans // blocks
    gated = (k_proj.astype(jnp.float32) * v_proj.astype(jnp.float32)).astype(jnp.bfloat16)
    inputs_t = all_to_all_ctx(
        jnp.stack([to_groups(gated, blocks), to_groups(filter_taps, blocks)], axis=1)
    )
    d_gated = gather_matmul(out_grad, out_weight)
    dq_grad = (d_gated * saved_conv.astype(jnp.float32)).astype(jnp.bfloat16)
    dz = d_gated * q_proj.astype(jnp.float32)
    dz_hi, dz_lo = split_bf16(dz)
    dz_t = scatter_lanes(jnp.stack([dz_hi, dz_lo]), sub)
    du_t, filter_t = long_correlations(
        dz_t[:, 0].reshape(seq, sub),
        dz_t[:, 1].reshape(seq, sub),
        inputs_t[:, 0].reshape(seq, sub),
        inputs_t[:, 1].reshape(seq, sub),
        float(seq) ** -0.5,
    )
    outgoing = jnp.stack([du_t, filter_t]).reshape(2, blocks, rows, sub).transpose(1, 0, 2, 3)
    du_local, filter_grad = gather_lanes(outgoing, chans)
    k_late, v_late = lax.optimization_barrier((k_proj, v_proj))
    dk_grad = (du_local * v_late.astype(jnp.float32)).astype(jnp.bfloat16)
    dv_grad = (du_local * k_late.astype(jnp.float32)).astype(jnp.bfloat16)
    return (dq_grad, dk_grad, dv_grad, filter_grad)


def solution(mesh):
    in_specs = (
        P("ctx", "tp"),
        P("ctx", "tp"),
        P("ctx", "tp"),
        P("ctx", "tp"),
        P("ctx", "tp"),
        P("tp", None),
        P("ctx", "tp"),
    )
    out_specs = (P("ctx", "tp"), P("ctx", "tp"), P("ctx", "tp"), P("ctx", "tp"))
    return jax.shard_map(body, mesh=mesh, in_specs=in_specs, out_specs=out_specs, check_vma=False)
```

```python
import math

import jax
import numpy as np
import jax.numpy as jnp
from jax import lax
from jax.sharding import PartitionSpec as P


BLOCK = 128


def split_bf16(value):
    upper = lax.optimization_barrier(value.astype(jnp.bfloat16))
    lower = (value - upper.astype(jnp.float32)).astype(jnp.bfloat16)
    return upper, lower


def gather_matmul(out_grad, out_weight):
    count = lax.axis_size("tp")
    me = lax.axis_index("tp")
    pieces = [out_grad]
    for shift in range(1, count):
        pieces.append(
            lax.ppermute(out_grad, "tp", [(i, (i + shift) % count) for i in range(count)])
        )
    stacked = jnp.stack(pieces)
    ordered = [
        lax.dynamic_index_in_dim(stacked, (me - source) % count, 0, keepdims=False)
        for source in range(count)
    ]
    gathered = jnp.concatenate(ordered, axis=1)
    return lax.dot_general(
        gathered, out_weight, (((1,), (1,)), ((), ())), preferred_element_type=jnp.float32
    )


def split_constant(table):
    upper = table.astype(jnp.bfloat16)
    lower = (table - upper.astype(np.float64)).astype(jnp.bfloat16)
    return jnp.asarray(upper), jnp.asarray(lower)


def make_tables(size):
    index = np.arange(size)
    long_index = np.arange(2 * size)
    angle = (index[:, None] * index[None, :] % (2 * size)) * (math.pi / size)
    angle_back = (long_index[:, None] * index[None, :] % (2 * size)) * (math.pi / size)
    weight = np.where(index == 0, 1.0, 2.0) / (2.0 * size)
    forward = np.concatenate([np.cos(angle), -np.sin(angle)], axis=0)
    backward = np.concatenate(
        [np.cos(angle_back) * weight[None, :], -np.sin(angle_back) * weight[None, :]], axis=1
    )
    alternate = 1.0 - 2.0 * (index % 2)
    alternate_back = (1.0 - 2.0 * (long_index % 2)) / (2.0 * size)
    return {
        "fwd": split_constant(forward),
        "alt": jnp.asarray(alternate.astype(jnp.bfloat16)),
        "inv": split_constant(backward),
        "ialt": jnp.asarray(alternate_back.astype(np.float32)),
    }


def table_times(table, signal):
    return jnp.einsum("kn,snc->skc", table, signal, preferred_element_type=jnp.float32)


def conj_times(first, second):
    real = first[0][None] * second[0] + first[1][None] * second[1]
    imag = first[0][None] * second[1] - first[1][None] * second[0]
    return real, imag, first[2][None] * second[2]


def long_correlations(dz_hi, dz_lo, gated, taps, seq_scale):
    seq, chans = gated.shape
    size = min(BLOCK, seq)
    blocks = seq // size
    tables = make_tables(size)
    signals = jnp.stack([dz_hi, dz_lo, gated, taps]).reshape(4 * blocks, size, chans)
    upper = table_times(tables["fwd"][0], signals).reshape(4, blocks, 2 * size, chans)
    exact = jnp.stack([dz_hi, gated, taps]).reshape(3 * blocks, size, chans)
    lower = table_times(tables["fwd"][1], exact).reshape(3, blocks, 2 * size, chans)
    top = jnp.einsum("n,snc->sc", tables["alt"], signals, preferred_element_type=jnp.float32)
    top = top.reshape(4, blocks, chans)
    dz_full = upper[0] + upper[1] + lower[0]
    gated_full = upper[2] + lower[1]
    taps_full = upper[3] + lower[2]
    dz_spec = (dz_full[:, :size], dz_full[:, size:], top[0] + top[1])
    gated_spec = (gated_full[:, :size], gated_full[:, size:], top[2])
    taps_spec = (taps_full[:, :size], taps_full[:, size:], top[3])
    parity = (1 - 2 * (jnp.arange(size, dtype=jnp.int32) % 2)).astype(jnp.float32)[None, :, None]
    parity_top = float(1 - 2 * (size % 2))

    def earlier(stack):
        return jnp.concatenate([jnp.zeros_like(stack[:1]), stack[:-1]], axis=0)

    lag_spec = (
        earlier(taps_spec[0]) + parity * taps_spec[0],
        earlier(taps_spec[1]) + parity * taps_spec[1],
        earlier(taps_spec[2]) + parity_top * taps_spec[2],
    )
    padded = tuple(jnp.concatenate([part, jnp.zeros_like(part)], axis=0) for part in dz_spec)
    du_spec = None
    lag_sums = None
    for offset in range(blocks):
        window = tuple(part[offset : offset + blocks] for part in padded)
        du_term = conj_times(tuple(part[offset] for part in lag_spec), window)
        lag_term = conj_times(tuple(part[offset] for part in gated_spec), window)
        if du_spec is None:
            du_spec, lag_sums = du_term, lag_term
        else:
            du_spec = tuple(a + b for a, b in zip(du_spec, du_term))
            lag_sums = tuple(a + b for a, b in zip(lag_sums, lag_term))
    spectra = jnp.stack(
        [
            jnp.concatenate([du_spec[0], du_spec[1]], axis=1),
            jnp.concatenate([lag_sums[0], lag_sums[1]], axis=1),
        ]
    ).reshape(2 * blocks, 2 * size, chans)
    spectra_hi, spectra_lo = split_bf16(spectra)
    inv_hi, inv_lo = tables["inv"]
    signal = (
        table_times(inv_hi, spectra_hi)
        + table_times(inv_hi, spectra_lo)
        + table_times(inv_lo, spectra_hi)
    ).reshape(2, blocks, 2 * size, chans)
    tops = jnp.stack([du_spec[2], lag_sums[2]])
    signal = signal + tables["ialt"][None, None, :, None] * tops[:, :, None, :]
    du = signal[0, :, size:].reshape(seq, chans)
    lagged = signal[1]
    later_half = jnp.concatenate([lagged[1:, size:], jnp.zeros_like(lagged[:1, size:])], axis=0)
    filter_grad = (lagged[:, :size] + later_half).reshape(seq, chans) * seq_scale
    return du, filter_grad


def to_groups(value, groups):
    rows, chans = value.shape
    return value.reshape(rows, groups, chans // groups).transpose(1, 0, 2)


def from_groups(value):
    groups, rows, chans = value.shape
    return value.transpose(1, 0, 2).reshape(rows, groups * chans)


def all_to_all_ctx(stacked):
    return lax.all_to_all(stacked, "ctx", 0, 0, tiled=True)


def transpose_ctx(stacked):
    count = lax.axis_size("ctx")
    me = lax.axis_index("ctx")
    received = []
    for shift in range(count):
        chunk = lax.dynamic_index_in_dim(stacked, (me + shift) % count, 0, keepdims=False)
        if shift:
            chunk = lax.ppermute(chunk, "ctx", [(i, (i + shift) % count) for i in range(count)])
        received.append(chunk)
    received = jnp.stack(received)
    return jnp.stack(
        [
            lax.dynamic_index_in_dim(received, (me - source) % count, 0, keepdims=False)
            for source in range(count)
        ]
    )


def scatter_lanes(value, sub):
    count = lax.axis_size("ctx")
    me = lax.axis_index("ctx")
    axis = value.ndim - 1
    received = []
    for shift in range(count):
        chunk = lax.dynamic_slice_in_dim(value, ((me + shift) % count) * sub, sub, axis=axis)
        if shift:
            chunk = lax.ppermute(chunk, "ctx", [(i, (i + shift) % count) for i in range(count)])
        received.append(chunk)
    received = jnp.stack(received)
    return jnp.stack(
        [
            lax.dynamic_index_in_dim(received, (me - source) % count, 0, keepdims=False)
            for source in range(count)
        ]
    )


def gather_lanes(value, chans):
    count = lax.axis_size("ctx")
    me = lax.axis_index("ctx")
    parts, rows, sub = value.shape[1:]
    results = [jnp.zeros((rows, chans), value.dtype) for _ in range(parts)]
    for shift in range(count):
        chunk = lax.dynamic_index_in_dim(value, (me + shift) % count, 0, keepdims=False)
        if shift:
            chunk = lax.ppermute(chunk, "ctx", [(i, (i + shift) % count) for i in range(count)])
        offset = ((me - shift) % count) * sub
        results = [
            lax.dynamic_update_slice_in_dim(result, chunk[part], offset, axis=1)
            for part, result in enumerate(results)
        ]
    return results


def body(q_proj, k_proj, v_proj, saved_conv, out_grad, out_weight, filter_taps):
    rows, chans = q_proj.shape
    blocks = lax.axis_size("ctx")
    seq = rows * blocks
    sub = chans // blocks
    gated = (k_proj.astype(jnp.float32) * v_proj.astype(jnp.float32)).astype(jnp.bfloat16)
    inputs_t = all_to_all_ctx(
        jnp.stack([to_groups(gated, blocks), to_groups(filter_taps, blocks)], axis=1)
    )
    d_gated = gather_matmul(out_grad, out_weight)
    dq_grad = (d_gated * saved_conv.astype(jnp.float32)).astype(jnp.bfloat16)
    dz = d_gated * q_proj.astype(jnp.float32)
    dz_hi, dz_lo = split_bf16(dz)
    dz_t = scatter_lanes(jnp.stack([dz_hi, dz_lo]), sub)
    du_t, filter_t = long_correlations(
        dz_t[:, 0].reshape(seq, sub),
        dz_t[:, 1].reshape(seq, sub),
        inputs_t[:, 0].reshape(seq, sub),
        inputs_t[:, 1].reshape(seq, sub),
        float(seq) ** -0.5,
    )
    filter_grad = from_groups(all_to_all_ctx(filter_t.reshape(blocks, rows, sub)))
    (du_local,) = gather_lanes(du_t.reshape(blocks, 1, rows, sub), chans)
    k_late, v_late = lax.optimization_barrier((k_proj, v_proj))
    dk_grad = (du_local * v_late.astype(jnp.float32)).astype(jnp.bfloat16)
    dv_grad = (du_local * k_late.astype(jnp.float32)).astype(jnp.bfloat16)
    return (dq_grad, dk_grad, dv_grad, filter_grad)


def solution(mesh):
    in_specs = (
        P("ctx", "tp"),
        P("ctx", "tp"),
        P("ctx", "tp"),
        P("ctx", "tp"),
        P("ctx", "tp"),
        P("tp", None),
        P("ctx", "tp"),
    )
    out_specs = (P("ctx", "tp"), P("ctx", "tp"), P("ctx", "tp"), P("ctx", "tp"))
    return jax.shard_map(body, mesh=mesh, in_specs=in_specs, out_specs=out_specs, check_vma=False)
```

```python
import math

import jax
import numpy as np
import jax.numpy as jnp
from jax import lax
from jax.sharding import PartitionSpec as P


BLOCK = 128


def split_bf16(value):
    upper = lax.optimization_barrier(value.astype(jnp.bfloat16))
    lower = (value - upper.astype(jnp.float32)).astype(jnp.bfloat16)
    return upper, lower


def gather_matmul(out_grad, out_weight):
    count = lax.axis_size("tp")
    me = lax.axis_index("tp")
    paired = count & (count - 1) == 0
    pieces = [out_grad]
    for step in range(1, count):
        pairs = [(i, i ^ step if paired else (i + step) % count) for i in range(count)]
        pieces.append(lax.ppermute(out_grad, "tp", pairs))
    stacked = jnp.stack(pieces)
    ordered = [
        lax.dynamic_index_in_dim(
            stacked, me ^ source if paired else (me - source) % count, 0, keepdims=False
        )
        for source in range(count)
    ]
    gathered = jnp.concatenate(ordered, axis=1)
    return lax.dot_general(
        gathered, out_weight, (((1,), (1,)), ((), ())), preferred_element_type=jnp.float32
    )


def split_constant(table):
    upper = table.astype(jnp.bfloat16)
    lower = (table - upper.astype(np.float64)).astype(jnp.bfloat16)
    return jnp.asarray(upper), jnp.asarray(lower)


def make_tables(size):
    index = np.arange(size)
    long_index = np.arange(2 * size)
    angle = (index[:, None] * index[None, :] % (2 * size)) * (math.pi / size)
    angle_back = (long_index[:, None] * index[None, :] % (2 * size)) * (math.pi / size)
    weight = np.where(index == 0, 1.0, 2.0) / (2.0 * size)
    forward = np.concatenate([np.cos(angle), -np.sin(angle)], axis=0)
    backward = np.concatenate(
        [np.cos(angle_back) * weight[None, :], -np.sin(angle_back) * weight[None, :]], axis=1
    )
    alternate = 1.0 - 2.0 * (index % 2)
    alternate_back = (1.0 - 2.0 * (long_index % 2)) / (2.0 * size)
    return {
        "fwd": split_constant(forward),
        "alt": jnp.asarray(alternate.astype(jnp.bfloat16)),
        "inv": split_constant(backward),
        "ialt": jnp.asarray(alternate_back.astype(np.float32)),
    }


def table_times(table, signal):
    return jnp.einsum("kn,snc->skc", table, signal, preferred_element_type=jnp.float32)


def conj_times(first, second):
    real = first[0][None] * second[0] + first[1][None] * second[1]
    imag = first[0][None] * second[1] - first[1][None] * second[0]
    return real, imag, first[2][None] * second[2]


def long_correlations(dz_hi, dz_lo, gated, taps, seq_scale):
    seq, chans = gated.shape
    size = min(BLOCK, seq)
    blocks = seq // size
    tables = make_tables(size)
    signals = jnp.stack([dz_hi, dz_lo, gated, taps]).reshape(4 * blocks, size, chans)
    upper = table_times(tables["fwd"][0], signals).reshape(4, blocks, 2 * size, chans)
    exact = jnp.stack([dz_hi, gated, taps]).reshape(3 * blocks, size, chans)
    lower = table_times(tables["fwd"][1], exact).reshape(3, blocks, 2 * size, chans)
    top = jnp.einsum("n,snc->sc", tables["alt"], signals, preferred_element_type=jnp.float32)
    top = top.reshape(4, blocks, chans)
    dz_full = upper[0] + upper[1] + lower[0]
    gated_full = upper[2] + lower[1]
    taps_full = upper[3] + lower[2]
    dz_spec = (dz_full[:, :size], dz_full[:, size:], top[0] + top[1])
    gated_spec = (gated_full[:, :size], gated_full[:, size:], top[2])
    taps_spec = (taps_full[:, :size], taps_full[:, size:], top[3])
    parity = (1 - 2 * (jnp.arange(size, dtype=jnp.int32) % 2)).astype(jnp.float32)[None, :, None]
    parity_top = float(1 - 2 * (size % 2))

    def earlier(stack):
        return jnp.concatenate([jnp.zeros_like(stack[:1]), stack[:-1]], axis=0)

    lag_spec = (
        earlier(taps_spec[0]) + parity * taps_spec[0],
        earlier(taps_spec[1]) + parity * taps_spec[1],
        earlier(taps_spec[2]) + parity_top * taps_spec[2],
    )
    padded = tuple(jnp.concatenate([part, jnp.zeros_like(part)], axis=0) for part in dz_spec)
    du_spec = None
    lag_sums = None
    for offset in range(blocks):
        window = tuple(part[offset : offset + blocks] for part in padded)
        du_term = conj_times(tuple(part[offset] for part in lag_spec), window)
        lag_term = conj_times(tuple(part[offset] for part in gated_spec), window)
        if du_spec is None:
            du_spec, lag_sums = du_term, lag_term
        else:
            du_spec = tuple(a + b for a, b in zip(du_spec, du_term))
            lag_sums = tuple(a + b for a, b in zip(lag_sums, lag_term))
    spectra = jnp.stack(
        [
            jnp.concatenate([du_spec[0], du_spec[1]], axis=1),
            jnp.concatenate([lag_sums[0], lag_sums[1]], axis=1),
        ]
    ).reshape(2 * blocks, 2 * size, chans)
    spectra_hi, spectra_lo = split_bf16(spectra)
    inv_hi, inv_lo = tables["inv"]
    signal = (
        table_times(inv_hi, spectra_hi)
        + table_times(inv_hi, spectra_lo)
        + table_times(inv_lo, spectra_hi)
    ).reshape(2, blocks, 2 * size, chans)
    tops = jnp.stack([du_spec[2], lag_sums[2]])
    signal = signal + tables["ialt"][None, None, :, None] * tops[:, :, None, :]
    du = signal[0, :, size:].reshape(seq, chans)
    lagged = signal[1]
    later_half = jnp.concatenate([lagged[1:, size:], jnp.zeros_like(lagged[:1, size:])], axis=0)
    filter_grad = (lagged[:, :size] + later_half).reshape(seq, chans) * seq_scale
    return du, filter_grad


def to_groups(value, groups):
    rows, chans = value.shape
    return value.reshape(rows, groups, chans // groups).transpose(1, 0, 2)


def from_groups(value):
    groups, rows, chans = value.shape
    return value.transpose(1, 0, 2).reshape(rows, groups * chans)


def all_to_all_ctx(stacked):
    return lax.all_to_all(stacked, "ctx", 0, 0, tiled=True)


def transpose_ctx(stacked):
    count = lax.axis_size("ctx")
    me = lax.axis_index("ctx")
    received = []
    for shift in range(count):
        chunk = lax.dynamic_index_in_dim(stacked, (me + shift) % count, 0, keepdims=False)
        if shift:
            chunk = lax.ppermute(chunk, "ctx", [(i, (i + shift) % count) for i in range(count)])
        received.append(chunk)
    received = jnp.stack(received)
    return jnp.stack(
        [
            lax.dynamic_index_in_dim(received, (me - source) % count, 0, keepdims=False)
            for source in range(count)
        ]
    )


def scatter_lanes(value, sub):
    count = lax.axis_size("ctx")
    me = lax.axis_index("ctx")
    axis = value.ndim - 1
    received = []
    for shift in range(count):
        chunk = lax.dynamic_slice_in_dim(value, ((me + shift) % count) * sub, sub, axis=axis)
        if shift:
            chunk = lax.ppermute(chunk, "ctx", [(i, (i + shift) % count) for i in range(count)])
        received.append(chunk)
    received = jnp.stack(received)
    return jnp.stack(
        [
            lax.dynamic_index_in_dim(received, (me - source) % count, 0, keepdims=False)
            for source in range(count)
        ]
    )


def gather_lanes(value, chans):
    count = lax.axis_size("ctx")
    me = lax.axis_index("ctx")
    parts, rows, sub = value.shape[1:]
    results = [jnp.zeros((rows, chans), value.dtype) for _ in range(parts)]
    for shift in range(count):
        chunk = lax.dynamic_index_in_dim(value, (me + shift) % count, 0, keepdims=False)
        if shift:
            chunk = lax.ppermute(chunk, "ctx", [(i, (i + shift) % count) for i in range(count)])
        offset = ((me - shift) % count) * sub
        results = [
            lax.dynamic_update_slice_in_dim(result, chunk[part], offset, axis=1)
            for part, result in enumerate(results)
        ]
    return results


def body(q_proj, k_proj, v_proj, saved_conv, out_grad, out_weight, filter_taps):
    rows, chans = q_proj.shape
    blocks = lax.axis_size("ctx")
    seq = rows * blocks
    sub = chans // blocks
    gated = (k_proj.astype(jnp.float32) * v_proj.astype(jnp.float32)).astype(jnp.bfloat16)
    inputs_t = all_to_all_ctx(
        jnp.stack([to_groups(gated, blocks), to_groups(filter_taps, blocks)], axis=1)
    )
    d_gated = gather_matmul(out_grad, out_weight)
    dq_grad = (d_gated * saved_conv.astype(jnp.float32)).astype(jnp.bfloat16)
    dz = d_gated * q_proj.astype(jnp.float32)
    dz_hi, dz_lo = split_bf16(dz)
    dz_t = scatter_lanes(jnp.stack([dz_hi, dz_lo]), sub)
    du_t, filter_t = long_correlations(
        dz_t[:, 0].reshape(seq, sub),
        dz_t[:, 1].reshape(seq, sub),
        inputs_t[:, 0].reshape(seq, sub),
        inputs_t[:, 1].reshape(seq, sub),
        float(seq) ** -0.5,
    )
    outgoing = jnp.stack([du_t, filter_t]).reshape(2, blocks, rows, sub).transpose(1, 0, 2, 3)
    du_local, filter_grad = gather_lanes(outgoing, chans)
    k_late, v_late = lax.optimization_barrier((k_proj, v_proj))
    dk_grad = (du_local * v_late.astype(jnp.float32)).astype(jnp.bfloat16)
    dv_grad = (du_local * k_late.astype(jnp.float32)).astype(jnp.bfloat16)
    return (dq_grad, dk_grad, dv_grad, filter_grad)


def solution(mesh):
    in_specs = (
        P("ctx", "tp"),
        P("ctx", "tp"),
        P("ctx", "tp"),
        P("ctx", "tp"),
        P("ctx", "tp"),
        P("tp", None),
        P("ctx", "tp"),
    )
    out_specs = (P("ctx", "tp"), P("ctx", "tp"), P("ctx", "tp"), P("ctx", "tp"))
    return jax.shard_map(body, mesh=mesh, in_specs=in_specs, out_specs=out_specs, check_vma=False)
```

```python
import math

import jax
import numpy as np
import jax.numpy as jnp
from jax import lax
from jax.sharding import PartitionSpec as P


BLOCK = 128


def split_bf16(value):
    upper = lax.optimization_barrier(value.astype(jnp.bfloat16))
    lower = (value - upper.astype(jnp.float32)).astype(jnp.bfloat16)
    return upper, lower


def gather_matmul(out_grad, out_weight):
    count = lax.axis_size("tp")
    me = lax.axis_index("tp")
    paired = count & (count - 1) == 0
    pieces = [out_grad]
    for step in range(1, count):
        pairs = [(i, i ^ step if paired else (i + step) % count) for i in range(count)]
        pieces.append(lax.ppermute(out_grad, "tp", pairs))
    stacked = jnp.stack(pieces)
    ordered = [
        lax.dynamic_index_in_dim(
            stacked, me ^ source if paired else (me - source) % count, 0, keepdims=False
        )
        for source in range(count)
    ]
    gathered = jnp.concatenate(ordered, axis=1)
    halves = 2 if out_weight.shape[0] % 256 == 0 else 1
    width = out_weight.shape[0] // halves
    parts = [
        lax.dot_general(
            gathered,
            out_weight[half * width : (half + 1) * width],
            (((1,), (1,)), ((), ())),
            preferred_element_type=jnp.float32,
        )
        for half in range(halves)
    ]
    return jnp.concatenate(parts, axis=1)


def split_constant(table):
    upper = table.astype(jnp.bfloat16)
    lower = (table - upper.astype(np.float64)).astype(jnp.bfloat16)
    return jnp.asarray(upper), jnp.asarray(lower)


def make_tables(size):
    index = np.arange(size)
    long_index = np.arange(2 * size)
    angle = (index[:, None] * index[None, :] % (2 * size)) * (math.pi / size)
    angle_back = (long_index[:, None] * index[None, :] % (2 * size)) * (math.pi / size)
    weight = np.where(index == 0, 1.0, 2.0) / (2.0 * size)
    forward = np.concatenate([np.cos(angle), -np.sin(angle)], axis=0)
    backward = np.concatenate(
        [np.cos(angle_back) * weight[None, :], -np.sin(angle_back) * weight[None, :]], axis=1
    )
    alternate = 1.0 - 2.0 * (index % 2)
    alternate_back = (1.0 - 2.0 * (long_index % 2)) / (2.0 * size)
    return {
        "fwd": split_constant(forward),
        "alt": jnp.asarray(alternate.astype(jnp.bfloat16)),
        "inv": split_constant(backward),
        "ialt": jnp.asarray(alternate_back.astype(np.float32)),
    }


def table_times(table, signal):
    return jnp.einsum("kn,snc->skc", table, signal, preferred_element_type=jnp.float32)


def conj_times(first, second):
    real = first[0][None] * second[0] + first[1][None] * second[1]
    imag = first[0][None] * second[1] - first[1][None] * second[0]
    return real, imag, first[2][None] * second[2]


def long_correlations(dz_hi, dz_lo, gated, taps, seq_scale):
    seq, chans = gated.shape
    size = min(BLOCK, seq)
    blocks = seq // size
    tables = make_tables(size)
    signals = jnp.stack([dz_hi, dz_lo, gated, taps]).reshape(4 * blocks, size, chans)
    upper = table_times(tables["fwd"][0], signals).reshape(4, blocks, 2 * size, chans)
    exact = jnp.stack([dz_hi, gated, taps]).reshape(3 * blocks, size, chans)
    lower = table_times(tables["fwd"][1], exact).reshape(3, blocks, 2 * size, chans)
    top = jnp.einsum("n,snc->sc", tables["alt"], signals, preferred_element_type=jnp.float32)
    top = top.reshape(4, blocks, chans)
    dz_full = upper[0] + upper[1] + lower[0]
    gated_full = upper[2] + lower[1]
    taps_full = upper[3] + lower[2]
    dz_spec = (dz_full[:, :size], dz_full[:, size:], top[0] + top[1])
    gated_spec = (gated_full[:, :size], gated_full[:, size:], top[2])
    taps_spec = (taps_full[:, :size], taps_full[:, size:], top[3])
    parity = (1 - 2 * (jnp.arange(size, dtype=jnp.int32) % 2)).astype(jnp.float32)[None, :, None]
    parity_top = float(1 - 2 * (size % 2))

    def earlier(stack):
        return jnp.concatenate([jnp.zeros_like(stack[:1]), stack[:-1]], axis=0)

    lag_spec = (
        earlier(taps_spec[0]) + parity * taps_spec[0],
        earlier(taps_spec[1]) + parity * taps_spec[1],
        earlier(taps_spec[2]) + parity_top * taps_spec[2],
    )
    padded = tuple(jnp.concatenate([part, jnp.zeros_like(part)], axis=0) for part in dz_spec)
    du_spec = None
    lag_sums = None
    for offset in range(blocks):
        window = tuple(part[offset : offset + blocks] for part in padded)
        du_term = conj_times(tuple(part[offset] for part in lag_spec), window)
        lag_term = conj_times(tuple(part[offset] for part in gated_spec), window)
        if du_spec is None:
            du_spec, lag_sums = du_term, lag_term
        else:
            du_spec = tuple(a + b for a, b in zip(du_spec, du_term))
            lag_sums = tuple(a + b for a, b in zip(lag_sums, lag_term))
    spectra = jnp.stack(
        [
            jnp.concatenate([du_spec[0], du_spec[1]], axis=1),
            jnp.concatenate([lag_sums[0], lag_sums[1]], axis=1),
        ]
    ).reshape(2 * blocks, 2 * size, chans)
    spectra_hi, spectra_lo = split_bf16(spectra)
    inv_hi, inv_lo = tables["inv"]
    signal = (
        table_times(inv_hi, spectra_hi)
        + table_times(inv_hi, spectra_lo)
        + table_times(inv_lo, spectra_hi)
    ).reshape(2, blocks, 2 * size, chans)
    tops = jnp.stack([du_spec[2], lag_sums[2]])
    signal = signal + tables["ialt"][None, None, :, None] * tops[:, :, None, :]
    du = signal[0, :, size:].reshape(seq, chans)
    lagged = signal[1]
    later_half = jnp.concatenate([lagged[1:, size:], jnp.zeros_like(lagged[:1, size:])], axis=0)
    filter_grad = (lagged[:, :size] + later_half).reshape(seq, chans) * seq_scale
    return du, filter_grad


def to_groups(value, groups):
    rows, chans = value.shape
    return value.reshape(rows, groups, chans // groups).transpose(1, 0, 2)


def from_groups(value):
    groups, rows, chans = value.shape
    return value.transpose(1, 0, 2).reshape(rows, groups * chans)


def all_to_all_ctx(stacked):
    return lax.all_to_all(stacked, "ctx", 0, 0, tiled=True)


def transpose_ctx(stacked):
    count = lax.axis_size("ctx")
    me = lax.axis_index("ctx")
    received = []
    for shift in range(count):
        chunk = lax.dynamic_index_in_dim(stacked, (me + shift) % count, 0, keepdims=False)
        if shift:
            chunk = lax.ppermute(chunk, "ctx", [(i, (i + shift) % count) for i in range(count)])
        received.append(chunk)
    received = jnp.stack(received)
    return jnp.stack(
        [
            lax.dynamic_index_in_dim(received, (me - source) % count, 0, keepdims=False)
            for source in range(count)
        ]
    )


def scatter_lanes(value, sub):
    count = lax.axis_size("ctx")
    me = lax.axis_index("ctx")
    axis = value.ndim - 1
    received = []
    for shift in range(count):
        chunk = lax.dynamic_slice_in_dim(value, ((me + shift) % count) * sub, sub, axis=axis)
        if shift:
            chunk = lax.ppermute(chunk, "ctx", [(i, (i + shift) % count) for i in range(count)])
        received.append(chunk)
    received = jnp.stack(received)
    return jnp.stack(
        [
            lax.dynamic_index_in_dim(received, (me - source) % count, 0, keepdims=False)
            for source in range(count)
        ]
    )


def gather_lanes(value, chans):
    count = lax.axis_size("ctx")
    me = lax.axis_index("ctx")
    parts, rows, sub = value.shape[1:]
    results = [jnp.zeros((rows, chans), value.dtype) for _ in range(parts)]
    for shift in range(count):
        chunk = lax.dynamic_index_in_dim(value, (me + shift) % count, 0, keepdims=False)
        if shift:
            chunk = lax.ppermute(chunk, "ctx", [(i, (i + shift) % count) for i in range(count)])
        offset = ((me - shift) % count) * sub
        results = [
            lax.dynamic_update_slice_in_dim(result, chunk[part], offset, axis=1)
            for part, result in enumerate(results)
        ]
    return results


def body(q_proj, k_proj, v_proj, saved_conv, out_grad, out_weight, filter_taps):
    rows, chans = q_proj.shape
    blocks = lax.axis_size("ctx")
    seq = rows * blocks
    sub = chans // blocks
    gated = (k_proj.astype(jnp.float32) * v_proj.astype(jnp.float32)).astype(jnp.bfloat16)
    inputs_t = all_to_all_ctx(
        jnp.stack([to_groups(gated, blocks), to_groups(filter_taps, blocks)], axis=1)
    )
    d_gated = gather_matmul(out_grad, out_weight)
    dq_grad = (d_gated * saved_conv.astype(jnp.float32)).astype(jnp.bfloat16)
    dz = d_gated * q_proj.astype(jnp.float32)
    dz_hi, dz_lo = split_bf16(dz)
    dz_t = scatter_lanes(jnp.stack([dz_hi, dz_lo]), sub)
    du_t, filter_t = long_correlations(
        dz_t[:, 0].reshape(seq, sub),
        dz_t[:, 1].reshape(seq, sub),
        inputs_t[:, 0].reshape(seq, sub),
        inputs_t[:, 1].reshape(seq, sub),
        float(seq) ** -0.5,
    )
    outgoing = jnp.stack([du_t, filter_t]).reshape(2, blocks, rows, sub).transpose(1, 0, 2, 3)
    du_local, filter_grad = gather_lanes(outgoing, chans)
    k_late, v_late = lax.optimization_barrier((k_proj, v_proj))
    dk_grad = (du_local * v_late.astype(jnp.float32)).astype(jnp.bfloat16)
    dv_grad = (du_local * k_late.astype(jnp.float32)).astype(jnp.bfloat16)
    return (dq_grad, dk_grad, dv_grad, filter_grad)


def solution(mesh):
    in_specs = (
        P("ctx", "tp"),
        P("ctx", "tp"),
        P("ctx", "tp"),
        P("ctx", "tp"),
        P("ctx", "tp"),
        P("tp", None),
        P("ctx", "tp"),
    )
    out_specs = (P("ctx", "tp"), P("ctx", "tp"), P("ctx", "tp"), P("ctx", "tp"))
    return jax.shard_map(body, mesh=mesh, in_specs=in_specs, out_specs=out_specs, check_vma=False)
```

```python
import math

import jax
import numpy as np
import jax.numpy as jnp
from jax import lax
from jax.sharding import PartitionSpec as P


BLOCK = 128


def split_bf16(value):
    upper = lax.optimization_barrier(value.astype(jnp.bfloat16))
    lower = (value - upper.astype(jnp.float32)).astype(jnp.bfloat16)
    return upper, lower


def gather_matmul(out_grad, out_weight):
    count = lax.axis_size("tp")
    me = lax.axis_index("tp")
    paired = count & (count - 1) == 0
    pieces = [out_grad]
    for step in range(1, count):
        pairs = [(i, i ^ step if paired else (i + step) % count) for i in range(count)]
        pieces.append(lax.ppermute(out_grad, "tp", pairs))
    stacked = jnp.stack(pieces)
    ordered = [
        lax.dynamic_index_in_dim(
            stacked, me ^ source if paired else (me - source) % count, 0, keepdims=False
        )
        for source in range(count)
    ]
    gathered = jnp.concatenate(ordered, axis=1)
    return lax.dot_general(
        gathered, out_weight, (((1,), (1,)), ((), ())), preferred_element_type=jnp.float32
    )


def split_constant(table):
    upper = table.astype(jnp.bfloat16)
    lower = (table - upper.astype(np.float64)).astype(jnp.bfloat16)
    return jnp.asarray(upper), jnp.asarray(lower)


def make_tables(size):
    index = np.arange(size)
    long_index = np.arange(2 * size)
    angle = (index[:, None] * index[None, :] % (2 * size)) * (math.pi / size)
    angle_back = (long_index[:, None] * index[None, :] % (2 * size)) * (math.pi / size)
    weight = np.where(index == 0, 1.0, 2.0) / (2.0 * size)
    forward = np.concatenate([np.cos(angle), -np.sin(angle)], axis=0)
    backward = np.concatenate(
        [np.cos(angle_back) * weight[None, :], -np.sin(angle_back) * weight[None, :]], axis=1
    )
    alternate = 1.0 - 2.0 * (index % 2)
    alternate_back = (1.0 - 2.0 * (long_index % 2)) / (2.0 * size)
    return {
        "fwd": split_constant(forward),
        "alt": jnp.asarray(alternate.astype(jnp.bfloat16)),
        "inv": split_constant(backward),
        "ialt": jnp.asarray(alternate_back.astype(np.float32)),
    }


def table_times(table, signal):
    return jnp.einsum("kn,snc->skc", table, signal, preferred_element_type=jnp.float32)


def conj_times(first, second):
    real = first[0][None] * second[0] + first[1][None] * second[1]
    imag = first[0][None] * second[1] - first[1][None] * second[0]
    return real, imag, first[2][None] * second[2]


def long_correlations(dz_hi, dz_lo, gated, taps, seq_scale):
    seq, chans = gated.shape
    size = min(BLOCK, seq)
    blocks = seq // size
    tables = make_tables(size)
    signals = jnp.stack([dz_hi, dz_lo, gated, taps]).reshape(4 * blocks, size, chans)
    upper = table_times(tables["fwd"][0], signals).reshape(4, blocks, 2 * size, chans)
    exact = jnp.stack([dz_hi, gated, taps]).reshape(3 * blocks, size, chans)
    lower = table_times(tables["fwd"][1], exact).reshape(3, blocks, 2 * size, chans)
    top = jnp.einsum("n,snc->sc", tables["alt"], signals, preferred_element_type=jnp.float32)
    top = top.reshape(4, blocks, chans)
    dz_full = upper[0] + upper[1] + lower[0]
    gated_full = upper[2] + lower[1]
    taps_full = upper[3] + lower[2]
    dz_spec = (dz_full[:, :size], dz_full[:, size:], top[0] + top[1])
    gated_spec = (gated_full[:, :size], gated_full[:, size:], top[2])
    taps_spec = (taps_full[:, :size], taps_full[:, size:], top[3])
    parity = (1 - 2 * (jnp.arange(size, dtype=jnp.int32) % 2)).astype(jnp.float32)[None, :, None]
    parity_top = float(1 - 2 * (size % 2))

    def earlier(stack):
        return jnp.concatenate([jnp.zeros_like(stack[:1]), stack[:-1]], axis=0)

    lag_spec = (
        earlier(taps_spec[0]) + parity * taps_spec[0],
        earlier(taps_spec[1]) + parity * taps_spec[1],
        earlier(taps_spec[2]) + parity_top * taps_spec[2],
    )
    padded = tuple(jnp.concatenate([part, jnp.zeros_like(part)], axis=0) for part in dz_spec)
    du_spec = None
    lag_sums = None
    for offset in range(blocks):
        window = tuple(part[offset : offset + blocks] for part in padded)
        du_term = conj_times(tuple(part[offset] for part in lag_spec), window)
        lag_term = conj_times(tuple(part[offset] for part in gated_spec), window)
        if du_spec is None:
            du_spec, lag_sums = du_term, lag_term
        else:
            du_spec = tuple(a + b for a, b in zip(du_spec, du_term))
            lag_sums = tuple(a + b for a, b in zip(lag_sums, lag_term))
    spectra = jnp.stack(
        [
            jnp.concatenate([du_spec[0], du_spec[1]], axis=1),
            jnp.concatenate([lag_sums[0], lag_sums[1]], axis=1),
        ]
    ).reshape(2 * blocks, 2 * size, chans)
    spectra_hi, spectra_lo = split_bf16(spectra)
    inv_hi, inv_lo = tables["inv"]
    signal = (
        table_times(inv_hi, spectra_hi)
        + table_times(inv_hi, spectra_lo)
        + table_times(inv_lo, spectra_hi)
    ).reshape(2, blocks, 2 * size, chans)
    tops = jnp.stack([du_spec[2], lag_sums[2]])
    signal = signal + tables["ialt"][None, None, :, None] * tops[:, :, None, :]
    du = signal[0, :, size:].reshape(seq, chans)
    lagged = signal[1]
    later_half = jnp.concatenate([lagged[1:, size:], jnp.zeros_like(lagged[:1, size:])], axis=0)
    filter_grad = (lagged[:, :size] + later_half).reshape(seq, chans) * seq_scale
    return du, filter_grad


def to_groups(value, groups):
    rows, chans = value.shape
    return value.reshape(rows, groups, chans // groups).transpose(1, 0, 2)


def from_groups(value):
    groups, rows, chans = value.shape
    return value.transpose(1, 0, 2).reshape(rows, groups * chans)


def all_to_all_ctx(stacked):
    return lax.all_to_all(stacked, "ctx", 0, 0, tiled=True)


def transpose_ctx(stacked):
    count = lax.axis_size("ctx")
    me = lax.axis_index("ctx")
    received = []
    for shift in range(count):
        chunk = lax.dynamic_index_in_dim(stacked, (me + shift) % count, 0, keepdims=False)
        if shift:
            chunk = lax.ppermute(chunk, "ctx", [(i, (i + shift) % count) for i in range(count)])
        received.append(chunk)
    received = jnp.stack(received)
    return jnp.stack(
        [
            lax.dynamic_index_in_dim(received, (me - source) % count, 0, keepdims=False)
            for source in range(count)
        ]
    )


def scatter_lanes(value, sub):
    count = lax.axis_size("ctx")
    me = lax.axis_index("ctx")
    axis = value.ndim - 1
    received = []
    for shift in range(count):
        chunk = lax.dynamic_slice_in_dim(value, ((me + shift) % count) * sub, sub, axis=axis)
        if shift:
            chunk = lax.ppermute(chunk, "ctx", [(i, (i + shift) % count) for i in range(count)])
        received.append(chunk)
    received = jnp.stack(received)
    return jnp.stack(
        [
            lax.dynamic_index_in_dim(received, (me - source) % count, 0, keepdims=False)
            for source in range(count)
        ]
    )


def gather_lanes(value, chans, parts):
    count = lax.axis_size("ctx")
    me = lax.axis_index("ctx")
    rows, width = value.shape[1:]
    sub = width // parts
    results = [jnp.zeros((rows, chans), value.dtype) for _ in range(parts)]
    for shift in range(count):
        chunk = lax.dynamic_index_in_dim(value, (me + shift) % count, 0, keepdims=False)
        if shift:
            chunk = lax.ppermute(chunk, "ctx", [(i, (i + shift) % count) for i in range(count)])
        offset = ((me - shift) % count) * sub
        results = [
            lax.dynamic_update_slice_in_dim(
                result, chunk[:, part * sub : (part + 1) * sub], offset, axis=1
            )
            for part, result in enumerate(results)
        ]
    return results


def body(q_proj, k_proj, v_proj, saved_conv, out_grad, out_weight, filter_taps):
    rows, chans = q_proj.shape
    blocks = lax.axis_size("ctx")
    seq = rows * blocks
    sub = chans // blocks
    gated = (k_proj.astype(jnp.float32) * v_proj.astype(jnp.float32)).astype(jnp.bfloat16)
    inputs_t = all_to_all_ctx(
        jnp.stack([to_groups(gated, blocks), to_groups(filter_taps, blocks)], axis=1)
    )
    d_gated = gather_matmul(out_grad, out_weight)
    dq_grad = (d_gated * saved_conv.astype(jnp.float32)).astype(jnp.bfloat16)
    dz = d_gated * q_proj.astype(jnp.float32)
    dz_hi, dz_lo = split_bf16(dz)
    dz_t = scatter_lanes(jnp.stack([dz_hi, dz_lo]), sub)
    du_t, filter_t = long_correlations(
        dz_t[:, 0].reshape(seq, sub),
        dz_t[:, 1].reshape(seq, sub),
        inputs_t[:, 0].reshape(seq, sub),
        inputs_t[:, 1].reshape(seq, sub),
        float(seq) ** -0.5,
    )
    outgoing = jnp.concatenate(
        [du_t.reshape(blocks, rows, sub), filter_t.reshape(blocks, rows, sub)], axis=2
    )
    du_local, filter_grad = gather_lanes(outgoing, chans, 2)
    k_late, v_late = lax.optimization_barrier((k_proj, v_proj))
    dk_grad = (du_local * v_late.astype(jnp.float32)).astype(jnp.bfloat16)
    dv_grad = (du_local * k_late.astype(jnp.float32)).astype(jnp.bfloat16)
    return (dq_grad, dk_grad, dv_grad, filter_grad)


def solution(mesh):
    in_specs = (
        P("ctx", "tp"),
        P("ctx", "tp"),
        P("ctx", "tp"),
        P("ctx", "tp"),
        P("ctx", "tp"),
        P("tp", None),
        P("ctx", "tp"),
    )
    out_specs = (P("ctx", "tp"), P("ctx", "tp"), P("ctx", "tp"), P("ctx", "tp"))
    return jax.shard_map(body, mesh=mesh, in_specs=in_specs, out_specs=out_specs, check_vma=False)
```

```python
import math

import jax
import numpy as np
import jax.numpy as jnp
from jax import lax
from jax.sharding import PartitionSpec as P


BLOCK = 128


def split_bf16(value):
    upper = lax.optimization_barrier(value.astype(jnp.bfloat16))
    lower = (value - upper.astype(jnp.float32)).astype(jnp.bfloat16)
    return upper, lower


def gather_matmul(out_grad, out_weight):
    count = lax.axis_size("tp")
    me = lax.axis_index("tp")
    paired = count & (count - 1) == 0
    pieces = [out_grad]
    for step in range(1, count):
        pairs = [(i, i ^ step if paired else (i + step) % count) for i in range(count)]
        pieces.append(lax.ppermute(out_grad, "tp", pairs))
    stacked = jnp.stack(pieces)
    ordered = [
        lax.dynamic_index_in_dim(
            stacked, me ^ source if paired else (me - source) % count, 0, keepdims=False
        )
        for source in range(count)
    ]
    gathered = jnp.concatenate(ordered, axis=1)
    return lax.dot_general(
        gathered, out_weight, (((1,), (1,)), ((), ())), preferred_element_type=jnp.float32
    )


def split_constant(table):
    upper = table.astype(jnp.bfloat16)
    lower = (table - upper.astype(np.float64)).astype(jnp.bfloat16)
    return jnp.asarray(upper), jnp.asarray(lower)


def make_tables(size):
    index = np.arange(size)
    long_index = np.arange(2 * size)
    angle = (index[:, None] * index[None, :] % (2 * size)) * (math.pi / size)
    angle_back = (long_index[:, None] * index[None, :] % (2 * size)) * (math.pi / size)
    weight = np.where(index == 0, 1.0, 2.0) / (2.0 * size)
    forward = np.concatenate([np.cos(angle), -np.sin(angle)], axis=0)
    backward = np.concatenate(
        [np.cos(angle_back) * weight[None, :], -np.sin(angle_back) * weight[None, :]], axis=1
    )
    alternate = 1.0 - 2.0 * (index % 2)
    alternate_back = (1.0 - 2.0 * (long_index % 2)) / (2.0 * size)
    return {
        "fwd": split_constant(forward),
        "alt": jnp.asarray(alternate.astype(jnp.bfloat16)),
        "inv": split_constant(backward),
        "ialt": jnp.asarray(alternate_back.astype(np.float32)),
    }


def table_times(table, signal):
    return jnp.einsum("kn,snc->skc", table, signal, preferred_element_type=jnp.float32)


def conj_times(first, second):
    real = first[0][None] * second[0] + first[1][None] * second[1]
    imag = first[0][None] * second[1] - first[1][None] * second[0]
    return real, imag, first[2][None] * second[2]


def long_correlations(dz_hi, dz_lo, gated, taps, seq_scale):
    seq, chans = gated.shape
    size = min(BLOCK, seq)
    blocks = seq // size
    tables = make_tables(size)
    signals = jnp.stack([dz_hi, dz_lo, gated, taps]).reshape(4 * blocks, size, chans)
    upper = table_times(tables["fwd"][0], signals).reshape(4, blocks, 2 * size, chans)
    exact = jnp.stack([dz_hi, gated, taps]).reshape(3 * blocks, size, chans)
    lower = table_times(tables["fwd"][1], exact).reshape(3, blocks, 2 * size, chans)
    top = jnp.einsum("n,snc->sc", tables["alt"], signals, preferred_element_type=jnp.float32)
    top = top.reshape(4, blocks, chans)
    dz_full = upper[0] + upper[1] + lower[0]
    gated_full = upper[2] + lower[1]
    taps_full = upper[3] + lower[2]
    dz_spec = (dz_full[:, :size], dz_full[:, size:], top[0] + top[1])
    gated_spec = (gated_full[:, :size], gated_full[:, size:], top[2])
    taps_spec = (taps_full[:, :size], taps_full[:, size:], top[3])
    parity = (1 - 2 * (jnp.arange(size, dtype=jnp.int32) % 2)).astype(jnp.float32)[None, :, None]
    parity_top = float(1 - 2 * (size % 2))

    def earlier(stack):
        return jnp.concatenate([jnp.zeros_like(stack[:1]), stack[:-1]], axis=0)

    lag_spec = (
        earlier(taps_spec[0]) + parity * taps_spec[0],
        earlier(taps_spec[1]) + parity * taps_spec[1],
        earlier(taps_spec[2]) + parity_top * taps_spec[2],
    )
    padded = tuple(jnp.concatenate([part, jnp.zeros_like(part)], axis=0) for part in dz_spec)
    du_spec = None
    lag_sums = None
    for offset in range(blocks):
        window = tuple(part[offset : offset + blocks] for part in padded)
        du_term = conj_times(tuple(part[offset] for part in lag_spec), window)
        lag_term = conj_times(tuple(part[offset] for part in gated_spec), window)
        if du_spec is None:
            du_spec, lag_sums = du_term, lag_term
        else:
            du_spec = tuple(a + b for a, b in zip(du_spec, du_term))
            lag_sums = tuple(a + b for a, b in zip(lag_sums, lag_term))
    spectra = jnp.stack(
        [
            jnp.concatenate([du_spec[0], du_spec[1]], axis=1),
            jnp.concatenate([lag_sums[0], lag_sums[1]], axis=1),
        ]
    ).reshape(2 * blocks, 2 * size, chans)
    spectra_hi, spectra_lo = split_bf16(spectra)
    inv_hi, inv_lo = tables["inv"]
    signal = (
        table_times(inv_hi, spectra_hi)
        + table_times(inv_hi, spectra_lo)
        + table_times(inv_lo, spectra_hi)
    ).reshape(2, blocks, 2 * size, chans)
    tops = jnp.stack([du_spec[2], lag_sums[2]])
    signal = signal + tables["ialt"][None, None, :, None] * tops[:, :, None, :]
    du = signal[0, :, size:].reshape(seq, chans)
    lagged = signal[1]
    later_half = jnp.concatenate([lagged[1:, size:], jnp.zeros_like(lagged[:1, size:])], axis=0)
    filter_grad = (lagged[:, :size] + later_half).reshape(seq, chans) * seq_scale
    return du, filter_grad


def to_groups(value, groups):
    rows, chans = value.shape
    return value.reshape(rows, groups, chans // groups).transpose(1, 0, 2)


def from_groups(value):
    groups, rows, chans = value.shape
    return value.transpose(1, 0, 2).reshape(rows, groups * chans)


def all_to_all_ctx(stacked):
    return lax.all_to_all(stacked, "ctx", 0, 0, tiled=True)


def transpose_ctx(stacked):
    count = lax.axis_size("ctx")
    me = lax.axis_index("ctx")
    received = []
    for shift in range(count):
        chunk = lax.dynamic_index_in_dim(stacked, (me + shift) % count, 0, keepdims=False)
        if shift:
            chunk = lax.ppermute(chunk, "ctx", [(i, (i + shift) % count) for i in range(count)])
        received.append(chunk)
    received = jnp.stack(received)
    return jnp.stack(
        [
            lax.dynamic_index_in_dim(received, (me - source) % count, 0, keepdims=False)
            for source in range(count)
        ]
    )


def scatter_lanes(value, sub):
    count = lax.axis_size("ctx")
    me = lax.axis_index("ctx")
    axis = value.ndim - 1
    received = []
    for shift in range(count):
        chunk = lax.dynamic_slice_in_dim(value, ((me + shift) % count) * sub, sub, axis=axis)
        if shift:
            chunk = lax.ppermute(chunk, "ctx", [(i, (i + shift) % count) for i in range(count)])
        received.append(chunk)
    received = jnp.stack(received)
    return jnp.stack(
        [
            lax.dynamic_index_in_dim(received, (me - source) % count, 0, keepdims=False)
            for source in range(count)
        ]
    )


def gather_lanes(value, chans):
    count = lax.axis_size("ctx")
    me = lax.axis_index("ctx")
    parts, rows, sub = value.shape[1:]
    results = [jnp.zeros((rows, chans), value.dtype) for _ in range(parts)]
    for shift in range(count):
        chunk = lax.dynamic_index_in_dim(value, (me + shift) % count, 0, keepdims=False)
        if shift:
            chunk = lax.ppermute(chunk, "ctx", [(i, (i + shift) % count) for i in range(count)])
        offset = ((me - shift) % count) * sub
        results = [
            lax.dynamic_update_slice_in_dim(result, chunk[part], offset, axis=1)
            for part, result in enumerate(results)
        ]
    return results


def body(q_proj, k_proj, v_proj, saved_conv, out_grad, out_weight, filter_taps):
    rows, chans = q_proj.shape
    blocks = lax.axis_size("ctx")
    seq = rows * blocks
    sub = chans // blocks
    gated = (k_proj.astype(jnp.float32) * v_proj.astype(jnp.float32)).astype(jnp.bfloat16)
    inputs_t = all_to_all_ctx(
        jnp.stack([to_groups(gated, blocks), to_groups(filter_taps, blocks)], axis=1)
    )
    d_gated = gather_matmul(out_grad, out_weight)
    dq_grad = (d_gated * saved_conv.astype(jnp.float32)).astype(jnp.bfloat16)
    dz = d_gated * q_proj.astype(jnp.float32)
    dz_t = scatter_lanes(dz, sub)
    dz_hi, dz_lo = split_bf16(dz_t.reshape(seq, sub))
    du_t, filter_t = long_correlations(
        dz_hi,
        dz_lo,
        inputs_t[:, 0].reshape(seq, sub),
        inputs_t[:, 1].reshape(seq, sub),
        float(seq) ** -0.5,
    )
    outgoing = jnp.stack([du_t, filter_t]).reshape(2, blocks, rows, sub).transpose(1, 0, 2, 3)
    du_local, filter_grad = gather_lanes(outgoing, chans)
    k_late, v_late = lax.optimization_barrier((k_proj, v_proj))
    dk_grad = (du_local * v_late.astype(jnp.float32)).astype(jnp.bfloat16)
    dv_grad = (du_local * k_late.astype(jnp.float32)).astype(jnp.bfloat16)
    return (dq_grad, dk_grad, dv_grad, filter_grad)


def solution(mesh):
    in_specs = (
        P("ctx", "tp"),
        P("ctx", "tp"),
        P("ctx", "tp"),
        P("ctx", "tp"),
        P("ctx", "tp"),
        P("tp", None),
        P("ctx", "tp"),
    )
    out_specs = (P("ctx", "tp"), P("ctx", "tp"), P("ctx", "tp"), P("ctx", "tp"))
    return jax.shard_map(body, mesh=mesh, in_specs=in_specs, out_specs=out_specs, check_vma=False)
```
